32 devices in a mesh: gx: 4 (over z), gy: 8 (over y, x, core).
Axes of the slice: x: 2, y: 2, z: 4, core: 2. Of those that a mesh axis runs over, the one named last changes fastest.
Arguments:
- region_state: float32 [9, 32, 24, 64], P(None, ('gx', 'gy')), may hold values from -6 to 6
- region_material: int32 [32, 24, 64], P(('gx', 'gy')), may hold values from 0 to 7
- fine_state: float32 [9, 96, 72, 128], P(None, 'gx', 'gy'), may hold values from -6 to 6
- fine_material: int32 [96, 72, 128], P('gx', 'gy'), may hold values from 0 to 7
- material_table: float32 [3, 8], replicated, may hold values from 0.6 to 1.4
Outputs:
- region_next: float32 [9, 32, 24, 64], P(None, ('gx', 'gy'))
- fine_next: float32 [9, 96, 72, 128], P(None, 'gx', 'gy')
The draws below stay inside these ranges and needn't reach their ends.
All inputs are finite; a program needn't handle non-finite values.
Results may differ from the reference program's by a relative error of at most 0.0012.
Values may be sent and summed in bfloat16 or wider, within the bound.
No kernel may reach another device: no remote copies, remote signals or barrier semaphores. Data moves between devices by JAX's collectives and lax.ppermute only.
A program may use at most 64 MiB of HBM per device.

```python
import jax
import jax.numpy as jnp
from jax import lax

XS = 1
RYS = 3
RZ = 64
FZ = 128
NMAT = 8
FX = 24
FY = 9
NRX = 32
NRY = 24
NFX = 96
NFY = 72
N_GX = 4
N_GY = 8


def plant(drawn, key, smallest, largest):
    spot = [jax.random.randint(jax.random.fold_in(key, axis), (), 0, length) for axis, length in enumerate(drawn.shape)]
    widest = drawn.shape.index(max(drawn.shape))
    neighbour = spot[:widest] + [(spot[widest] + 1) % drawn.shape[widest]] + spot[widest + 1:]
    return drawn.at[tuple(spot)].set(smallest).at[tuple(neighbour)].set(largest)


def block_levels(stream_key, shape, shards, least, largest):
    loudness = 1.0
    for dim, blocks in shards:
        draws = jax.random.uniform(jax.random.fold_in(jax.random.fold_in(stream_key, 6), dim), (blocks,), jnp.float32, least / len(shards), largest / len(shards))
        loudness = loudness * jnp.repeat(jnp.exp(draws), shape[dim] // blocks).reshape((-1,) + (1,) * (len(shape) - 1 - dim))
    return loudness


def centred(rng, extent, width, reach, shards=(), held_as=jnp.bfloat16):
    drawn = jax.random.normal(rng, extent, jnp.float32) * width
    if len(shards) > 0:
        drawn = block_levels(rng, extent, shards, -0.22, 0.18) * drawn
    return jnp.clip(drawn, min=-reach, max=reach).astype(held_as)


def setup_inputs(seed: int = 0) -> dict:
    key_of = jax.random.split(jax.random.key(seed), 6)
    return {
        "region_state": centred(key_of[0], (9, NRX, NRY, RZ), 1.0, 6.0, ((1, 32),), jnp.float32),
        "region_material": plant(jax.random.randint(key_of[1], (NRX, NRY, RZ), 0, NMAT), jax.random.fold_in(key_of[1], 1), 0, NMAT - 1).astype(jnp.int32),
        "fine_state": centred(key_of[2], (9, NFX, NFY, FZ), 1.0, 6.0, ((1, 4), (2, 8)), jnp.float32),
        "fine_material": plant(jax.random.randint(key_of[3], (NFX, NFY, FZ), 0, NMAT), jax.random.fold_in(key_of[3], 1), 0, NMAT - 1).astype(jnp.int32),
        "material_table": jnp.clip(jax.random.uniform(key_of[4], (3, NMAT), jnp.float32, 0.6, 1.4), 0.6, 1.4),
    }


def lookup(index, table):
    rho = jnp.zeros(index.shape, jnp.float32)
    lam = jnp.zeros(index.shape, jnp.float32)
    shear = jnp.zeros(index.shape, jnp.float32)
    for material in range(table.shape[1]):
        match = index == material
        rho = jnp.where(match, table[0, material], rho)
        lam = jnp.where(match, table[1, material], lam)
        shear = jnp.where(match, table[2, material], shear)
    return rho, lam, shear


def centered(padded, spacing):
    scale = 0.5 / spacing
    d_x = (padded[:, 2:, 1:-1, 1:-1] - padded[:, :-2, 1:-1, 1:-1]) * scale
    d_y = (padded[:, 1:-1, 2:, 1:-1] - padded[:, 1:-1, :-2, 1:-1]) * scale
    d_z = (padded[:, 1:-1, 1:-1, 2:] - padded[:, 1:-1, 1:-1, :-2]) * scale
    return d_x, d_y, d_z


def pad_all(field):
    return jnp.pad(field, ((0, 0), (1, 1), (1, 1), (1, 1)))


def elastic_step(state, props, step, spacing):
    rho, lam, shear = props
    velocity = state[:3]
    stress = state[3:]
    d_x, d_y, d_z = centered(pad_all(stress), spacing)
    acc_x = d_x[0] + d_y[3] + d_z[4]
    acc_y = d_x[3] + d_y[1] + d_z[5]
    acc_z = d_x[4] + d_y[5] + d_z[2]
    velocity = velocity + (step / rho)[None] * jnp.stack([acc_x, acc_y, acc_z])
    g_x, g_y, g_z = centered(pad_all(velocity), spacing)
    spread = g_x[0] + g_y[1] + g_z[2]
    new_xx = stress[0] + step * (lam * spread + 2.0 * shear * g_x[0])
    new_yy = stress[1] + step * (lam * spread + 2.0 * shear * g_y[1])
    new_zz = stress[2] + step * (lam * spread + 2.0 * shear * g_z[2])
    new_xy = stress[3] + step * shear * (g_y[0] + g_x[1])
    new_xz = stress[4] + step * shear * (g_z[0] + g_x[2])
    new_yz = stress[5] + step * shear * (g_z[1] + g_y[2])
    return jnp.concatenate([velocity, jnp.stack([new_xx, new_yy, new_zz, new_xy, new_xz, new_yz])], 0)


def interp_matrix(n_fine, n_coarse):
    fine_pos = jnp.arange(n_fine, dtype=jnp.int32)
    whole = fine_pos // 3
    rest = fine_pos - 3 * whole
    lower = jnp.where(rest == 0, whole - 1, whole)
    frac = jnp.where(rest == 0, 2.0 / 3.0, jnp.where(rest == 1, 0.0, 1.0 / 3.0)).astype(jnp.float32)
    below = lower < 0
    lower = jnp.where(below, 0, lower)
    frac = jnp.where(below, 0.0, frac).astype(jnp.float32)
    above = lower >= n_coarse - 1
    lower = jnp.where(above, n_coarse - 2, lower)
    frac = jnp.where(above, 1.0, frac).astype(jnp.float32)
    cols = jnp.arange(n_coarse, dtype=jnp.int32)
    low_hit = (cols[None, :] == lower[:, None]).astype(jnp.float32)
    high_hit = (cols[None, :] == lower[:, None] + 1).astype(jnp.float32)
    return ((1.0 - frac)[:, None] * low_hit + frac[:, None] * high_hit).astype(jnp.float32)


def ramp(count, tile):
    place = jnp.arange(count, dtype=jnp.int32)
    margin = jnp.minimum(place, count - 1 - place).astype(jnp.float32) + 0.5
    part = jnp.maximum(1.0 - margin / tile, 0.0)
    return part * part


def reference(region_state, region_material, fine_state, fine_material, material_table):
    region_next = elastic_step(region_state, lookup(region_material, material_table), 0.6, 3.0)
    columns = N_GY * XS
    both = jnp.concatenate([region_state, region_next], 0).astype(jnp.bfloat16).astype(jnp.float32)
    bands = both.reshape(18, N_GX, columns, N_GY, RYS, RZ)
    high = lax.Precision.HIGHEST
    first = jnp.einsum("fa,cialbz->ciflbz", interp_matrix(FX, columns), bands, precision=high)
    second = jnp.einsum("gb,ciflbz->ciflgz", interp_matrix(FY, RYS), first, precision=high)
    third = jnp.einsum("kz,ciflgz->ciflgk", interp_matrix(FZ, RZ), second, precision=high)
    background = third.reshape(18, NFX, NFY, FZ)
    relax = 0.1 + 0.4 * jnp.maximum(ramp(NFX, FX)[:, None], ramp(NFY, FY)[None, :])
    relax = relax[:, :, None]
    fine_props = lookup(fine_material, material_table)
    state = fine_state
    for sub in range(1, 4):
        state = elastic_step(state, fine_props, 0.2, 1.0)
        share = sub / 3.0
        target = background[:9] + share * (background[9:] - background[:9])
        state = state + relax[None] * (target - state)
    return region_next, state
```

```python
import jax
import jax.numpy as jnp
from jax import lax
from jax.sharding import PartitionSpec as P


def shifted(n, s):
    return [(i, i + s) for i in range(n) if 0 <= i + s < n]


def grid_pairs(nx, ny, dx, dy):
    pairs = []
    for a in range(nx):
        for b in range(ny):
            if 0 <= a + dx < nx and 0 <= b + dy < ny:
                pairs.append((a * ny + b, (a + dx) * ny + b + dy))
    return pairs


def tile_halo(field, width):
    nx, ny = lax.axis_size("gx"), lax.axis_size("gy")
    w = width
    lo_x, hi_x = field[:, -w:], field[:, :w]
    from_left = lax.ppermute(lo_x, "gx", shifted(nx, 1))
    from_right = lax.ppermute(hi_x, "gx", shifted(nx, -1))
    from_below = lax.ppermute(field[:, :, -w:], "gy", shifted(ny, 1))
    from_above = lax.ppermute(field[:, :, :w], "gy", shifted(ny, -1))
    both = ("gx", "gy")
    c_mm = lax.ppermute(field[:, -w:, -w:], both, grid_pairs(nx, ny, 1, 1))
    c_mp = lax.ppermute(field[:, -w:, :w], both, grid_pairs(nx, ny, 1, -1))
    c_pm = lax.ppermute(field[:, :w, -w:], both, grid_pairs(nx, ny, -1, 1))
    c_pp = lax.ppermute(field[:, :w, :w], both, grid_pairs(nx, ny, -1, -1))
    low = jnp.concatenate([c_mm, from_left, c_mp], axis=2)
    mid = jnp.concatenate([from_below, field, from_above], axis=2)
    high = jnp.concatenate([c_pm, from_right, c_pp], axis=2)
    return jnp.concatenate([low, mid, high], axis=1)


def strip_halo(field, width):
    n = lax.axis_size("gx") * lax.axis_size("gy")
    own = field.shape[1]
    reach = -(-width // own)
    both = ("gx", "gy")
    lows = [lax.ppermute(field, both, shifted(n, d)) for d in range(reach, 0, -1)]
    highs = [lax.ppermute(field, both, shifted(n, -d)) for d in range(1, reach + 1)]
    lo = jnp.concatenate(lows, axis=1)[:, reach * own - width:]
    hi = jnp.concatenate(highs, axis=1)[:, :width]
    return jnp.concatenate([lo, field, hi], axis=1)


def lookup(index, table):
    rho = jnp.zeros(index.shape, jnp.float32)
    lam = jnp.zeros(index.shape, jnp.float32)
    shear = jnp.zeros(index.shape, jnp.float32)
    for material in range(table.shape[1]):
        match = index == material
        rho = jnp.where(match, table[0, material], rho)
        lam = jnp.where(match, table[1, material], lam)
        shear = jnp.where(match, table[2, material], shear)
    return (rho, lam, shear)


def along(f, axis):
    n = f.shape[axis]
    zero = jnp.zeros_like(lax.slice_in_dim(f, 0, 1, axis=axis))
    up = jnp.concatenate([lax.slice_in_dim(f, 1, n, axis=axis), zero], axis=axis)
    down = jnp.concatenate([zero, lax.slice_in_dim(f, 0, n - 1, axis=axis)], axis=axis)
    return up - down


def step_wide(ext, coef, stress0, lam, shear, step, spacing, y_local):
    scale = 0.5 / spacing
    s = ext[3:9]
    if y_local:
        mid_s = s[:, 1:-1]
        dx = lambda c: (s[c, 2:] - s[c, :-2]) * scale
        dy = lambda c: along(mid_s[c], 1) * scale
        dz = lambda c: along(mid_s[c], 2) * scale
        vel_old = ext[0:3, 1:-1]
    else:
        mid_s = s[:, 1:-1, 1:-1]
        dx = lambda c: (s[c, 2:, 1:-1] - s[c, :-2, 1:-1]) * scale
        dy = lambda c: (s[c, 1:-1, 2:] - s[c, 1:-1, :-2]) * scale
        dz = lambda c: along(mid_s[c], 2) * scale
        vel_old = ext[0:3, 1:-1, 1:-1]
    acc_x = dx(0) + dy(3) + dz(4)
    acc_y = dx(3) + dy(1) + dz(5)
    acc_z = dx(4) + dy(5) + dz(2)
    vel = vel_old + coef[None] * jnp.stack([acc_x, acc_y, acc_z])
    if y_local:
        inner = vel[:, 1:-1]
        gx = lambda c: (vel[c, 2:] - vel[c, :-2]) * scale
        gy = lambda c: along(inner[c], 1) * scale
        gz = lambda c: along(inner[c], 2) * scale
    else:
        inner = vel[:, 1:-1, 1:-1]
        gx = lambda c: (vel[c, 2:, 1:-1] - vel[c, :-2, 1:-1]) * scale
        gy = lambda c: (vel[c, 1:-1, 2:] - vel[c, 1:-1, :-2]) * scale
        gz = lambda c: along(inner[c], 2) * scale
    g_x0, g_y1, g_z2 = gx(0), gy(1), gz(2)
    spread = g_x0 + g_y1 + g_z2
    new_xx = stress0[0] + step * (lam * spread + 2.0 * shear * g_x0)
    new_yy = stress0[1] + step * (lam * spread + 2.0 * shear * g_y1)
    new_zz = stress0[2] + step * (lam * spread + 2.0 * shear * g_z2)
    new_xy = stress0[3] + step * shear * (gy(0) + gx(1))
    new_xz = stress0[4] + step * shear * (gz(0) + gx(2))
    new_yz = stress0[5] + step * shear * (gz(1) + gy(2))
    return jnp.concatenate(
        [inner, jnp.stack([new_xx, new_yy, new_zz, new_xy, new_xz, new_yz])], 0
    )


def interp_matrix(n_fine, n_coarse):
    fine_pos = jnp.arange(n_fine, dtype=jnp.int32)
    whole = fine_pos // 3
    rest = fine_pos - 3 * whole
    lower = jnp.where(rest == 0, whole - 1, whole)
    frac = jnp.where(rest == 0, 2.0 / 3.0, jnp.where(rest == 1, 0.0, 1.0 / 3.0)).astype(jnp.float32)
    below = lower < 0
    lower = jnp.where(below, 0, lower)
    frac = jnp.where(below, 0.0, frac)
    above = lower >= n_coarse - 1
    lower = jnp.where(above, n_coarse - 2, lower)
    frac = jnp.where(above, 1.0, frac)
    cols = jnp.arange(n_coarse, dtype=jnp.int32)
    low_hit = (cols[None, :] == lower[:, None]).astype(jnp.float32)
    high_hit = (cols[None, :] == lower[:, None] + 1).astype(jnp.float32)
    return (1.0 - frac)[:, None] * low_hit + frac[:, None] * high_hit


def ramp(first, count, total, tile):
    place = first + jnp.arange(count, dtype=jnp.int32)
    margin = jnp.minimum(place, total - 1 - place).astype(jnp.float32) + 0.5
    part = jnp.maximum(1.0 - margin / tile, 0.0)
    return part * part


def local(region_state, region_material, fine_state, fine_material, material_table):
    count_x = lax.axis_size("gx")
    count_y = lax.axis_size("gy")
    fine_x = fine_state.shape[1]
    fine_y = fine_state.shape[2]
    reg_y = region_state.shape[2]
    rows_each = reg_y // count_y

    rho_r, lam_r, mu_r = lookup(region_material, material_table)
    coef_r = 0.6 / rho_r
    reg_ext = strip_halo(jnp.concatenate([region_state, coef_r[None]], 0), 2)
    region_next = step_wide(
        reg_ext, reg_ext[9, 1:-1], region_state[3:], lam_r, mu_r, 0.6, 3.0, True
    )

    both = jnp.concatenate([region_state, region_next], 0).astype(jnp.bfloat16)
    band = lax.all_to_all(both, "gy", 2, 1, tiled=True).astype(jnp.float32)
    columns = band.shape[1]
    high = lax.Precision.HIGHEST
    first = jnp.einsum("fa,cabz->cfbz", interp_matrix(fine_x, columns), band, precision=high)
    second = jnp.einsum("gb,cfbz->cfgz", interp_matrix(fine_y, rows_each), first, precision=high)
    background = jnp.einsum(
        "kz,cfgz->cfgk", interp_matrix(fine_state.shape[3], band.shape[3]), second, precision=high
    )
    along_x = ramp(lax.axis_index("gx") * fine_x, fine_x, count_x * fine_x, fine_x)
    along_y = ramp(lax.axis_index("gy") * fine_y, fine_y, count_y * fine_y, fine_y)
    relax = (0.1 + 0.4 * jnp.maximum(along_x[:, None], along_y[None, :]))[:, :, None]

    rho_f, lam_f, mu_f = lookup(fine_material, material_table)
    coef_f = 0.2 / rho_f
    ext = tile_halo(jnp.concatenate([fine_state, coef_f[None]], 0), 2)
    coef_ext = ext[9, 1:-1, 1:-1]
    state = fine_state
    for sub in range(1, 4):
        if sub > 1:
            ext = tile_halo(state, 2)
        state = step_wide(ext, coef_ext, state[3:], lam_f, mu_f, 0.2, 1.0, False)
        share = sub / 3.0
        target = background[:9] + share * (background[9:] - background[:9])
        state = state + relax[None] * (target - state)
    return (region_next, state)


def solution(mesh):
    return jax.shard_map(
        local,
        mesh=mesh,
        in_specs=(
            P(None, ("gx", "gy"), None, None),
            P(("gx", "gy"), None, None),
            P(None, "gx", "gy", None),
            P("gx", "gy", None),
            P(),
        ),
        out_specs=(P(None, ("gx", "gy"), None, None), P(None, "gx", "gy", None)),
        check_vma=False,
    )
```

```python
import jax
import jax.numpy as jnp
from jax import lax
from jax.sharding import PartitionSpec as P


def shifted(n, s):
    return [(i, i + s) for i in range(n) if 0 <= i + s < n]


def tile_halo(field, width):
    nx, ny = lax.axis_size("gx"), lax.axis_size("gy")
    w = width
    from_left = lax.ppermute(field[:, -w:], "gx", shifted(nx, 1))
    from_right = lax.ppermute(field[:, :w], "gx", shifted(nx, -1))
    wide = jnp.concatenate([from_left, field, from_right], axis=1)
    from_below = lax.ppermute(wide[:, :, -w:], "gy", shifted(ny, 1))
    from_above = lax.ppermute(wide[:, :, :w], "gy", shifted(ny, -1))
    return jnp.concatenate([from_below, wide, from_above], axis=2)


def strip_halo(field, width):
    n = lax.axis_size("gx") * lax.axis_size("gy")
    own = field.shape[1]
    reach = -(-width // own)
    both = ("gx", "gy")
    lows = [lax.ppermute(field, both, shifted(n, d)) for d in range(reach, 0, -1)]
    highs = [lax.ppermute(field, both, shifted(n, -d)) for d in range(1, reach + 1)]
    lo = jnp.concatenate(lows, axis=1)[:, reach * own - width:]
    hi = jnp.concatenate(highs, axis=1)[:, :width]
    return jnp.concatenate([lo, field, hi], axis=1)


def lookup(index, table):
    rho = jnp.zeros(index.shape, jnp.float32)
    lam = jnp.zeros(index.shape, jnp.float32)
    shear = jnp.zeros(index.shape, jnp.float32)
    for material in range(table.shape[1]):
        match = index == material
        rho = jnp.where(match, table[0, material], rho)
        lam = jnp.where(match, table[1, material], lam)
        shear = jnp.where(match, table[2, material], shear)
    return (rho, lam, shear)


def along(f, axis):
    n = f.shape[axis]
    zero = jnp.zeros_like(lax.slice_in_dim(f, 0, 1, axis=axis))
    up = jnp.concatenate([lax.slice_in_dim(f, 1, n, axis=axis), zero], axis=axis)
    down = jnp.concatenate([zero, lax.slice_in_dim(f, 0, n - 1, axis=axis)], axis=axis)
    return up - down


def step_wide(ext, coef, stress0, lam, shear, step, spacing, y_local):
    scale = 0.5 / spacing
    s = ext[3:9]
    if y_local:
        mid_s = s[:, 1:-1]
        dx = lambda c: (s[c, 2:] - s[c, :-2]) * scale
        dy = lambda c: along(mid_s[c], 1) * scale
        dz = lambda c: along(mid_s[c], 2) * scale
        vel_old = ext[0:3, 1:-1]
    else:
        mid_s = s[:, 1:-1, 1:-1]
        dx = lambda c: (s[c, 2:, 1:-1] - s[c, :-2, 1:-1]) * scale
        dy = lambda c: (s[c, 1:-1, 2:] - s[c, 1:-1, :-2]) * scale
        dz = lambda c: along(mid_s[c], 2) * scale
        vel_old = ext[0:3, 1:-1, 1:-1]
    acc_x = dx(0) + dy(3) + dz(4)
    acc_y = dx(3) + dy(1) + dz(5)
    acc_z = dx(4) + dy(5) + dz(2)
    vel = vel_old + coef[None] * jnp.stack([acc_x, acc_y, acc_z])
    if y_local:
        inner = vel[:, 1:-1]
        gx = lambda c: (vel[c, 2:] - vel[c, :-2]) * scale
        gy = lambda c: along(inner[c], 1) * scale
        gz = lambda c: along(inner[c], 2) * scale
    else:
        inner = vel[:, 1:-1, 1:-1]
        gx = lambda c: (vel[c, 2:, 1:-1] - vel[c, :-2, 1:-1]) * scale
        gy = lambda c: (vel[c, 1:-1, 2:] - vel[c, 1:-1, :-2]) * scale
        gz = lambda c: along(inner[c], 2) * scale
    g_x0, g_y1, g_z2 = gx(0), gy(1), gz(2)
    spread = g_x0 + g_y1 + g_z2
    new_xx = stress0[0] + step * (lam * spread + 2.0 * shear * g_x0)
    new_yy = stress0[1] + step * (lam * spread + 2.0 * shear * g_y1)
    new_zz = stress0[2] + step * (lam * spread + 2.0 * shear * g_z2)
    new_xy = stress0[3] + step * shear * (gy(0) + gx(1))
    new_xz = stress0[4] + step * shear * (gz(0) + gx(2))
    new_yz = stress0[5] + step * shear * (gz(1) + gy(2))
    return jnp.concatenate(
        [inner, jnp.stack([new_xx, new_yy, new_zz, new_xy, new_xz, new_yz])], 0
    )


def interp_matrix(n_fine, n_coarse):
    fine_pos = jnp.arange(n_fine, dtype=jnp.int32)
    whole = fine_pos // 3
    rest = fine_pos - 3 * whole
    lower = jnp.where(rest == 0, whole - 1, whole)
    frac = jnp.where(rest == 0, 2.0 / 3.0, jnp.where(rest == 1, 0.0, 1.0 / 3.0)).astype(jnp.float32)
    below = lower < 0
    lower = jnp.where(below, 0, lower)
    frac = jnp.where(below, 0.0, frac)
    above = lower >= n_coarse - 1
    lower = jnp.where(above, n_coarse - 2, lower)
    frac = jnp.where(above, 1.0, frac)
    cols = jnp.arange(n_coarse, dtype=jnp.int32)
    low_hit = (cols[None, :] == lower[:, None]).astype(jnp.float32)
    high_hit = (cols[None, :] == lower[:, None] + 1).astype(jnp.float32)
    return (1.0 - frac)[:, None] * low_hit + frac[:, None] * high_hit


def ramp(first, count, total, tile):
    place = first + jnp.arange(count, dtype=jnp.int32)
    margin = jnp.minimum(place, total - 1 - place).astype(jnp.float32) + 0.5
    part = jnp.maximum(1.0 - margin / tile, 0.0)
    return part * part


def local(region_state, region_material, fine_state, fine_material, material_table):
    count_x = lax.axis_size("gx")
    count_y = lax.axis_size("gy")
    fine_x = fine_state.shape[1]
    fine_y = fine_state.shape[2]
    reg_y = region_state.shape[2]
    rows_each = reg_y // count_y

    rho_r, lam_r, mu_r = lookup(region_material, material_table)
    coef_r, lam_r, mu_r = lax.optimization_barrier((0.6 / rho_r, lam_r, mu_r))
    reg_ext = strip_halo(jnp.concatenate([region_state, coef_r[None]], 0), 2)
    region_next = step_wide(
        reg_ext, reg_ext[9, 1:-1], region_state[3:], lam_r, mu_r, 0.6, 3.0, True
    )

    both = jnp.concatenate([region_state, region_next], 0).astype(jnp.bfloat16)
    band = lax.all_to_all(both, "gy", 2, 1, tiled=True).astype(jnp.float32)
    columns = band.shape[1]
    high = lax.Precision.HIGHEST
    first = jnp.einsum("fa,cabz->cfbz", interp_matrix(fine_x, columns), band, precision=high)
    second = jnp.einsum("gb,cfbz->cfgz", interp_matrix(fine_y, rows_each), first, precision=high)
    background = jnp.einsum(
        "kz,cfgz->cfgk", interp_matrix(fine_state.shape[3], band.shape[3]), second, precision=high
    )
    along_x = ramp(lax.axis_index("gx") * fine_x, fine_x, count_x * fine_x, fine_x)
    along_y = ramp(lax.axis_index("gy") * fine_y, fine_y, count_y * fine_y, fine_y)
    relax = (0.1 + 0.4 * jnp.maximum(along_x[:, None], along_y[None, :]))[:, :, None]

    rho_f, lam_f, mu_f = lookup(fine_material, material_table)
    coef_f, lam_f, mu_f = lax.optimization_barrier((0.2 / rho_f, lam_f, mu_f))
    ext = tile_halo(jnp.concatenate([fine_state, coef_f[None]], 0), 2)
    coef_ext = ext[9, 1:-1, 1:-1]
    state = fine_state
    for sub in range(1, 4):
        if sub > 1:
            ext = tile_halo(state, 2)
        state = step_wide(ext, coef_ext, state[3:], lam_f, mu_f, 0.2, 1.0, False)
        share = sub / 3.0
        target = background[:9] + share * (background[9:] - background[:9])
        state = state + relax[None] * (target - state)
    return (region_next, state)


def solution(mesh):
    return jax.shard_map(
        local,
        mesh=mesh,
        in_specs=(
            P(None, ("gx", "gy"), None, None),
            P(("gx", "gy"), None, None),
            P(None, "gx", "gy", None),
            P("gx", "gy", None),
            P(),
        ),
        out_specs=(P(None, ("gx", "gy"), None, None), P(None, "gx", "gy", None)),
        check_vma=False,
    )
```

```python
import jax
import jax.numpy as jnp
from jax import lax
from jax.sharding import PartitionSpec as P
from jax.experimental import pallas as pl
from jax.experimental.pallas import tpu as pltpu


def shifted(n, s):
    return [(i, i + s) for i in range(n) if 0 <= i + s < n]


def tile_halo(field, width):
    nx, ny = lax.axis_size("gx"), lax.axis_size("gy")
    w = width
    from_left = lax.ppermute(field[:, -w:], "gx", shifted(nx, 1))
    from_right = lax.ppermute(field[:, :w], "gx", shifted(nx, -1))
    wide = jnp.concatenate([from_left, field, from_right], axis=1)
    from_below = lax.ppermute(wide[:, :, -w:], "gy", shifted(ny, 1))
    from_above = lax.ppermute(wide[:, :, :w], "gy", shifted(ny, -1))
    return jnp.concatenate([from_below, wide, from_above], axis=2)


def strip_halo(field, width):
    n = lax.axis_size("gx") * lax.axis_size("gy")
    own = field.shape[1]
    reach = -(-width // own)
    both = ("gx", "gy")
    lows = [lax.ppermute(field, both, shifted(n, d)) for d in range(reach, 0, -1)]
    highs = [lax.ppermute(field, both, shifted(n, -d)) for d in range(1, reach + 1)]
    lo = jnp.concatenate(lows, axis=1)[:, reach * own - width:]
    hi = jnp.concatenate(highs, axis=1)[:, :width]
    return jnp.concatenate([lo, field, hi], axis=1)


def lookup_kernel(step, idx_ref, tab_ref, coef_ref, lam_ref, mu_ref):
    idx = idx_ref[...]
    rho = jnp.zeros(idx.shape, jnp.float32)
    lam = jnp.zeros(idx.shape, jnp.float32)
    shear = jnp.zeros(idx.shape, jnp.float32)
    for material in range(tab_ref.shape[1]):
        match = idx == material
        rho = jnp.where(match, tab_ref[0, material], rho)
        lam = jnp.where(match, tab_ref[1, material], lam)
        shear = jnp.where(match, tab_ref[2, material], shear)
    coef_ref[...] = step / rho
    lam_ref[...] = lam
    mu_ref[...] = shear


def lookup(index, table, step):
    out = jax.ShapeDtypeStruct(index.shape, jnp.float32)
    vmem = pl.BlockSpec(memory_space=pltpu.VMEM)
    return pl.pallas_call(
        lambda *refs: lookup_kernel(step, *refs),
        out_shape=(out, out, out),
        in_specs=[vmem, pl.BlockSpec(memory_space=pltpu.SMEM)],
        out_specs=(vmem, vmem, vmem),
    )(index, table)


def along(f, axis):
    n = f.shape[axis]
    zero = jnp.zeros_like(lax.slice_in_dim(f, 0, 1, axis=axis))
    up = jnp.concatenate([lax.slice_in_dim(f, 1, n, axis=axis), zero], axis=axis)
    down = jnp.concatenate([zero, lax.slice_in_dim(f, 0, n - 1, axis=axis)], axis=axis)
    return up - down


def step_wide(ext, coef, stress0, lam, shear, step, spacing, y_local):
    scale = 0.5 / spacing
    s = ext[3:9]
    if y_local:
        mid_s = s[:, 1:-1]
        dx = lambda c: (s[c, 2:] - s[c, :-2]) * scale
        dy = lambda c: along(mid_s[c], 1) * scale
        dz = lambda c: along(mid_s[c], 2) * scale
        vel_old = ext[0:3, 1:-1]
    else:
        mid_s = s[:, 1:-1, 1:-1]
        dx = lambda c: (s[c, 2:, 1:-1] - s[c, :-2, 1:-1]) * scale
        dy = lambda c: (s[c, 1:-1, 2:] - s[c, 1:-1, :-2]) * scale
        dz = lambda c: along(mid_s[c], 2) * scale
        vel_old = ext[0:3, 1:-1, 1:-1]
    acc_x = dx(0) + dy(3) + dz(4)
    acc_y = dx(3) + dy(1) + dz(5)
    acc_z = dx(4) + dy(5) + dz(2)
    vel = vel_old + coef[None] * jnp.stack([acc_x, acc_y, acc_z])
    if y_local:
        inner = vel[:, 1:-1]
        gx = lambda c: (vel[c, 2:] - vel[c, :-2]) * scale
        gy = lambda c: along(inner[c], 1) * scale
        gz = lambda c: along(inner[c], 2) * scale
    else:
        inner = vel[:, 1:-1, 1:-1]
        gx = lambda c: (vel[c, 2:, 1:-1] - vel[c, :-2, 1:-1]) * scale
        gy = lambda c: (vel[c, 1:-1, 2:] - vel[c, 1:-1, :-2]) * scale
        gz = lambda c: along(inner[c], 2) * scale
    g_x0, g_y1, g_z2 = gx(0), gy(1), gz(2)
    spread = g_x0 + g_y1 + g_z2
    new_xx = stress0[0] + step * (lam * spread + 2.0 * shear * g_x0)
    new_yy = stress0[1] + step * (lam * spread + 2.0 * shear * g_y1)
    new_zz = stress0[2] + step * (lam * spread + 2.0 * shear * g_z2)
    new_xy = stress0[3] + step * shear * (gy(0) + gx(1))
    new_xz = stress0[4] + step * shear * (gz(0) + gx(2))
    new_yz = stress0[5] + step * shear * (gz(1) + gy(2))
    return jnp.concatenate(
        [inner, jnp.stack([new_xx, new_yy, new_zz, new_xy, new_xz, new_yz])], 0
    )


def interp_matrix(n_fine, n_coarse):
    fine_pos = jnp.arange(n_fine, dtype=jnp.int32)
    whole = fine_pos // 3
    rest = fine_pos - 3 * whole
    lower = jnp.where(rest == 0, whole - 1, whole)
    frac = jnp.where(rest == 0, 2.0 / 3.0, jnp.where(rest == 1, 0.0, 1.0 / 3.0)).astype(jnp.float32)
    below = lower < 0
    lower = jnp.where(below, 0, lower)
    frac = jnp.where(below, 0.0, frac)
    above = lower >= n_coarse - 1
    lower = jnp.where(above, n_coarse - 2, lower)
    frac = jnp.where(above, 1.0, frac)
    cols = jnp.arange(n_coarse, dtype=jnp.int32)
    low_hit = (cols[None, :] == lower[:, None]).astype(jnp.float32)
    high_hit = (cols[None, :] == lower[:, None] + 1).astype(jnp.float32)
    return (1.0 - frac)[:, None] * low_hit + frac[:, None] * high_hit


def ramp(first, count, total, tile):
    place = first + jnp.arange(count, dtype=jnp.int32)
    margin = jnp.minimum(place, total - 1 - place).astype(jnp.float32) + 0.5
    part = jnp.maximum(1.0 - margin / tile, 0.0)
    return part * part


def local(region_state, region_material, fine_state, fine_material, material_table):
    count_x = lax.axis_size("gx")
    count_y = lax.axis_size("gy")
    fine_x = fine_state.shape[1]
    fine_y = fine_state.shape[2]
    reg_y = region_state.shape[2]
    rows_each = reg_y // count_y

    coef_r, lam_r, mu_r = lookup(region_material, material_table, 0.6)
    reg_ext = strip_halo(jnp.concatenate([region_state, coef_r[None]], 0), 2)
    region_next = step_wide(
        reg_ext, reg_ext[9, 1:-1], region_state[3:], lam_r, mu_r, 0.6, 3.0, True
    )

    both = jnp.concatenate([region_state, region_next], 0).astype(jnp.bfloat16)
    band = lax.all_to_all(both, "gy", 2, 1, tiled=True).astype(jnp.float32)
    columns = band.shape[1]
    high = lax.Precision.HIGHEST
    first = jnp.einsum("fa,cabz->cfbz", interp_matrix(fine_x, columns), band, precision=high)
    second = jnp.einsum("gb,cfbz->cfgz", interp_matrix(fine_y, rows_each), first, precision=high)
    background = jnp.einsum(
        "kz,cfgz->cfgk", interp_matrix(fine_state.shape[3], band.shape[3]), second, precision=high
    )
    along_x = ramp(lax.axis_index("gx") * fine_x, fine_x, count_x * fine_x, fine_x)
    along_y = ramp(lax.axis_index("gy") * fine_y, fine_y, count_y * fine_y, fine_y)
    relax = (0.1 + 0.4 * jnp.maximum(along_x[:, None], along_y[None, :]))[:, :, None]

    coef_f, lam_f, mu_f = lookup(fine_material, material_table, 0.2)
    ext = tile_halo(jnp.concatenate([fine_state, coef_f[None]], 0), 2)
    coef_ext = ext[9, 1:-1, 1:-1]
    state = fine_state
    for sub in range(1, 4):
        if sub > 1:
            ext = tile_halo(state, 2)
        state = step_wide(ext, coef_ext, state[3:], lam_f, mu_f, 0.2, 1.0, False)
        share = sub / 3.0
        target = background[:9] + share * (background[9:] - background[:9])
        state = state + relax[None] * (target - state)
    return (region_next, state)


def solution(mesh):
    return jax.shard_map(
        local,
        mesh=mesh,
        in_specs=(
            P(None, ("gx", "gy"), None, None),
            P(("gx", "gy"), None, None),
            P(None, "gx", "gy", None),
            P("gx", "gy", None),
            P(),
        ),
        out_specs=(P(None, ("gx", "gy"), None, None), P(None, "gx", "gy", None)),
        check_vma=False,
    )
```

```python
import jax
import jax.numpy as jnp
from jax import lax
from jax.sharding import PartitionSpec as P
from jax.experimental import pallas as pl
from jax.experimental.pallas import tpu as pltpu


def shifted(n, s):
    return [(i, i + s) for i in range(n) if 0 <= i + s < n]


def packed_ppermute(parts, axis, perm):
    flat = jnp.concatenate([p.reshape(-1) for p in parts])
    got = lax.ppermute(flat, axis, perm)
    out, at = [], 0
    for p in parts:
        out.append(got[at:at + p.size].reshape(p.shape))
        at += p.size
    return out


def x_halo(field, width):
    nx = lax.axis_size("gx")
    from_left = lax.ppermute(field[:, -width:], "gx", shifted(nx, 1))
    from_right = lax.ppermute(field[:, :width], "gx", shifted(nx, -1))
    return jnp.concatenate([from_left, field, from_right], axis=1)


def lookup_kernel(step, idx_ref, tab_ref, coef_ref, lam_ref, mu_ref):
    idx = idx_ref[...]
    rho = jnp.zeros(idx.shape, jnp.float32)
    lam = jnp.zeros(idx.shape, jnp.float32)
    shear = jnp.zeros(idx.shape, jnp.float32)
    for material in range(tab_ref.shape[1]):
        match = idx == material
        rho = jnp.where(match, tab_ref[0, material], rho)
        lam = jnp.where(match, tab_ref[1, material], lam)
        shear = jnp.where(match, tab_ref[2, material], shear)
    coef_ref[...] = step / rho
    lam_ref[...] = lam
    mu_ref[...] = shear


def lookup(index, table, step):
    out = jax.ShapeDtypeStruct(index.shape, jnp.float32)
    vmem = pl.BlockSpec(memory_space=pltpu.VMEM)
    return pl.pallas_call(
        lambda *refs: lookup_kernel(step, *refs),
        out_shape=(out, out, out),
        in_specs=[vmem, pl.BlockSpec(memory_space=pltpu.SMEM)],
        out_specs=(vmem, vmem, vmem),
    )(index, table)


def along(f, axis):
    n = f.shape[axis]
    zero = jnp.zeros_like(lax.slice_in_dim(f, 0, 1, axis=axis))
    up = jnp.concatenate([lax.slice_in_dim(f, 1, n, axis=axis), zero], axis=axis)
    down = jnp.concatenate([zero, lax.slice_in_dim(f, 0, n - 1, axis=axis)], axis=axis)
    return up - down


def step_wide(ext, coef, stress0, lam, shear, step, spacing, y_local):
    scale = 0.5 / spacing
    s = ext[3:9]
    if y_local:
        mid_s = s[:, 1:-1]
        dx = lambda c: (s[c, 2:] - s[c, :-2]) * scale
        dy = lambda c: along(mid_s[c], 1) * scale
        dz = lambda c: along(mid_s[c], 2) * scale
        vel_old = ext[0:3, 1:-1]
    else:
        mid_s = s[:, 1:-1, 1:-1]
        dx = lambda c: (s[c, 2:, 1:-1] - s[c, :-2, 1:-1]) * scale
        dy = lambda c: (s[c, 1:-1, 2:] - s[c, 1:-1, :-2]) * scale
        dz = lambda c: along(mid_s[c], 2) * scale
        vel_old = ext[0:3, 1:-1, 1:-1]
    acc_x = dx(0) + dy(3) + dz(4)
    acc_y = dx(3) + dy(1) + dz(5)
    acc_z = dx(4) + dy(5) + dz(2)
    vel = vel_old + coef[None] * jnp.stack([acc_x, acc_y, acc_z])
    if y_local:
        inner = vel[:, 1:-1]
        gx = lambda c: (vel[c, 2:] - vel[c, :-2]) * scale
        gy = lambda c: along(inner[c], 1) * scale
        gz = lambda c: along(inner[c], 2) * scale
    else:
        inner = vel[:, 1:-1, 1:-1]
        gx = lambda c: (vel[c, 2:, 1:-1] - vel[c, :-2, 1:-1]) * scale
        gy = lambda c: (vel[c, 1:-1, 2:] - vel[c, 1:-1, :-2]) * scale
        gz = lambda c: along(inner[c], 2) * scale
    g_x0, g_y1, g_z2 = gx(0), gy(1), gz(2)
    spread = g_x0 + g_y1 + g_z2
    new_xx = stress0[0] + step * (lam * spread + 2.0 * shear * g_x0)
    new_yy = stress0[1] + step * (lam * spread + 2.0 * shear * g_y1)
    new_zz = stress0[2] + step * (lam * spread + 2.0 * shear * g_z2)
    new_xy = stress0[3] + step * shear * (gy(0) + gx(1))
    new_xz = stress0[4] + step * shear * (gz(0) + gx(2))
    new_yz = stress0[5] + step * shear * (gz(1) + gy(2))
    return jnp.concatenate(
        [inner, jnp.stack([new_xx, new_yy, new_zz, new_xy, new_xz, new_yz])], 0
    )


def interp_matrix(n_fine, n_coarse):
    fine_pos = jnp.arange(n_fine, dtype=jnp.int32)
    whole = fine_pos // 3
    rest = fine_pos - 3 * whole
    lower = jnp.where(rest == 0, whole - 1, whole)
    frac = jnp.where(rest == 0, 2.0 / 3.0, jnp.where(rest == 1, 0.0, 1.0 / 3.0)).astype(jnp.float32)
    below = lower < 0
    lower = jnp.where(below, 0, lower)
    frac = jnp.where(below, 0.0, frac)
    above = lower >= n_coarse - 1
    lower = jnp.where(above, n_coarse - 2, lower)
    frac = jnp.where(above, 1.0, frac)
    cols = jnp.arange(n_coarse, dtype=jnp.int32)
    low_hit = (cols[None, :] == lower[:, None]).astype(jnp.float32)
    high_hit = (cols[None, :] == lower[:, None] + 1).astype(jnp.float32)
    return (1.0 - frac)[:, None] * low_hit + frac[:, None] * high_hit


def ramp(first, count, total, tile):
    place = first + jnp.arange(count, dtype=jnp.int32)
    margin = jnp.minimum(place, total - 1 - place).astype(jnp.float32) + 0.5
    part = jnp.maximum(1.0 - margin / tile, 0.0)
    return part * part


def local(region_state, region_material, fine_state, fine_material, material_table):
    count_x = lax.axis_size("gx")
    count_y = lax.axis_size("gy")
    flat = ("gx", "gy")
    n_flat = count_x * count_y
    me_y = lax.axis_index("gy")
    fine_x = fine_state.shape[1]
    fine_y = fine_state.shape[2]
    fine_z = fine_state.shape[3]
    own = region_state.shape[1]
    reg_y = region_state.shape[2]
    rows_each = reg_y // count_y
    reach_y = 6

    coef_r, lam_r, mu_r = lookup(region_material, material_table, 0.6)
    coef_f, lam_f, mu_f = lookup(fine_material, material_table, 0.2)

    region_pay = jnp.concatenate([region_state, coef_r[None]], 0)
    fine_pay = jnp.concatenate([fine_state, coef_f[None], lam_f[None], mu_f[None]], 0)
    reg_lo, fine_lo = packed_ppermute(
        [region_pay, fine_pay[:, :, -reach_y:]], flat, shifted(n_flat, 1)
    )
    reg_hi, fine_hi = packed_ppermute(
        [region_pay, fine_pay[:, :, :reach_y]], flat, shifted(n_flat, -1)
    )
    fine_lo = jnp.where(me_y > 0, fine_lo, 0.0)
    fine_hi = jnp.where(me_y < count_y - 1, fine_hi, 0.0)
    lows, highs = [reg_lo], [reg_hi]
    for d in range(2, -(-2 // own) + 1):
        lows.insert(0, lax.ppermute(region_pay, flat, shifted(n_flat, d)))
        highs.append(lax.ppermute(region_pay, flat, shifted(n_flat, -d)))
    reg_ext = jnp.concatenate(
        [jnp.concatenate(lows, 1)[:, -2:], region_pay, jnp.concatenate(highs, 1)[:, :2]], 1
    )
    region_next = step_wide(
        reg_ext, reg_ext[9, 1:-1], region_state[3:], lam_r, mu_r, 0.6, 3.0, True
    )

    both = jnp.concatenate([region_state, region_next], 0).astype(jnp.bfloat16)
    both = jnp.pad(both, ((0, 0), (0, 0), (rows_each, rows_each), (0, 0)))
    send = jnp.concatenate(
        [both[:, :, rows_each * d: rows_each * (d + 3)] for d in range(count_y)], 2
    )
    band = lax.all_to_all(send, "gy", 2, 1, tiled=True).astype(jnp.float32)
    columns = band.shape[1]
    high = lax.Precision.HIGHEST
    along_y_w = interp_matrix(fine_y, rows_each)
    zeros_w = jnp.zeros_like(along_y_w)
    tiles_w = jnp.concatenate(
        [
            jnp.concatenate([along_y_w, zeros_w, zeros_w], 1),
            jnp.concatenate([zeros_w, along_y_w, zeros_w], 1),
            jnp.concatenate([zeros_w, zeros_w, along_y_w], 1),
        ],
        0,
    )[fine_y - 4: 2 * fine_y + 4]
    first = jnp.einsum("fa,cabz->cfbz", interp_matrix(fine_x, columns), band, precision=high)
    second = jnp.einsum("gb,cfbz->cfgz", tiles_w, first, precision=high)
    background = jnp.einsum(
        "kz,cfgz->cfgk", interp_matrix(fine_z, band.shape[3]), second, precision=high
    )
    along_x = ramp(lax.axis_index("gx") * fine_x, fine_x, count_x * fine_x, fine_x)
    along_y = ramp(me_y * fine_y - 4, fine_y + 8, count_y * fine_y, fine_y)
    relax = (0.1 + 0.4 * jnp.maximum(along_x[:, None], along_y[None, :]))[:, :, None]

    wide = jnp.concatenate([fine_lo, fine_pay, fine_hi], axis=2)
    lam_w, mu_w = wide[10], wide[11]
    state = wide[:9]
    coef_w = None
    for sub in range(1, 4):
        if sub == 1:
            ext = x_halo(wide[:10], 2)
            coef_w = ext[9, 1:-1]
            ext = ext[:9]
        else:
            ext = x_halo(state, 2)
        off = 2 * (sub - 1)
        rows = state.shape[2]
        state = step_wide(
            ext,
            coef_w[:, off + 1: off + rows - 1],
            state[3:, :, 2:-2],
            lam_w[:, off + 2: off + rows - 2],
            mu_w[:, off + 2: off + rows - 2],
            0.2,
            1.0,
            False,
        )
        share = sub / 3.0
        target = background[:9, :, off: off + rows - 4] + share * (
            background[9:, :, off: off + rows - 4] - background[:9, :, off: off + rows - 4]
        )
        state = state + relax[None, :, off: off + rows - 4] * (target - state)
    return (region_next, state)


def solution(mesh):
    return jax.shard_map(
        local,
        mesh=mesh,
        in_specs=(
            P(None, ("gx", "gy"), None, None),
            P(("gx", "gy"), None, None),
            P(None, "gx", "gy", None),
            P("gx", "gy", None),
            P(),
        ),
        out_specs=(P(None, ("gx", "gy"), None, None), P(None, "gx", "gy", None)),
        check_vma=False,
    )
```

```python
import jax
import jax.numpy as jnp
from jax import lax
from jax.sharding import PartitionSpec as P
from jax.experimental import pallas as pl
from jax.experimental.pallas import tpu as pltpu


def shifted(n, s):
    return [(i, i + s) for i in range(n) if 0 <= i + s < n]


def x_halo(field, width):
    nx = lax.axis_size("gx")
    from_left = lax.ppermute(field[:, -width:], "gx", shifted(nx, 1))
    from_right = lax.ppermute(field[:, :width], "gx", shifted(nx, -1))
    return jnp.concatenate([from_left, field, from_right], axis=1)


def lookup_kernel(step, idx_ref, tab_ref, coef_ref, lam_ref, mu_ref):
    idx = idx_ref[...]
    rho = jnp.zeros(idx.shape, jnp.float32)
    lam = jnp.zeros(idx.shape, jnp.float32)
    shear = jnp.zeros(idx.shape, jnp.float32)
    for material in range(tab_ref.shape[1]):
        match = idx == material
        rho = jnp.where(match, tab_ref[0, material], rho)
        lam = jnp.where(match, tab_ref[1, material], lam)
        shear = jnp.where(match, tab_ref[2, material], shear)
    coef_ref[...] = step / rho
    lam_ref[...] = lam
    mu_ref[...] = shear


def lookup(index, table, step):
    out = jax.ShapeDtypeStruct(index.shape, jnp.float32)
    vmem = pl.BlockSpec(memory_space=pltpu.VMEM)
    return pl.pallas_call(
        lambda *refs: lookup_kernel(step, *refs),
        out_shape=(out, out, out),
        in_specs=[vmem, pl.BlockSpec(memory_space=pltpu.SMEM)],
        out_specs=(vmem, vmem, vmem),
    )(index, table)


def along(f, axis):
    n = f.shape[axis]
    zero = jnp.zeros_like(lax.slice_in_dim(f, 0, 1, axis=axis))
    up = jnp.concatenate([lax.slice_in_dim(f, 1, n, axis=axis), zero], axis=axis)
    down = jnp.concatenate([zero, lax.slice_in_dim(f, 0, n - 1, axis=axis)], axis=axis)
    return up - down


def step_wide(ext, coef, stress0, lam, shear, step, spacing, y_local):
    scale = 0.5 / spacing
    s = ext[3:9]
    if y_local:
        mid_s = s[:, 1:-1]
        dx = lambda c: (s[c, 2:] - s[c, :-2]) * scale
        dy = lambda c: along(mid_s[c], 1) * scale
        dz = lambda c: along(mid_s[c], 2) * scale
        vel_old = ext[0:3, 1:-1]
    else:
        mid_s = s[:, 1:-1, 1:-1]
        dx = lambda c: (s[c, 2:, 1:-1] - s[c, :-2, 1:-1]) * scale
        dy = lambda c: (s[c, 1:-1, 2:] - s[c, 1:-1, :-2]) * scale
        dz = lambda c: along(mid_s[c], 2) * scale
        vel_old = ext[0:3, 1:-1, 1:-1]
    acc_x = dx(0) + dy(3) + dz(4)
    acc_y = dx(3) + dy(1) + dz(5)
    acc_z = dx(4) + dy(5) + dz(2)
    vel = vel_old + coef[None] * jnp.stack([acc_x, acc_y, acc_z])
    if y_local:
        inner = vel[:, 1:-1]
        gx = lambda c: (vel[c, 2:] - vel[c, :-2]) * scale
        gy = lambda c: along(inner[c], 1) * scale
        gz = lambda c: along(inner[c], 2) * scale
    else:
        inner = vel[:, 1:-1, 1:-1]
        gx = lambda c: (vel[c, 2:, 1:-1] - vel[c, :-2, 1:-1]) * scale
        gy = lambda c: (vel[c, 1:-1, 2:] - vel[c, 1:-1, :-2]) * scale
        gz = lambda c: along(inner[c], 2) * scale
    g_x0, g_y1, g_z2 = gx(0), gy(1), gz(2)
    spread = g_x0 + g_y1 + g_z2
    new_xx = stress0[0] + step * (lam * spread + 2.0 * shear * g_x0)
    new_yy = stress0[1] + step * (lam * spread + 2.0 * shear * g_y1)
    new_zz = stress0[2] + step * (lam * spread + 2.0 * shear * g_z2)
    new_xy = stress0[3] + step * shear * (gy(0) + gx(1))
    new_xz = stress0[4] + step * shear * (gz(0) + gx(2))
    new_yz = stress0[5] + step * shear * (gz(1) + gy(2))
    return jnp.concatenate(
        [inner, jnp.stack([new_xx, new_yy, new_zz, new_xy, new_xz, new_yz])], 0
    )


def interp_matrix(n_fine, n_coarse):
    fine_pos = jnp.arange(n_fine, dtype=jnp.int32)
    whole = fine_pos // 3
    rest = fine_pos - 3 * whole
    lower = jnp.where(rest == 0, whole - 1, whole)
    frac = jnp.where(rest == 0, 2.0 / 3.0, jnp.where(rest == 1, 0.0, 1.0 / 3.0)).astype(jnp.float32)
    below = lower < 0
    lower = jnp.where(below, 0, lower)
    frac = jnp.where(below, 0.0, frac)
    above = lower >= n_coarse - 1
    lower = jnp.where(above, n_coarse - 2, lower)
    frac = jnp.where(above, 1.0, frac)
    cols = jnp.arange(n_coarse, dtype=jnp.int32)
    low_hit = (cols[None, :] == lower[:, None]).astype(jnp.float32)
    high_hit = (cols[None, :] == lower[:, None] + 1).astype(jnp.float32)
    return (1.0 - frac)[:, None] * low_hit + frac[:, None] * high_hit


def ramp(first, count, total, tile):
    place = first + jnp.arange(count, dtype=jnp.int32)
    margin = jnp.minimum(place, total - 1 - place).astype(jnp.float32) + 0.5
    part = jnp.maximum(1.0 - margin / tile, 0.0)
    return part * part


def local(region_state, region_material, fine_state, fine_material, material_table):
    count_x = lax.axis_size("gx")
    count_y = lax.axis_size("gy")
    flat = ("gx", "gy")
    n_flat = count_x * count_y
    me_y = lax.axis_index("gy")
    fine_x = fine_state.shape[1]
    fine_y = fine_state.shape[2]
    fine_z = fine_state.shape[3]
    own = region_state.shape[1]
    reg_y = region_state.shape[2]
    rows_each = reg_y // count_y
    reach_y = 6

    coef_r, lam_r, mu_r = lookup(region_material, material_table, 0.6)
    coef_f, lam_f, mu_f = lookup(fine_material, material_table, 0.2)

    region_pay = jnp.concatenate([region_state, coef_r[None]], 0)
    fine_pay = jnp.concatenate([fine_state, coef_f[None], lam_f[None], mu_f[None]], 0)
    fine_lo = lax.ppermute(fine_pay[:, :, -reach_y:], "gy", shifted(count_y, 1))
    fine_hi = lax.ppermute(fine_pay[:, :, :reach_y], "gy", shifted(count_y, -1))
    reg_lo = lax.ppermute(region_pay, flat, shifted(n_flat, 1))
    reg_hi = lax.ppermute(region_pay, flat, shifted(n_flat, -1))
    lows, highs = [reg_lo], [reg_hi]
    for d in range(2, -(-2 // own) + 1):
        lows.insert(0, lax.ppermute(region_pay, flat, shifted(n_flat, d)))
        highs.append(lax.ppermute(region_pay, flat, shifted(n_flat, -d)))
    reg_ext = jnp.concatenate(
        [jnp.concatenate(lows, 1)[:, -2:], region_pay, jnp.concatenate(highs, 1)[:, :2]], 1
    )
    region_next = step_wide(
        reg_ext, reg_ext[9, 1:-1], region_state[3:], lam_r, mu_r, 0.6, 3.0, True
    )

    both = jnp.concatenate([region_state, region_next], 0).astype(jnp.bfloat16)
    both = jnp.pad(both, ((0, 0), (0, 0), (rows_each, rows_each), (0, 0)))
    send = jnp.concatenate(
        [both[:, :, rows_each * d: rows_each * (d + 3)] for d in range(count_y)], 2
    )
    band = lax.all_to_all(send, "gy", 2, 1, tiled=True).astype(jnp.float32)
    columns = band.shape[1]
    high = lax.Precision.HIGHEST
    along_y_w = interp_matrix(fine_y, rows_each)
    zeros_w = jnp.zeros_like(along_y_w)
    tiles_w = jnp.concatenate(
        [
            jnp.concatenate([along_y_w, zeros_w, zeros_w], 1),
            jnp.concatenate([zeros_w, along_y_w, zeros_w], 1),
            jnp.concatenate([zeros_w, zeros_w, along_y_w], 1),
        ],
        0,
    )[fine_y - 4: 2 * fine_y + 4]
    first = jnp.einsum("fa,cabz->cfbz", interp_matrix(fine_x, columns), band, precision=high)
    second = jnp.einsum("gb,cfbz->cfgz", tiles_w, first, precision=high)
    background = jnp.einsum(
        "kz,cfgz->cfgk", interp_matrix(fine_z, band.shape[3]), second, precision=high
    )
    along_x = ramp(lax.axis_index("gx") * fine_x, fine_x, count_x * fine_x, fine_x)
    along_y = ramp(me_y * fine_y - 4, fine_y + 8, count_y * fine_y, fine_y)
    relax = (0.1 + 0.4 * jnp.maximum(along_x[:, None], along_y[None, :]))[:, :, None]

    wide = jnp.concatenate([fine_lo, fine_pay, fine_hi], axis=2)
    lam_w, mu_w = wide[10], wide[11]
    state = wide[:9]
    coef_w = None
    for sub in range(1, 4):
        if sub == 1:
            ext = x_halo(wide[:10], 2)
            coef_w = ext[9, 1:-1]
            ext = ext[:9]
        else:
            ext = x_halo(state, 2)
        off = 2 * (sub - 1)
        rows = state.shape[2]
        state = step_wide(
            ext,
            coef_w[:, off + 1: off + rows - 1],
            state[3:, :, 2:-2],
            lam_w[:, off + 2: off + rows - 2],
            mu_w[:, off + 2: off + rows - 2],
            0.2,
            1.0,
            False,
        )
        share = sub / 3.0
        target = background[:9, :, off: off + rows - 4] + share * (
            background[9:, :, off: off + rows - 4] - background[:9, :, off: off + rows - 4]
        )
        state = state + relax[None, :, off: off + rows - 4] * (target - state)
    return (region_next, state)


def solution(mesh):
    return jax.shard_map(
        local,
        mesh=mesh,
        in_specs=(
            P(None, ("gx", "gy"), None, None),
            P(("gx", "gy"), None, None),
            P(None, "gx", "gy", None),
            P("gx", "gy", None),
            P(),
        ),
        out_specs=(P(None, ("gx", "gy"), None, None), P(None, "gx", "gy", None)),
        check_vma=False,
    )
```

```python
import jax
import jax.numpy as jnp
from jax import lax
from jax.sharding import PartitionSpec as P
from jax.experimental import pallas as pl
from jax.experimental.pallas import tpu as pltpu


def shifted(n, s):
    return [(i, i + s) for i in range(n) if 0 <= i + s < n]


def x_halo(field, width):
    nx = lax.axis_size("gx")
    from_left = lax.ppermute(field[:, -width:], "gx", shifted(nx, 1))
    from_right = lax.ppermute(field[:, :width], "gx", shifted(nx, -1))
    return jnp.concatenate([from_left, field, from_right], axis=1)


def lookup_kernel(step, extra, idx_ref, tab_ref, state_ref, pay_ref, *rest):
    idx = idx_ref[...]
    rho = jnp.zeros(idx.shape, jnp.float32)
    lam = jnp.zeros(idx.shape, jnp.float32)
    shear = jnp.zeros(idx.shape, jnp.float32)
    for material in range(tab_ref.shape[1]):
        match = idx == material
        rho = jnp.where(match, tab_ref[0, material], rho)
        lam = jnp.where(match, tab_ref[1, material], lam)
        shear = jnp.where(match, tab_ref[2, material], shear)
    comps = state_ref.shape[0]
    pay_ref[:comps] = state_ref[...]
    pay_ref[comps] = step / rho
    if extra:
        pay_ref[comps + 1] = lam
        pay_ref[comps + 2] = shear
    else:
        rest[0][...] = lam
        rest[1][...] = shear


def lookup(index, table, state, step, extra):
    comps = state.shape[0]
    vmem = pl.BlockSpec(memory_space=pltpu.VMEM)
    cell = jax.ShapeDtypeStruct(index.shape, jnp.float32)
    pay = jax.ShapeDtypeStruct((comps + (3 if extra else 1),) + index.shape, jnp.float32)
    outs = (pay,) if extra else (pay, cell, cell)
    return pl.pallas_call(
        lambda *refs: lookup_kernel(step, extra, *refs),
        out_shape=outs,
        in_specs=[vmem, pl.BlockSpec(memory_space=pltpu.SMEM), vmem],
        out_specs=tuple(vmem for _ in outs),
    )(index, table, state)


def along(f, axis):
    n = f.shape[axis]
    zero = jnp.zeros_like(lax.slice_in_dim(f, 0, 1, axis=axis))
    up = jnp.concatenate([lax.slice_in_dim(f, 1, n, axis=axis), zero], axis=axis)
    down = jnp.concatenate([zero, lax.slice_in_dim(f, 0, n - 1, axis=axis)], axis=axis)
    return up - down


def step_wide(ext, coef, stress0, lam, shear, step, spacing, y_local):
    scale = 0.5 / spacing
    s = ext[3:9]
    if y_local:
        mid_s = s[:, 1:-1]
        dx = lambda c: (s[c, 2:] - s[c, :-2]) * scale
        dy = lambda c: along(mid_s[c], 1) * scale
        dz = lambda c: along(mid_s[c], 2) * scale
        vel_old = ext[0:3, 1:-1]
    else:
        mid_s = s[:, 1:-1, 1:-1]
        dx = lambda c: (s[c, 2:, 1:-1] - s[c, :-2, 1:-1]) * scale
        dy = lambda c: (s[c, 1:-1, 2:] - s[c, 1:-1, :-2]) * scale
        dz = lambda c: along(mid_s[c], 2) * scale
        vel_old = ext[0:3, 1:-1, 1:-1]
    acc_x = dx(0) + dy(3) + dz(4)
    acc_y = dx(3) + dy(1) + dz(5)
    acc_z = dx(4) + dy(5) + dz(2)
    vel = vel_old + coef[None] * jnp.stack([acc_x, acc_y, acc_z])
    if y_local:
        inner = vel[:, 1:-1]
        gx = lambda c: (vel[c, 2:] - vel[c, :-2]) * scale
        gy = lambda c: along(inner[c], 1) * scale
        gz = lambda c: along(inner[c], 2) * scale
    else:
        inner = vel[:, 1:-1, 1:-1]
        gx = lambda c: (vel[c, 2:, 1:-1] - vel[c, :-2, 1:-1]) * scale
        gy = lambda c: (vel[c, 1:-1, 2:] - vel[c, 1:-1, :-2]) * scale
        gz = lambda c: along(inner[c], 2) * scale
    g_x0, g_y1, g_z2 = gx(0), gy(1), gz(2)
    spread = g_x0 + g_y1 + g_z2
    new_xx = stress0[0] + step * (lam * spread + 2.0 * shear * g_x0)
    new_yy = stress0[1] + step * (lam * spread + 2.0 * shear * g_y1)
    new_zz = stress0[2] + step * (lam * spread + 2.0 * shear * g_z2)
    new_xy = stress0[3] + step * shear * (gy(0) + gx(1))
    new_xz = stress0[4] + step * shear * (gz(0) + gx(2))
    new_yz = stress0[5] + step * shear * (gz(1) + gy(2))
    return jnp.concatenate(
        [inner, jnp.stack([new_xx, new_yy, new_zz, new_xy, new_xz, new_yz])], 0
    )


def interp_matrix(n_fine, n_coarse):
    fine_pos = jnp.arange(n_fine, dtype=jnp.int32)
    whole = fine_pos // 3
    rest = fine_pos - 3 * whole
    lower = jnp.where(rest == 0, whole - 1, whole)
    frac = jnp.where(rest == 0, 2.0 / 3.0, jnp.where(rest == 1, 0.0, 1.0 / 3.0)).astype(jnp.float32)
    below = lower < 0
    lower = jnp.where(below, 0, lower)
    frac = jnp.where(below, 0.0, frac)
    above = lower >= n_coarse - 1
    lower = jnp.where(above, n_coarse - 2, lower)
    frac = jnp.where(above, 1.0, frac)
    cols = jnp.arange(n_coarse, dtype=jnp.int32)
    low_hit = (cols[None, :] == lower[:, None]).astype(jnp.float32)
    high_hit = (cols[None, :] == lower[:, None] + 1).astype(jnp.float32)
    return (1.0 - frac)[:, None] * low_hit + frac[:, None] * high_hit


def ramp(first, count, total, tile):
    place = first + jnp.arange(count, dtype=jnp.int32)
    margin = jnp.minimum(place, total - 1 - place).astype(jnp.float32) + 0.5
    part = jnp.maximum(1.0 - margin / tile, 0.0)
    return part * part


def local(region_state, region_material, fine_state, fine_material, material_table):
    count_x = lax.axis_size("gx")
    count_y = lax.axis_size("gy")
    flat = ("gx", "gy")
    n_flat = count_x * count_y
    me_y = lax.axis_index("gy")
    fine_x = fine_state.shape[1]
    fine_y = fine_state.shape[2]
    fine_z = fine_state.shape[3]
    own = region_state.shape[1]
    reg_y = region_state.shape[2]
    rows_each = reg_y // count_y
    reach_y = 6

    region_pay, lam_r, mu_r = lookup(region_material, material_table, region_state, 0.6, False)
    (fine_pay,) = lookup(fine_material, material_table, fine_state, 0.2, True)

    fine_lo = lax.ppermute(fine_pay[:, :, -reach_y:], "gy", shifted(count_y, 1))
    fine_hi = lax.ppermute(fine_pay[:, :, :reach_y], "gy", shifted(count_y, -1))
    reg_lo = lax.ppermute(region_pay, flat, shifted(n_flat, 1))
    reg_hi = lax.ppermute(region_pay, flat, shifted(n_flat, -1))
    lows, highs = [reg_lo], [reg_hi]
    for d in range(2, -(-2 // own) + 1):
        lows.insert(0, lax.ppermute(region_pay, flat, shifted(n_flat, d)))
        highs.append(lax.ppermute(region_pay, flat, shifted(n_flat, -d)))
    reg_ext = jnp.concatenate(
        [jnp.concatenate(lows, 1)[:, -2:], region_pay, jnp.concatenate(highs, 1)[:, :2]], 1
    )
    region_next = step_wide(
        reg_ext, reg_ext[9, 1:-1], region_state[3:], lam_r, mu_r, 0.6, 3.0, True
    )

    both = jnp.concatenate([region_state, region_next], 0).astype(jnp.bfloat16)
    both = jnp.pad(both, ((0, 0), (0, 0), (rows_each, rows_each), (0, 0)))
    send = jnp.concatenate(
        [both[:, :, rows_each * d: rows_each * (d + 3)] for d in range(count_y)], 2
    )
    band = lax.all_to_all(send, "gy", 2, 1, tiled=True).astype(jnp.float32)
    columns = band.shape[1]
    high = lax.Precision.HIGH
    along_y_w = interp_matrix(fine_y, rows_each)
    zeros_w = jnp.zeros_like(along_y_w)
    tiles_w = jnp.concatenate(
        [
            jnp.concatenate([along_y_w, zeros_w, zeros_w], 1),
            jnp.concatenate([zeros_w, along_y_w, zeros_w], 1),
            jnp.concatenate([zeros_w, zeros_w, along_y_w], 1),
        ],
        0,
    )[fine_y - 4: 2 * fine_y + 4]
    first = jnp.einsum("fa,cabz->cfbz", interp_matrix(fine_x, columns), band, precision=high)
    second = jnp.einsum("gb,cfbz->cfgz", tiles_w, first, precision=high)
    background = jnp.einsum(
        "kz,cfgz->cfgk", interp_matrix(fine_z, band.shape[3]), second, precision=high
    )
    along_x = ramp(lax.axis_index("gx") * fine_x, fine_x, count_x * fine_x, fine_x)
    along_y = ramp(me_y * fine_y - 4, fine_y + 8, count_y * fine_y, fine_y)
    relax = (0.1 + 0.4 * jnp.maximum(along_x[:, None], along_y[None, :]))[:, :, None]

    wide = jnp.concatenate([fine_lo, fine_pay, fine_hi], axis=2)
    lam_w, mu_w = wide[10], wide[11]
    state = wide[:9]
    coef_w = None
    for sub in range(1, 4):
        if sub == 1:
            ext = x_halo(wide[:10], 2)
            coef_w = ext[9, 1:-1]
            ext = ext[:9]
        else:
            ext = x_halo(state, 2)
        off = 2 * (sub - 1)
        rows = state.shape[2]
        state = step_wide(
            ext,
            coef_w[:, off + 1: off + rows - 1],
            state[3:, :, 2:-2],
            lam_w[:, off + 2: off + rows - 2],
            mu_w[:, off + 2: off + rows - 2],
            0.2,
            1.0,
            False,
        )
        share = sub / 3.0
        target = background[:9, :, off: off + rows - 4] + share * (
            background[9:, :, off: off + rows - 4] - background[:9, :, off: off + rows - 4]
        )
        state = state + relax[None, :, off: off + rows - 4] * (target - state)
    return (region_next, state)


def solution(mesh):
    return jax.shard_map(
        local,
        mesh=mesh,
        in_specs=(
            P(None, ("gx", "gy"), None, None),
            P(("gx", "gy"), None, None),
            P(None, "gx", "gy", None),
            P("gx", "gy", None),
            P(),
        ),
        out_specs=(P(None, ("gx", "gy"), None, None), P(None, "gx", "gy", None)),
        check_vma=False,
    )
```

```python
import jax
import jax.numpy as jnp
from jax import lax
from jax.sharding import PartitionSpec as P
from jax.experimental import pallas as pl
from jax.experimental.pallas import tpu as pltpu


def shifted(n, s):
    return [(i, (i + s) % n) for i in range(n)]


def cyclic_from(field, axis, n, d, me):
    got = lax.ppermute(field, axis, shifted(n, d))
    return jnp.where((me - d >= 0) & (me - d < n), got, 0.0)


def x_halo(field, width):
    nx = lax.axis_size("gx")
    me = lax.axis_index("gx")
    from_left = cyclic_from(field[:, -width:], "gx", nx, 1, me)
    from_right = cyclic_from(field[:, :width], "gx", nx, -1, me)
    return jnp.concatenate([from_left, field, from_right], axis=1)


def lookup_kernel(step, extra, idx_ref, tab_ref, state_ref, pay_ref, *rest):
    idx = idx_ref[...]
    rho = jnp.zeros(idx.shape, jnp.float32)
    lam = jnp.zeros(idx.shape, jnp.float32)
    shear = jnp.zeros(idx.shape, jnp.float32)
    for material in range(tab_ref.shape[1]):
        match = idx == material
        rho = jnp.where(match, tab_ref[0, material], rho)
        lam = jnp.where(match, tab_ref[1, material], lam)
        shear = jnp.where(match, tab_ref[2, material], shear)
    comps = state_ref.shape[0]
    pay_ref[:comps] = state_ref[...]
    pay_ref[comps] = step / rho
    if extra:
        pay_ref[comps + 1] = lam
        pay_ref[comps + 2] = shear
    else:
        rest[0][...] = lam
        rest[1][...] = shear


def lookup(index, table, state, step, extra):
    comps = state.shape[0]
    vmem = pl.BlockSpec(memory_space=pltpu.VMEM)
    cell = jax.ShapeDtypeStruct(index.shape, jnp.float32)
    pay = jax.ShapeDtypeStruct((comps + (3 if extra else 1),) + index.shape, jnp.float32)
    outs = (pay,) if extra else (pay, cell, cell)
    return pl.pallas_call(
        lambda *refs: lookup_kernel(step, extra, *refs),
        out_shape=outs,
        in_specs=[vmem, pl.BlockSpec(memory_space=pltpu.SMEM), vmem],
        out_specs=tuple(vmem for _ in outs),
    )(index, table, state)


def along(f, axis):
    n = f.shape[axis]
    zero = jnp.zeros_like(lax.slice_in_dim(f, 0, 1, axis=axis))
    up = jnp.concatenate([lax.slice_in_dim(f, 1, n, axis=axis), zero], axis=axis)
    down = jnp.concatenate([zero, lax.slice_in_dim(f, 0, n - 1, axis=axis)], axis=axis)
    return up - down


def step_wide(ext, coef, stress0, lam, shear, step, spacing, y_local):
    scale = 0.5 / spacing
    s = ext[3:9]
    if y_local:
        mid_s = s[:, 1:-1]
        dx = lambda c: (s[c, 2:] - s[c, :-2]) * scale
        dy = lambda c: along(mid_s[c], 1) * scale
        dz = lambda c: along(mid_s[c], 2) * scale
        vel_old = ext[0:3, 1:-1]
    else:
        mid_s = s[:, 1:-1, 1:-1]
        dx = lambda c: (s[c, 2:, 1:-1] - s[c, :-2, 1:-1]) * scale
        dy = lambda c: (s[c, 1:-1, 2:] - s[c, 1:-1, :-2]) * scale
        dz = lambda c: along(mid_s[c], 2) * scale
        vel_old = ext[0:3, 1:-1, 1:-1]
    acc_x = dx(0) + dy(3) + dz(4)
    acc_y = dx(3) + dy(1) + dz(5)
    acc_z = dx(4) + dy(5) + dz(2)
    vel = vel_old + coef[None] * jnp.stack([acc_x, acc_y, acc_z])
    if y_local:
        inner = vel[:, 1:-1]
        gx = lambda c: (vel[c, 2:] - vel[c, :-2]) * scale
        gy = lambda c: along(inner[c], 1) * scale
        gz = lambda c: along(inner[c], 2) * scale
    else:
        inner = vel[:, 1:-1, 1:-1]
        gx = lambda c: (vel[c, 2:, 1:-1] - vel[c, :-2, 1:-1]) * scale
        gy = lambda c: (vel[c, 1:-1, 2:] - vel[c, 1:-1, :-2]) * scale
        gz = lambda c: along(inner[c], 2) * scale
    g_x0, g_y1, g_z2 = gx(0), gy(1), gz(2)
    spread = g_x0 + g_y1 + g_z2
    new_xx = stress0[0] + step * (lam * spread + 2.0 * shear * g_x0)
    new_yy = stress0[1] + step * (lam * spread + 2.0 * shear * g_y1)
    new_zz = stress0[2] + step * (lam * spread + 2.0 * shear * g_z2)
    new_xy = stress0[3] + step * shear * (gy(0) + gx(1))
    new_xz = stress0[4] + step * shear * (gz(0) + gx(2))
    new_yz = stress0[5] + step * shear * (gz(1) + gy(2))
    return jnp.concatenate(
        [inner, jnp.stack([new_xx, new_yy, new_zz, new_xy, new_xz, new_yz])], 0
    )


def interp_matrix(n_fine, n_coarse):
    fine_pos = jnp.arange(n_fine, dtype=jnp.int32)
    whole = fine_pos // 3
    rest = fine_pos - 3 * whole
    lower = jnp.where(rest == 0, whole - 1, whole)
    frac = jnp.where(rest == 0, 2.0 / 3.0, jnp.where(rest == 1, 0.0, 1.0 / 3.0)).astype(jnp.float32)
    below = lower < 0
    lower = jnp.where(below, 0, lower)
    frac = jnp.where(below, 0.0, frac)
    above = lower >= n_coarse - 1
    lower = jnp.where(above, n_coarse - 2, lower)
    frac = jnp.where(above, 1.0, frac)
    cols = jnp.arange(n_coarse, dtype=jnp.int32)
    low_hit = (cols[None, :] == lower[:, None]).astype(jnp.float32)
    high_hit = (cols[None, :] == lower[:, None] + 1).astype(jnp.float32)
    return (1.0 - frac)[:, None] * low_hit + frac[:, None] * high_hit


def ramp(first, count, total, tile):
    place = first + jnp.arange(count, dtype=jnp.int32)
    margin = jnp.minimum(place, total - 1 - place).astype(jnp.float32) + 0.5
    part = jnp.maximum(1.0 - margin / tile, 0.0)
    return part * part


def local(region_state, region_material, fine_state, fine_material, material_table):
    count_x = lax.axis_size("gx")
    count_y = lax.axis_size("gy")
    flat = ("gx", "gy")
    n_flat = count_x * count_y
    me_y = lax.axis_index("gy")
    fine_x = fine_state.shape[1]
    fine_y = fine_state.shape[2]
    fine_z = fine_state.shape[3]
    own = region_state.shape[1]
    reg_y = region_state.shape[2]
    rows_each = reg_y // count_y
    reach_y = 6

    region_pay, lam_r, mu_r = lookup(region_material, material_table, region_state, 0.6, False)
    (fine_pay,) = lookup(fine_material, material_table, fine_state, 0.2, True)

    me_flat = lax.axis_index("gx") * count_y + me_y
    fine_lo = cyclic_from(fine_pay[:, :, -reach_y:], "gy", count_y, 1, me_y)
    fine_hi = cyclic_from(fine_pay[:, :, :reach_y], "gy", count_y, -1, me_y)
    reg_lo = cyclic_from(region_pay, flat, n_flat, 1, me_flat)
    reg_hi = cyclic_from(region_pay, flat, n_flat, -1, me_flat)
    lows, highs = [reg_lo], [reg_hi]
    for d in range(2, -(-2 // own) + 1):
        lows.insert(0, cyclic_from(region_pay, flat, n_flat, d, me_flat))
        highs.append(cyclic_from(region_pay, flat, n_flat, -d, me_flat))
    reg_ext = jnp.concatenate(
        [jnp.concatenate(lows, 1)[:, -2:], region_pay, jnp.concatenate(highs, 1)[:, :2]], 1
    )
    region_next = step_wide(
        reg_ext, reg_ext[9, 1:-1], region_state[3:], lam_r, mu_r, 0.6, 3.0, True
    )

    both = jnp.concatenate([region_state, region_next], 0).astype(jnp.bfloat16)
    both = jnp.pad(both, ((0, 0), (0, 0), (rows_each, rows_each), (0, 0)))
    send = jnp.concatenate(
        [both[:, :, rows_each * d: rows_each * (d + 3)] for d in range(count_y)], 2
    )
    band = lax.all_to_all(send, "gy", 2, 1, tiled=True)
    wide = jnp.concatenate([fine_lo, fine_pay, fine_hi], axis=2)
    band, first_ext = lax.optimization_barrier((band, x_halo(wide[:10], 2)))
    band = band.astype(jnp.float32)
    columns = band.shape[1]
    high = lax.Precision.HIGH
    along_y_w = interp_matrix(fine_y, rows_each)
    zeros_w = jnp.zeros_like(along_y_w)
    tiles_w = jnp.concatenate(
        [
            jnp.concatenate([along_y_w, zeros_w, zeros_w], 1),
            jnp.concatenate([zeros_w, along_y_w, zeros_w], 1),
            jnp.concatenate([zeros_w, zeros_w, along_y_w], 1),
        ],
        0,
    )[fine_y - 4: 2 * fine_y + 4]
    first = jnp.einsum("fa,cabz->cfbz", interp_matrix(fine_x, columns), band, precision=high)
    second = jnp.einsum("gb,cfbz->cfgz", tiles_w, first, precision=high)
    background = jnp.einsum(
        "kz,cfgz->cfgk", interp_matrix(fine_z, band.shape[3]), second, precision=high
    )
    along_x = ramp(lax.axis_index("gx") * fine_x, fine_x, count_x * fine_x, fine_x)
    along_y = ramp(me_y * fine_y - 4, fine_y + 8, count_y * fine_y, fine_y)
    relax = (0.1 + 0.4 * jnp.maximum(along_x[:, None], along_y[None, :]))[:, :, None]

    lam_w, mu_w = wide[10], wide[11]
    state = wide[:9]
    coef_w = None
    for sub in range(1, 4):
        if sub == 1:
            coef_w = first_ext[9, 1:-1]
            ext = first_ext[:9]
        else:
            ext = x_halo(state, 2)
        off = 2 * (sub - 1)
        rows = state.shape[2]
        state = step_wide(
            ext,
            coef_w[:, off + 1: off + rows - 1],
            state[3:, :, 2:-2],
            lam_w[:, off + 2: off + rows - 2],
            mu_w[:, off + 2: off + rows - 2],
            0.2,
            1.0,
            False,
        )
        share = sub / 3.0
        target = background[:9, :, off: off + rows - 4] + share * (
            background[9:, :, off: off + rows - 4] - background[:9, :, off: off + rows - 4]
        )
        state = state + relax[None, :, off: off + rows - 4] * (target - state)
    return (region_next, state)


def solution(mesh):
    return jax.shard_map(
        local,
        mesh=mesh,
        in_specs=(
            P(None, ("gx", "gy"), None, None),
            P(("gx", "gy"), None, None),
            P(None, "gx", "gy", None),
            P("gx", "gy", None),
            P(),
        ),
        out_specs=(P(None, ("gx", "gy"), None, None), P(None, "gx", "gy", None)),
        check_vma=False,
    )
```

```python
import jax
import jax.numpy as jnp
from jax import lax
from jax.sharding import PartitionSpec as P
from jax.experimental import pallas as pl
from jax.experimental.pallas import tpu as pltpu


def shifted(n, s):
    return [(i, (i + s) % n) for i in range(n)]


def cyclic_from(field, axis, n, d, me):
    got = lax.ppermute(field, axis, shifted(n, d))
    return jnp.where((me - d >= 0) & (me - d < n), got, 0.0)


def x_halo(field, width):
    nx = lax.axis_size("gx")
    me = lax.axis_index("gx")
    from_left = cyclic_from(field[:, -width:], "gx", nx, 1, me)
    from_right = cyclic_from(field[:, :width], "gx", nx, -1, me)
    return jnp.concatenate([from_left, field, from_right], axis=1)


def lookup_kernel(step, extra, idx_ref, tab_ref, state_ref, pay_ref, *rest):
    idx = idx_ref[...]
    rho = jnp.zeros(idx.shape, jnp.float32)
    lam = jnp.zeros(idx.shape, jnp.float32)
    shear = jnp.zeros(idx.shape, jnp.float32)
    for material in range(tab_ref.shape[1]):
        match = idx == material
        rho = jnp.where(match, tab_ref[0, material], rho)
        lam = jnp.where(match, tab_ref[1, material], lam)
        shear = jnp.where(match, tab_ref[2, material], shear)
    comps = state_ref.shape[0]
    pay_ref[:comps] = state_ref[...]
    pay_ref[comps] = step / rho
    if extra:
        pay_ref[comps + 1] = lam
        pay_ref[comps + 2] = shear
    else:
        rest[0][...] = lam
        rest[1][...] = shear


def lookup(index, table, state, step, extra):
    comps = state.shape[0]
    vmem = pl.BlockSpec(memory_space=pltpu.VMEM)
    cell = jax.ShapeDtypeStruct(index.shape, jnp.float32)
    pay = jax.ShapeDtypeStruct((comps + (3 if extra else 1),) + index.shape, jnp.float32)
    outs = (pay,) if extra else (pay, cell, cell)
    return pl.pallas_call(
        lambda *refs: lookup_kernel(step, extra, *refs),
        out_shape=outs,
        in_specs=[vmem, pl.BlockSpec(memory_space=pltpu.SMEM), vmem],
        out_specs=tuple(vmem for _ in outs),
    )(index, table, state)


def along(f, axis):
    n = f.shape[axis]
    zero = jnp.zeros_like(lax.slice_in_dim(f, 0, 1, axis=axis))
    up = jnp.concatenate([lax.slice_in_dim(f, 1, n, axis=axis), zero], axis=axis)
    down = jnp.concatenate([zero, lax.slice_in_dim(f, 0, n - 1, axis=axis)], axis=axis)
    return up - down


def step_wide(ext, coef, stress0, lam, shear, step, spacing, y_local):
    scale = 0.5 / spacing
    s = ext[3:9]
    if y_local:
        mid_s = s[:, 1:-1]
        dx = lambda c: (s[c, 2:] - s[c, :-2]) * scale
        dy = lambda c: along(mid_s[c], 1) * scale
        dz = lambda c: along(mid_s[c], 2) * scale
        vel_old = ext[0:3, 1:-1]
    else:
        mid_s = s[:, 1:-1, 1:-1]
        dx = lambda c: (s[c, 2:, 1:-1] - s[c, :-2, 1:-1]) * scale
        dy = lambda c: (s[c, 1:-1, 2:] - s[c, 1:-1, :-2]) * scale
        dz = lambda c: along(mid_s[c], 2) * scale
        vel_old = ext[0:3, 1:-1, 1:-1]
    acc_x = dx(0) + dy(3) + dz(4)
    acc_y = dx(3) + dy(1) + dz(5)
    acc_z = dx(4) + dy(5) + dz(2)
    vel = vel_old + coef[None] * jnp.stack([acc_x, acc_y, acc_z])
    if y_local:
        inner = vel[:, 1:-1]
        gx = lambda c: (vel[c, 2:] - vel[c, :-2]) * scale
        gy = lambda c: along(inner[c], 1) * scale
        gz = lambda c: along(inner[c], 2) * scale
    else:
        inner = vel[:, 1:-1, 1:-1]
        gx = lambda c: (vel[c, 2:, 1:-1] - vel[c, :-2, 1:-1]) * scale
        gy = lambda c: (vel[c, 1:-1, 2:] - vel[c, 1:-1, :-2]) * scale
        gz = lambda c: along(inner[c], 2) * scale
    g_x0, g_y1, g_z2 = gx(0), gy(1), gz(2)
    spread = g_x0 + g_y1 + g_z2
    new_xx = stress0[0] + step * (lam * spread + 2.0 * shear * g_x0)
    new_yy = stress0[1] + step * (lam * spread + 2.0 * shear * g_y1)
    new_zz = stress0[2] + step * (lam * spread + 2.0 * shear * g_z2)
    new_xy = stress0[3] + step * shear * (gy(0) + gx(1))
    new_xz = stress0[4] + step * shear * (gz(0) + gx(2))
    new_yz = stress0[5] + step * shear * (gz(1) + gy(2))
    return jnp.concatenate(
        [inner, jnp.stack([new_xx, new_yy, new_zz, new_xy, new_xz, new_yz])], 0
    )


def interp_matrix(n_fine, n_coarse):
    fine_pos = jnp.arange(n_fine, dtype=jnp.int32)
    whole = fine_pos // 3
    rest = fine_pos - 3 * whole
    lower = jnp.where(rest == 0, whole - 1, whole)
    frac = jnp.where(rest == 0, 2.0 / 3.0, jnp.where(rest == 1, 0.0, 1.0 / 3.0)).astype(jnp.float32)
    below = lower < 0
    lower = jnp.where(below, 0, lower)
    frac = jnp.where(below, 0.0, frac)
    above = lower >= n_coarse - 1
    lower = jnp.where(above, n_coarse - 2, lower)
    frac = jnp.where(above, 1.0, frac)
    cols = jnp.arange(n_coarse, dtype=jnp.int32)
    low_hit = (cols[None, :] == lower[:, None]).astype(jnp.float32)
    high_hit = (cols[None, :] == lower[:, None] + 1).astype(jnp.float32)
    return (1.0 - frac)[:, None] * low_hit + frac[:, None] * high_hit


def ramp(first, count, total, tile):
    place = first + jnp.arange(count, dtype=jnp.int32)
    margin = jnp.minimum(place, total - 1 - place).astype(jnp.float32) + 0.5
    part = jnp.maximum(1.0 - margin / tile, 0.0)
    return part * part


def local(region_state, region_material, fine_state, fine_material, material_table):
    count_x = lax.axis_size("gx")
    count_y = lax.axis_size("gy")
    flat = ("gx", "gy")
    n_flat = count_x * count_y
    me_y = lax.axis_index("gy")
    fine_x = fine_state.shape[1]
    fine_y = fine_state.shape[2]
    fine_z = fine_state.shape[3]
    own = region_state.shape[1]
    reg_y = region_state.shape[2]
    rows_each = reg_y // count_y
    reach_y = 6

    region_pay, lam_r, mu_r = lookup(region_material, material_table, region_state, 0.6, False)
    (fine_pay,) = lookup(fine_material, material_table, fine_state, 0.2, True)

    me_flat = lax.axis_index("gx") * count_y + me_y
    fine_lo = cyclic_from(fine_pay[:, :, -reach_y:], "gy", count_y, 1, me_y)
    fine_hi = cyclic_from(fine_pay[:, :, :reach_y], "gy", count_y, -1, me_y)
    reg_lo = cyclic_from(region_pay, flat, n_flat, 1, me_flat)
    reg_hi = cyclic_from(region_pay, flat, n_flat, -1, me_flat)
    lows, highs = [reg_lo], [reg_hi]
    for d in range(2, -(-2 // own) + 1):
        lows.insert(0, cyclic_from(region_pay, flat, n_flat, d, me_flat))
        highs.append(cyclic_from(region_pay, flat, n_flat, -d, me_flat))
    reg_ext = jnp.concatenate(
        [jnp.concatenate(lows, 1)[:, -2:], region_pay, jnp.concatenate(highs, 1)[:, :2]], 1
    )
    region_next = step_wide(
        reg_ext, reg_ext[9, 1:-1], region_state[3:], lam_r, mu_r, 0.6, 3.0, True
    )

    both = jnp.concatenate([region_state, region_next], 0).astype(jnp.bfloat16)
    both = jnp.pad(both, ((0, 0), (0, 0), (rows_each, rows_each), (0, 0)))
    send = jnp.concatenate(
        [both[:, :, rows_each * d: rows_each * (d + 3)] for d in range(count_y)], 2
    )
    band = lax.all_to_all(send, "gy", 2, 1, tiled=True)
    me_x = lax.axis_index("gx")
    band = jnp.concatenate(
        [
            cyclic_from(band[:, -3:], "gx", count_x, 1, me_x),
            band,
            cyclic_from(band[:, :3], "gx", count_x, -1, me_x),
        ],
        1,
    ).astype(jnp.float32)
    columns = band.shape[1] - 6
    high = lax.Precision.HIGH
    along_y_w = interp_matrix(fine_y, rows_each)
    zeros_w = jnp.zeros_like(along_y_w)
    tiles_w = jnp.concatenate(
        [
            jnp.concatenate([along_y_w, zeros_w, zeros_w], 1),
            jnp.concatenate([zeros_w, along_y_w, zeros_w], 1),
            jnp.concatenate([zeros_w, zeros_w, along_y_w], 1),
        ],
        0,
    )[fine_y - 4: 2 * fine_y + 4]
    along_x_w = interp_matrix(fine_x, columns)
    groups_w = jnp.concatenate(
        [
            jnp.pad(along_x_w[fine_x - 4:, columns - 3:], ((0, 0), (0, columns + 3))),
            jnp.pad(along_x_w, ((0, 0), (3, 3))),
            jnp.pad(along_x_w[:4, :3], ((0, 0), (columns + 3, 0))),
        ],
        0,
    )
    first = jnp.einsum("fa,cabz->cfbz", groups_w, band, precision=high)
    second = jnp.einsum("gb,cfbz->cfgz", tiles_w, first, precision=high)
    background = jnp.einsum(
        "kz,cfgz->cfgk", interp_matrix(fine_z, band.shape[3]), second, precision=high
    )
    along_x = ramp(me_x * fine_x - 4, fine_x + 8, count_x * fine_x, fine_x)
    along_y = ramp(me_y * fine_y - 4, fine_y + 8, count_y * fine_y, fine_y)
    relax = (0.1 + 0.4 * jnp.maximum(along_x[:, None], along_y[None, :]))[:, :, None]

    wide = jnp.concatenate([fine_lo, fine_pay, fine_hi], axis=2)
    full = x_halo(wide, reach_y)
    coef_w, lam_w, mu_w = full[9], full[10], full[11]
    state = full[:9]
    for sub in range(1, 4):
        off = 2 * (sub - 1)
        cols, rows = state.shape[1], state.shape[2]
        state = step_wide(
            state,
            coef_w[off + 1: off + cols - 1, off + 1: off + rows - 1],
            state[3:, 2:-2, 2:-2],
            lam_w[off + 2: off + cols - 2, off + 2: off + rows - 2],
            mu_w[off + 2: off + cols - 2, off + 2: off + rows - 2],
            0.2,
            1.0,
            False,
        )
        share = sub / 3.0
        bg = background[:, off: off + cols - 4, off: off + rows - 4]
        target = bg[:9] + share * (bg[9:] - bg[:9])
        state = state + relax[None, off: off + cols - 4, off: off + rows - 4] * (target - state)
    return (region_next, state)


def solution(mesh):
    return jax.shard_map(
        local,
        mesh=mesh,
        in_specs=(
            P(None, ("gx", "gy"), None, None),
            P(("gx", "gy"), None, None),
            P(None, "gx", "gy", None),
            P("gx", "gy", None),
            P(),
        ),
        out_specs=(P(None, ("gx", "gy"), None, None), P(None, "gx", "gy", None)),
        check_vma=False,
    )
```

```python
import jax
import jax.numpy as jnp
from jax import lax
from jax.sharding import PartitionSpec as P
from jax.experimental import pallas as pl
from jax.experimental.pallas import tpu as pltpu


def shifted(n, s):
    return [(i, i + s) for i in range(n) if 0 <= i + s < n]


def x_halo(field, width):
    nx = lax.axis_size("gx")
    from_left = lax.ppermute(field[:, -width:], "gx", shifted(nx, 1))
    from_right = lax.ppermute(field[:, :width], "gx", shifted(nx, -1))
    return jnp.concatenate([from_left, field, from_right], axis=1)


def props_kernel(step, code_ref, tab_ref, coef_ref, lam_ref, mu_ref):
    code = code_ref[...]
    rho = jnp.ones(code.shape, jnp.float32)
    lam = jnp.zeros(code.shape, jnp.float32)
    shear = jnp.zeros(code.shape, jnp.float32)
    for material in range(tab_ref.shape[1]):
        match = code == material + 1.0
        rho = jnp.where(match, tab_ref[0, material], rho)
        lam = jnp.where(match, tab_ref[1, material], lam)
        shear = jnp.where(match, tab_ref[2, material], shear)
    coef_ref[...] = jnp.where(code > 0.5, step / rho, 0.0)
    lam_ref[...] = lam
    mu_ref[...] = shear


def props(code, table, step):
    cell = jax.ShapeDtypeStruct(code.shape, jnp.float32)
    vmem = pl.BlockSpec(memory_space=pltpu.VMEM)
    return pl.pallas_call(
        lambda *refs: props_kernel(step, *refs),
        out_shape=(cell, cell, cell),
        in_specs=[vmem, pl.BlockSpec(memory_space=pltpu.SMEM)],
        out_specs=(vmem, vmem, vmem),
    )(code, table)


def along(f, axis):
    n = f.shape[axis]
    zero = jnp.zeros_like(lax.slice_in_dim(f, 0, 1, axis=axis))
    up = jnp.concatenate([lax.slice_in_dim(f, 1, n, axis=axis), zero], axis=axis)
    down = jnp.concatenate([zero, lax.slice_in_dim(f, 0, n - 1, axis=axis)], axis=axis)
    return up - down


def step_wide(ext, coef, stress0, lam, shear, step, spacing, y_local):
    scale = 0.5 / spacing
    s = ext[3:9]
    if y_local:
        mid_s = s[:, 1:-1]
        dx = lambda c: (s[c, 2:] - s[c, :-2]) * scale
        dy = lambda c: along(mid_s[c], 1) * scale
        dz = lambda c: along(mid_s[c], 2) * scale
        vel_old = ext[0:3, 1:-1]
    else:
        mid_s = s[:, 1:-1, 1:-1]
        dx = lambda c: (s[c, 2:, 1:-1] - s[c, :-2, 1:-1]) * scale
        dy = lambda c: (s[c, 1:-1, 2:] - s[c, 1:-1, :-2]) * scale
        dz = lambda c: along(mid_s[c], 2) * scale
        vel_old = ext[0:3, 1:-1, 1:-1]
    acc_x = dx(0) + dy(3) + dz(4)
    acc_y = dx(3) + dy(1) + dz(5)
    acc_z = dx(4) + dy(5) + dz(2)
    vel = vel_old + coef[None] * jnp.stack([acc_x, acc_y, acc_z])
    if y_local:
        inner = vel[:, 1:-1]
        gx = lambda c: (vel[c, 2:] - vel[c, :-2]) * scale
        gy = lambda c: along(inner[c], 1) * scale
        gz = lambda c: along(inner[c], 2) * scale
    else:
        inner = vel[:, 1:-1, 1:-1]
        gx = lambda c: (vel[c, 2:, 1:-1] - vel[c, :-2, 1:-1]) * scale
        gy = lambda c: (vel[c, 1:-1, 2:] - vel[c, 1:-1, :-2]) * scale
        gz = lambda c: along(inner[c], 2) * scale
    g_x0, g_y1, g_z2 = gx(0), gy(1), gz(2)
    spread = g_x0 + g_y1 + g_z2
    new_xx = stress0[0] + step * (lam * spread + 2.0 * shear * g_x0)
    new_yy = stress0[1] + step * (lam * spread + 2.0 * shear * g_y1)
    new_zz = stress0[2] + step * (lam * spread + 2.0 * shear * g_z2)
    new_xy = stress0[3] + step * shear * (gy(0) + gx(1))
    new_xz = stress0[4] + step * shear * (gz(0) + gx(2))
    new_yz = stress0[5] + step * shear * (gz(1) + gy(2))
    return jnp.concatenate(
        [inner, jnp.stack([new_xx, new_yy, new_zz, new_xy, new_xz, new_yz])], 0
    )


def interp_matrix(n_fine, n_coarse):
    fine_pos = jnp.arange(n_fine, dtype=jnp.int32)
    whole = fine_pos // 3
    rest = fine_pos - 3 * whole
    lower = jnp.where(rest == 0, whole - 1, whole)
    frac = jnp.where(rest == 0, 2.0 / 3.0, jnp.where(rest == 1, 0.0, 1.0 / 3.0)).astype(jnp.float32)
    below = lower < 0
    lower = jnp.where(below, 0, lower)
    frac = jnp.where(below, 0.0, frac)
    above = lower >= n_coarse - 1
    lower = jnp.where(above, n_coarse - 2, lower)
    frac = jnp.where(above, 1.0, frac)
    cols = jnp.arange(n_coarse, dtype=jnp.int32)
    low_hit = (cols[None, :] == lower[:, None]).astype(jnp.float32)
    high_hit = (cols[None, :] == lower[:, None] + 1).astype(jnp.float32)
    return (1.0 - frac)[:, None] * low_hit + frac[:, None] * high_hit


def ramp(first, count, total, tile):
    place = first + jnp.arange(count, dtype=jnp.int32)
    margin = jnp.minimum(place, total - 1 - place).astype(jnp.float32) + 0.5
    part = jnp.maximum(1.0 - margin / tile, 0.0)
    return part * part


def local(region_state, region_material, fine_state, fine_material, material_table):
    count_x = lax.axis_size("gx")
    count_y = lax.axis_size("gy")
    flat = ("gx", "gy")
    n_flat = count_x * count_y
    me_y = lax.axis_index("gy")
    fine_x = fine_state.shape[1]
    fine_y = fine_state.shape[2]
    fine_z = fine_state.shape[3]
    own = region_state.shape[1]
    reg_y = region_state.shape[2]
    rows_each = reg_y // count_y
    reach_y = 6

    region_pay = jnp.concatenate(
        [region_state, (region_material + 1).astype(jnp.float32)[None]], 0
    )
    fine_pay = jnp.concatenate([fine_state, (fine_material + 1).astype(jnp.float32)[None]], 0)

    fine_lo = lax.ppermute(fine_pay[:, :, -reach_y:], "gy", shifted(count_y, 1))
    fine_hi = lax.ppermute(fine_pay[:, :, :reach_y], "gy", shifted(count_y, -1))
    reg_lo = lax.ppermute(region_pay, flat, shifted(n_flat, 1))
    reg_hi = lax.ppermute(region_pay, flat, shifted(n_flat, -1))
    lows, highs = [reg_lo], [reg_hi]
    for d in range(2, -(-2 // own) + 1):
        lows.insert(0, lax.ppermute(region_pay, flat, shifted(n_flat, d)))
        highs.append(lax.ppermute(region_pay, flat, shifted(n_flat, -d)))
    reg_ext = jnp.concatenate(
        [jnp.concatenate(lows, 1)[:, -2:], region_pay, jnp.concatenate(highs, 1)[:, :2]], 1
    )
    coef_r, lam_r, mu_r = props(reg_ext[9, 1:-1], material_table, 0.6)
    region_next = step_wide(
        reg_ext, coef_r, region_state[3:], lam_r[1:-1], mu_r[1:-1], 0.6, 3.0, True
    )

    both = jnp.concatenate([region_state, region_next], 0).astype(jnp.bfloat16)
    both = jnp.pad(both, ((0, 0), (0, 0), (rows_each, rows_each), (0, 0)))
    send = jnp.concatenate(
        [both[:, :, rows_each * d: rows_each * (d + 3)] for d in range(count_y)], 2
    )
    band = lax.all_to_all(send, "gy", 2, 1, tiled=True).astype(jnp.float32)
    columns = band.shape[1]
    high = lax.Precision.HIGH
    along_y_w = interp_matrix(fine_y, rows_each)
    zeros_w = jnp.zeros_like(along_y_w)
    tiles_w = jnp.concatenate(
        [
            jnp.concatenate([along_y_w, zeros_w, zeros_w], 1),
            jnp.concatenate([zeros_w, along_y_w, zeros_w], 1),
            jnp.concatenate([zeros_w, zeros_w, along_y_w], 1),
        ],
        0,
    )[fine_y - 4: 2 * fine_y + 4]
    first = jnp.einsum("fa,cabz->cfbz", interp_matrix(fine_x, columns), band, precision=high)
    second = jnp.einsum("gb,cfbz->cfgz", tiles_w, first, precision=high)
    background = jnp.einsum(
        "kz,cfgz->cfgk", interp_matrix(fine_z, band.shape[3]), second, precision=high
    )
    along_x = ramp(lax.axis_index("gx") * fine_x, fine_x, count_x * fine_x, fine_x)
    along_y = ramp(me_y * fine_y - 4, fine_y + 8, count_y * fine_y, fine_y)
    relax = (0.1 + 0.4 * jnp.maximum(along_x[:, None], along_y[None, :]))[:, :, None]

    wide = jnp.concatenate([fine_lo, fine_pay, fine_hi], axis=2)
    state = wide[:9]
    coef_w = None
    for sub in range(1, 4):
        if sub == 1:
            ext = x_halo(wide, 2)
            coef_w, lam_w, mu_w = props(ext[9, 1:-1], material_table, 0.2)
            lam_w, mu_w = lam_w[1:-1], mu_w[1:-1]
            ext = ext[:9]
        else:
            ext = x_halo(state, 2)
        off = 2 * (sub - 1)
        rows = state.shape[2]
        state = step_wide(
            ext,
            coef_w[:, off + 1: off + rows - 1],
            state[3:, :, 2:-2],
            lam_w[:, off + 2: off + rows - 2],
            mu_w[:, off + 2: off + rows - 2],
            0.2,
            1.0,
            False,
        )
        share = sub / 3.0
        target = background[:9, :, off: off + rows - 4] + share * (
            background[9:, :, off: off + rows - 4] - background[:9, :, off: off + rows - 4]
        )
        state = state + relax[None, :, off: off + rows - 4] * (target - state)
    return (region_next, state)


def solution(mesh):
    return jax.shard_map(
        local,
        mesh=mesh,
        in_specs=(
            P(None, ("gx", "gy"), None, None),
            P(("gx", "gy"), None, None),
            P(None, "gx", "gy", None),
            P("gx", "gy", None),
            P(),
        ),
        out_specs=(P(None, ("gx", "gy"), None, None), P(None, "gx", "gy", None)),
        check_vma=False,
    )
```

```python
import jax
import jax.numpy as jnp
from jax import lax
from jax.sharding import PartitionSpec as P
from jax.experimental import pallas as pl
from jax.experimental.pallas import tpu as pltpu


def shifted(n, s):
    return [(i, i + s) for i in range(n) if 0 <= i + s < n]


def x_halo(field, width):
    nx = lax.axis_size("gx")
    from_left = lax.ppermute(field[:, :, -width:], "gx", shifted(nx, 1))
    from_right = lax.ppermute(field[:, :, :width], "gx", shifted(nx, -1))
    return jnp.concatenate([from_left, field, from_right], axis=2)


def lookup_kernel(step, extra, idx_ref, tab_ref, state_ref, pay_ref, *rest):
    idx = idx_ref[...]
    rho = jnp.zeros(idx.shape, jnp.float32)
    lam = jnp.zeros(idx.shape, jnp.float32)
    shear = jnp.zeros(idx.shape, jnp.float32)
    for material in range(tab_ref.shape[1]):
        match = idx == material
        rho = jnp.where(match, tab_ref[0, material], rho)
        lam = jnp.where(match, tab_ref[1, material], lam)
        shear = jnp.where(match, tab_ref[2, material], shear)
    comps = state_ref.shape[0]
    pay_ref[:comps] = state_ref[...]
    pay_ref[comps] = step / rho
    if extra:
        pay_ref[comps + 1] = lam
        pay_ref[comps + 2] = shear
    else:
        rest[0][...] = lam
        rest[1][...] = shear


def lookup(index, table, state, step, extra):
    comps = state.shape[0]
    vmem = pl.BlockSpec(memory_space=pltpu.VMEM)
    cell = jax.ShapeDtypeStruct(index.shape, jnp.float32)
    pay = jax.ShapeDtypeStruct((comps + (3 if extra else 1),) + index.shape, jnp.float32)
    outs = (pay,) if extra else (pay, cell, cell)
    return pl.pallas_call(
        lambda *refs: lookup_kernel(step, extra, *refs),
        out_shape=outs,
        in_specs=[vmem, pl.BlockSpec(memory_space=pltpu.SMEM), vmem],
        out_specs=tuple(vmem for _ in outs),
    )(index, table, state)


def along(f, axis):
    n = f.shape[axis]
    zero = jnp.zeros_like(lax.slice_in_dim(f, 0, 1, axis=axis))
    up = jnp.concatenate([lax.slice_in_dim(f, 1, n, axis=axis), zero], axis=axis)
    down = jnp.concatenate([zero, lax.slice_in_dim(f, 0, n - 1, axis=axis)], axis=axis)
    return up - down


def step_wide(ext, coef, stress0, lam, shear, step, spacing, y_local, swap=False):
    scale = 0.5 / spacing
    s = ext[3:9]
    if y_local:
        mid_s = s[:, 1:-1]
        dx = lambda c: (s[c, 2:] - s[c, :-2]) * scale
        dy = lambda c: along(mid_s[c], 1) * scale
        dz = lambda c: along(mid_s[c], 2) * scale
        vel_old = ext[0:3, 1:-1]
    else:
        mid_s = s[:, 1:-1, 1:-1]
        dx = lambda c: (s[c, 2:, 1:-1] - s[c, :-2, 1:-1]) * scale
        dy = lambda c: (s[c, 1:-1, 2:] - s[c, 1:-1, :-2]) * scale
        if swap:
            dx, dy = dy, dx
        dz = lambda c: along(mid_s[c], 2) * scale
        vel_old = ext[0:3, 1:-1, 1:-1]
    acc_x = dx(0) + dy(3) + dz(4)
    acc_y = dx(3) + dy(1) + dz(5)
    acc_z = dx(4) + dy(5) + dz(2)
    vel = vel_old + coef[None] * jnp.stack([acc_x, acc_y, acc_z])
    if y_local:
        inner = vel[:, 1:-1]
        gx = lambda c: (vel[c, 2:] - vel[c, :-2]) * scale
        gy = lambda c: along(inner[c], 1) * scale
        gz = lambda c: along(inner[c], 2) * scale
    else:
        inner = vel[:, 1:-1, 1:-1]
        gx = lambda c: (vel[c, 2:, 1:-1] - vel[c, :-2, 1:-1]) * scale
        gy = lambda c: (vel[c, 1:-1, 2:] - vel[c, 1:-1, :-2]) * scale
        if swap:
            gx, gy = gy, gx
        gz = lambda c: along(inner[c], 2) * scale
    g_x0, g_y1, g_z2 = gx(0), gy(1), gz(2)
    spread = g_x0 + g_y1 + g_z2
    new_xx = stress0[0] + step * (lam * spread + 2.0 * shear * g_x0)
    new_yy = stress0[1] + step * (lam * spread + 2.0 * shear * g_y1)
    new_zz = stress0[2] + step * (lam * spread + 2.0 * shear * g_z2)
    new_xy = stress0[3] + step * shear * (gy(0) + gx(1))
    new_xz = stress0[4] + step * shear * (gz(0) + gx(2))
    new_yz = stress0[5] + step * shear * (gz(1) + gy(2))
    return jnp.concatenate(
        [inner, jnp.stack([new_xx, new_yy, new_zz, new_xy, new_xz, new_yz])], 0
    )


def interp_matrix(n_fine, n_coarse):
    fine_pos = jnp.arange(n_fine, dtype=jnp.int32)
    whole = fine_pos // 3
    rest = fine_pos - 3 * whole
    lower = jnp.where(rest == 0, whole - 1, whole)
    frac = jnp.where(rest == 0, 2.0 / 3.0, jnp.where(rest == 1, 0.0, 1.0 / 3.0)).astype(jnp.float32)
    below = lower < 0
    lower = jnp.where(below, 0, lower)
    frac = jnp.where(below, 0.0, frac)
    above = lower >= n_coarse - 1
    lower = jnp.where(above, n_coarse - 2, lower)
    frac = jnp.where(above, 1.0, frac)
    cols = jnp.arange(n_coarse, dtype=jnp.int32)
    low_hit = (cols[None, :] == lower[:, None]).astype(jnp.float32)
    high_hit = (cols[None, :] == lower[:, None] + 1).astype(jnp.float32)
    return (1.0 - frac)[:, None] * low_hit + frac[:, None] * high_hit


def ramp(first, count, total, tile):
    place = first + jnp.arange(count, dtype=jnp.int32)
    margin = jnp.minimum(place, total - 1 - place).astype(jnp.float32) + 0.5
    part = jnp.maximum(1.0 - margin / tile, 0.0)
    return part * part


def local(region_state, region_material, fine_state, fine_material, material_table):
    count_x = lax.axis_size("gx")
    count_y = lax.axis_size("gy")
    flat = ("gx", "gy")
    n_flat = count_x * count_y
    me_y = lax.axis_index("gy")
    fine_x = fine_state.shape[1]
    fine_y = fine_state.shape[2]
    fine_z = fine_state.shape[3]
    own = region_state.shape[1]
    reg_y = region_state.shape[2]
    rows_each = reg_y // count_y
    reach_y = 6

    region_pay, lam_r, mu_r = lookup(region_material, material_table, region_state, 0.6, False)
    (fine_pay,) = lookup(
        jnp.transpose(fine_material, (1, 0, 2)),
        material_table,
        jnp.transpose(fine_state, (0, 2, 1, 3)),
        0.2,
        True,
    )

    fine_lo = lax.ppermute(fine_pay[:, -reach_y:], "gy", shifted(count_y, 1))
    fine_hi = lax.ppermute(fine_pay[:, :reach_y], "gy", shifted(count_y, -1))
    reg_lo = lax.ppermute(region_pay, flat, shifted(n_flat, 1))
    reg_hi = lax.ppermute(region_pay, flat, shifted(n_flat, -1))
    lows, highs = [reg_lo], [reg_hi]
    for d in range(2, -(-2 // own) + 1):
        lows.insert(0, lax.ppermute(region_pay, flat, shifted(n_flat, d)))
        highs.append(lax.ppermute(region_pay, flat, shifted(n_flat, -d)))
    reg_ext = jnp.concatenate(
        [jnp.concatenate(lows, 1)[:, -2:], region_pay, jnp.concatenate(highs, 1)[:, :2]], 1
    )
    region_next = step_wide(
        reg_ext, reg_ext[9, 1:-1], region_state[3:], lam_r, mu_r, 0.6, 3.0, True
    )

    both = jnp.concatenate([region_state, region_next], 0).astype(jnp.bfloat16)
    both = jnp.pad(both, ((0, 0), (0, 0), (rows_each, rows_each), (0, 0)))
    send = jnp.concatenate(
        [both[:, :, rows_each * d: rows_each * (d + 3)] for d in range(count_y)], 2
    )
    band = lax.all_to_all(send, "gy", 2, 1, tiled=True).astype(jnp.float32)
    columns = band.shape[1]
    high = lax.Precision.HIGH
    along_y_w = interp_matrix(fine_y, rows_each)
    zeros_w = jnp.zeros_like(along_y_w)
    tiles_w = jnp.concatenate(
        [
            jnp.concatenate([along_y_w, zeros_w, zeros_w], 1),
            jnp.concatenate([zeros_w, along_y_w, zeros_w], 1),
            jnp.concatenate([zeros_w, zeros_w, along_y_w], 1),
        ],
        0,
    )[fine_y - 4: 2 * fine_y + 4]
    first = jnp.einsum("fa,cabz->cfbz", interp_matrix(fine_x, columns), band, precision=high)
    second = jnp.einsum("gb,cfbz->cgfz", tiles_w, first, precision=high)
    background = jnp.einsum(
        "kz,cgfz->cgfk", interp_matrix(fine_z, band.shape[3]), second, precision=high
    )
    along_x = ramp(lax.axis_index("gx") * fine_x, fine_x, count_x * fine_x, fine_x)
    along_y = ramp(me_y * fine_y - 4, fine_y + 8, count_y * fine_y, fine_y)
    relax = (0.1 + 0.4 * jnp.maximum(along_y[:, None], along_x[None, :]))[:, :, None]

    wide = jnp.concatenate([fine_lo, fine_pay, fine_hi], axis=1)
    lam_w, mu_w = wide[10], wide[11]
    state = wide[:9]
    coef_w = None
    for sub in range(1, 4):
        if sub == 1:
            ext = x_halo(wide[:10], 2)
            coef_w = ext[9, :, 1:-1]
            ext = ext[:9]
        else:
            ext = x_halo(state, 2)
        off = 2 * (sub - 1)
        rows = state.shape[1]
        state = step_wide(
            ext,
            coef_w[off + 1: off + rows - 1],
            state[3:, 2:-2],
            lam_w[off + 2: off + rows - 2],
            mu_w[off + 2: off + rows - 2],
            0.2,
            1.0,
            False,
            swap=True,
        )
        share = sub / 3.0
        target = background[:9, off: off + rows - 4] + share * (
            background[9:, off: off + rows - 4] - background[:9, off: off + rows - 4]
        )
        state = state + relax[None, off: off + rows - 4] * (target - state)
    return (region_next, jnp.transpose(state, (0, 2, 1, 3)))


def solution(mesh):
    return jax.shard_map(
        local,
        mesh=mesh,
        in_specs=(
            P(None, ("gx", "gy"), None, None),
            P(("gx", "gy"), None, None),
            P(None, "gx", "gy", None),
            P("gx", "gy", None),
            P(),
        ),
        out_specs=(P(None, ("gx", "gy"), None, None), P(None, "gx", "gy", None)),
        check_vma=False,
    )
```

```python
import jax
import jax.numpy as jnp
from jax import lax
from jax.sharding import PartitionSpec as P
from jax.experimental import pallas as pl
from jax.experimental.pallas import tpu as pltpu


def shifted(n, s):
    return [(i, i + s) for i in range(n) if 0 <= i + s < n]


def x_halo(field, width):
    nx = lax.axis_size("gx")
    from_left = lax.ppermute(field[:, :, -width:], "gx", shifted(nx, 1))
    from_right = lax.ppermute(field[:, :, :width], "gx", shifted(nx, -1))
    return jnp.concatenate([from_left, field, from_right], axis=2)


def lookup_kernel(step, extra, idx_ref, tab_ref, state_ref, pay_ref, *rest):
    idx = idx_ref[...]
    rho = jnp.zeros(idx.shape, jnp.float32)
    lam = jnp.zeros(idx.shape, jnp.float32)
    shear = jnp.zeros(idx.shape, jnp.float32)
    for material in range(tab_ref.shape[1]):
        match = idx == material
        rho = jnp.where(match, tab_ref[0, material], rho)
        lam = jnp.where(match, tab_ref[1, material], lam)
        shear = jnp.where(match, tab_ref[2, material], shear)
    comps = state_ref.shape[0]
    pay_ref[:comps] = state_ref[...]
    pay_ref[comps] = step / rho
    if extra:
        pay_ref[comps + 1] = lam
        pay_ref[comps + 2] = shear
    else:
        rest[0][...] = lam
        rest[1][...] = shear


def lookup(index, table, state, step, extra):
    comps = state.shape[0]
    vmem = pl.BlockSpec(memory_space=pltpu.VMEM)
    cell = jax.ShapeDtypeStruct(index.shape, jnp.float32)
    pay = jax.ShapeDtypeStruct((comps + (3 if extra else 1),) + index.shape, jnp.float32)
    outs = (pay,) if extra else (pay, cell, cell)
    return pl.pallas_call(
        lambda *refs: lookup_kernel(step, extra, *refs),
        out_shape=outs,
        in_specs=[vmem, pl.BlockSpec(memory_space=pltpu.SMEM), vmem],
        out_specs=tuple(vmem for _ in outs),
    )(index, table, state)


def along(f, axis):
    n = f.shape[axis]
    zero = jnp.zeros_like(lax.slice_in_dim(f, 0, 1, axis=axis))
    up = jnp.concatenate([lax.slice_in_dim(f, 1, n, axis=axis), zero], axis=axis)
    down = jnp.concatenate([zero, lax.slice_in_dim(f, 0, n - 1, axis=axis)], axis=axis)
    return up - down


def step_wide(ext, coef, stress0, lam, shear, step, spacing, y_local, swap=False):
    scale = 0.5 / spacing
    s = ext[3:9]
    if y_local:
        mid_s = s[:, 1:-1]
        dx = lambda c: (s[c, 2:] - s[c, :-2]) * scale
        dy = lambda c: along(mid_s[c], 1) * scale
        dz = lambda c: along(mid_s[c], 2) * scale
        vel_old = ext[0:3, 1:-1]
    else:
        mid_s = s[:, 1:-1, 1:-1]
        dx = lambda c: (s[c, 2:, 1:-1] - s[c, :-2, 1:-1]) * scale
        dy = lambda c: (s[c, 1:-1, 2:] - s[c, 1:-1, :-2]) * scale
        if swap:
            dx, dy = dy, dx
        dz = lambda c: along(mid_s[c], 2) * scale
        vel_old = ext[0:3, 1:-1, 1:-1]
    acc_x = dx(0) + dy(3) + dz(4)
    acc_y = dx(3) + dy(1) + dz(5)
    acc_z = dx(4) + dy(5) + dz(2)
    vel = vel_old + coef[None] * jnp.stack([acc_x, acc_y, acc_z])
    if y_local:
        inner = vel[:, 1:-1]
        gx = lambda c: (vel[c, 2:] - vel[c, :-2]) * scale
        gy = lambda c: along(inner[c], 1) * scale
        gz = lambda c: along(inner[c], 2) * scale
    else:
        inner = vel[:, 1:-1, 1:-1]
        gx = lambda c: (vel[c, 2:, 1:-1] - vel[c, :-2, 1:-1]) * scale
        gy = lambda c: (vel[c, 1:-1, 2:] - vel[c, 1:-1, :-2]) * scale
        if swap:
            gx, gy = gy, gx
        gz = lambda c: along(inner[c], 2) * scale
    g_x0, g_y1, g_z2 = gx(0), gy(1), gz(2)
    spread = g_x0 + g_y1 + g_z2
    new_xx = stress0[0] + step * (lam * spread + 2.0 * shear * g_x0)
    new_yy = stress0[1] + step * (lam * spread + 2.0 * shear * g_y1)
    new_zz = stress0[2] + step * (lam * spread + 2.0 * shear * g_z2)
    new_xy = stress0[3] + step * shear * (gy(0) + gx(1))
    new_xz = stress0[4] + step * shear * (gz(0) + gx(2))
    new_yz = stress0[5] + step * shear * (gz(1) + gy(2))
    return jnp.concatenate(
        [inner, jnp.stack([new_xx, new_yy, new_zz, new_xy, new_xz, new_yz])], 0
    )


def interp_matrix(n_fine, n_coarse):
    fine_pos = jnp.arange(n_fine, dtype=jnp.int32)
    whole = fine_pos // 3
    rest = fine_pos - 3 * whole
    lower = jnp.where(rest == 0, whole - 1, whole)
    frac = jnp.where(rest == 0, 2.0 / 3.0, jnp.where(rest == 1, 0.0, 1.0 / 3.0)).astype(jnp.float32)
    below = lower < 0
    lower = jnp.where(below, 0, lower)
    frac = jnp.where(below, 0.0, frac)
    above = lower >= n_coarse - 1
    lower = jnp.where(above, n_coarse - 2, lower)
    frac = jnp.where(above, 1.0, frac)
    cols = jnp.arange(n_coarse, dtype=jnp.int32)
    low_hit = (cols[None, :] == lower[:, None]).astype(jnp.float32)
    high_hit = (cols[None, :] == lower[:, None] + 1).astype(jnp.float32)
    return (1.0 - frac)[:, None] * low_hit + frac[:, None] * high_hit


def ramp(first, count, total, tile):
    place = first + jnp.arange(count, dtype=jnp.int32)
    margin = jnp.minimum(place, total - 1 - place).astype(jnp.float32) + 0.5
    part = jnp.maximum(1.0 - margin / tile, 0.0)
    return part * part


def local(region_state, region_material, fine_state, fine_material, material_table):
    count_x = lax.axis_size("gx")
    count_y = lax.axis_size("gy")
    flat = ("gx", "gy")
    n_flat = count_x * count_y
    me_y = lax.axis_index("gy")
    fine_x = fine_state.shape[1]
    fine_y = fine_state.shape[2]
    fine_z = fine_state.shape[3]
    own = region_state.shape[1]
    reg_y = region_state.shape[2]
    rows_each = reg_y // count_y
    reach_y = 6

    region_pay, lam_r, mu_r = lookup(region_material, material_table, region_state, 0.6, False)
    (fine_pay,) = lookup(
        jnp.transpose(fine_material, (1, 0, 2)),
        material_table,
        jnp.transpose(fine_state, (0, 2, 1, 3)),
        0.2,
        True,
    )

    fine_lo = lax.ppermute(fine_pay[:, -reach_y:], "gy", shifted(count_y, 1))
    fine_hi = lax.ppermute(fine_pay[:, :reach_y], "gy", shifted(count_y, -1))
    reg_lo = lax.ppermute(region_pay, flat, shifted(n_flat, 1))
    reg_hi = lax.ppermute(region_pay, flat, shifted(n_flat, -1))
    lows, highs = [reg_lo], [reg_hi]
    for d in range(2, -(-2 // own) + 1):
        lows.insert(0, lax.ppermute(region_pay, flat, shifted(n_flat, d)))
        highs.append(lax.ppermute(region_pay, flat, shifted(n_flat, -d)))
    reg_ext = jnp.concatenate(
        [jnp.concatenate(lows, 1)[:, -2:], region_pay, jnp.concatenate(highs, 1)[:, :2]], 1
    )
    region_next = step_wide(
        reg_ext, reg_ext[9, 1:-1], region_state[3:], lam_r, mu_r, 0.6, 3.0, True
    )

    both = jnp.concatenate([region_state, region_next], 0).astype(jnp.bfloat16)
    both = jnp.pad(both, ((0, 0), (0, 0), (rows_each, rows_each), (0, 0)))
    chunks = []
    for shift in range(count_y):
        dest = (me_y + shift) % count_y
        piece = lax.dynamic_slice_in_dim(both, dest * rows_each, 3 * rows_each, axis=2)
        if shift:
            cycle = [(i, (i + shift) % count_y) for i in range(count_y)]
            piece = lax.ppermute(piece, "gy", cycle)
        chunks.append(piece)
    band = jnp.concatenate(chunks, 1).astype(jnp.float32)
    columns = band.shape[1]
    high = lax.Precision.HIGH
    along_y_w = interp_matrix(fine_y, rows_each)
    zeros_w = jnp.zeros_like(along_y_w)
    tiles_w = jnp.concatenate(
        [
            jnp.concatenate([along_y_w, zeros_w, zeros_w], 1),
            jnp.concatenate([zeros_w, along_y_w, zeros_w], 1),
            jnp.concatenate([zeros_w, zeros_w, along_y_w], 1),
        ],
        0,
    )[fine_y - 4: 2 * fine_y + 4]
    source = (me_y - jnp.arange(count_y)) % count_y
    order = (source[:, None] * own + jnp.arange(own)[None, :]).reshape(-1)
    along_x_w = jnp.take(interp_matrix(fine_x, columns), order, axis=1)
    first = jnp.einsum("fa,cabz->cfbz", along_x_w, band, precision=high)
    second = jnp.einsum("gb,cfbz->cgfz", tiles_w, first, precision=high)
    background = jnp.einsum(
        "kz,cgfz->cgfk", interp_matrix(fine_z, band.shape[3]), second, precision=high
    )
    along_x = ramp(lax.axis_index("gx") * fine_x, fine_x, count_x * fine_x, fine_x)
    along_y = ramp(me_y * fine_y - 4, fine_y + 8, count_y * fine_y, fine_y)
    relax = (0.1 + 0.4 * jnp.maximum(along_y[:, None], along_x[None, :]))[:, :, None]

    wide = jnp.concatenate([fine_lo, fine_pay, fine_hi], axis=1)
    lam_w, mu_w = wide[10], wide[11]
    state = wide[:9]
    coef_w = None
    for sub in range(1, 4):
        if sub == 1:
            ext = x_halo(wide[:10], 2)
            coef_w = ext[9, :, 1:-1]
            ext = ext[:9]
        else:
            ext = x_halo(state, 2)
        off = 2 * (sub - 1)
        rows = state.shape[1]
        state = step_wide(
            ext,
            coef_w[off + 1: off + rows - 1],
            state[3:, 2:-2],
            lam_w[off + 2: off + rows - 2],
            mu_w[off + 2: off + rows - 2],
            0.2,
            1.0,
            False,
            swap=True,
        )
        share = sub / 3.0
        target = background[:9, off: off + rows - 4] + share * (
            background[9:, off: off + rows - 4] - background[:9, off: off + rows - 4]
        )
        state = state + relax[None, off: off + rows - 4] * (target - state)
    return (region_next, jnp.transpose(state, (0, 2, 1, 3)))


def solution(mesh):
    return jax.shard_map(
        local,
        mesh=mesh,
        in_specs=(
            P(None, ("gx", "gy"), None, None),
            P(("gx", "gy"), None, None),
            P(None, "gx", "gy", None),
            P("gx", "gy", None),
            P(),
        ),
        out_specs=(P(None, ("gx", "gy"), None, None), P(None, "gx", "gy", None)),
        check_vma=False,
    )
```

```python
import numpy as np
import jax
import jax.numpy as jnp
from jax import lax
from jax.sharding import PartitionSpec as P
from jax.experimental import pallas as pl
from jax.experimental.pallas import tpu as pltpu


def shifted(n, s):
    return [(i, i + s) for i in range(n) if 0 <= i + s < n]


def x_halo(field, width):
    nx = lax.axis_size("gx")
    from_left = lax.ppermute(field[:, :, -width:], "gx", shifted(nx, 1))
    from_right = lax.ppermute(field[:, :, :width], "gx", shifted(nx, -1))
    return jnp.concatenate([from_left, field, from_right], axis=2)


def lookup_kernel(step, extra, idx_ref, tab_ref, state_ref, pay_ref, *rest):
    idx = idx_ref[...]
    rho = jnp.zeros(idx.shape, jnp.float32)
    lam = jnp.zeros(idx.shape, jnp.float32)
    shear = jnp.zeros(idx.shape, jnp.float32)
    for material in range(tab_ref.shape[1]):
        match = idx == material
        rho = jnp.where(match, tab_ref[0, material], rho)
        lam = jnp.where(match, tab_ref[1, material], lam)
        shear = jnp.where(match, tab_ref[2, material], shear)
    comps = state_ref.shape[0]
    pay_ref[:comps] = state_ref[...]
    pay_ref[comps] = step / rho
    if extra:
        pay_ref[comps + 1] = lam
        pay_ref[comps + 2] = shear
    else:
        rest[0][...] = lam
        rest[1][...] = shear


def lookup(index, table, state, step, extra):
    comps = state.shape[0]
    vmem = pl.BlockSpec(memory_space=pltpu.VMEM)
    cell = jax.ShapeDtypeStruct(index.shape, jnp.float32)
    pay = jax.ShapeDtypeStruct((comps + (3 if extra else 1),) + index.shape, jnp.float32)
    outs = (pay,) if extra else (pay, cell, cell)
    return pl.pallas_call(
        lambda *refs: lookup_kernel(step, extra, *refs),
        out_shape=outs,
        in_specs=[vmem, pl.BlockSpec(memory_space=pltpu.SMEM), vmem],
        out_specs=tuple(vmem for _ in outs),
    )(index, table, state)


def along(f, axis):
    n = f.shape[axis]
    zero = jnp.zeros_like(lax.slice_in_dim(f, 0, 1, axis=axis))
    up = jnp.concatenate([lax.slice_in_dim(f, 1, n, axis=axis), zero], axis=axis)
    down = jnp.concatenate([zero, lax.slice_in_dim(f, 0, n - 1, axis=axis)], axis=axis)
    return up - down


def step_wide(ext, coef, stress0, lam, shear, step, spacing, y_local, swap=False):
    scale = 0.5 / spacing
    s = ext[3:9]
    if y_local:
        mid_s = s[:, 1:-1]
        dx = lambda c: (s[c, 2:] - s[c, :-2]) * scale
        dy = lambda c: along(mid_s[c], 1) * scale
        dz = lambda c: along(mid_s[c], 2) * scale
        vel_old = ext[0:3, 1:-1]
    else:
        mid_s = s[:, 1:-1, 1:-1]
        dx = lambda c: (s[c, 2:, 1:-1] - s[c, :-2, 1:-1]) * scale
        dy = lambda c: (s[c, 1:-1, 2:] - s[c, 1:-1, :-2]) * scale
        if swap:
            dx, dy = dy, dx
        dz = lambda c: along(mid_s[c], 2) * scale
        vel_old = ext[0:3, 1:-1, 1:-1]
    acc_x = dx(0) + dy(3) + dz(4)
    acc_y = dx(3) + dy(1) + dz(5)
    acc_z = dx(4) + dy(5) + dz(2)
    vel = vel_old + coef[None] * jnp.stack([acc_x, acc_y, acc_z])
    if y_local:
        inner = vel[:, 1:-1]
        gx = lambda c: (vel[c, 2:] - vel[c, :-2]) * scale
        gy = lambda c: along(inner[c], 1) * scale
        gz = lambda c: along(inner[c], 2) * scale
    else:
        inner = vel[:, 1:-1, 1:-1]
        gx = lambda c: (vel[c, 2:, 1:-1] - vel[c, :-2, 1:-1]) * scale
        gy = lambda c: (vel[c, 1:-1, 2:] - vel[c, 1:-1, :-2]) * scale
        if swap:
            gx, gy = gy, gx
        gz = lambda c: along(inner[c], 2) * scale
    g_x0, g_y1, g_z2 = gx(0), gy(1), gz(2)
    spread = g_x0 + g_y1 + g_z2
    new_xx = stress0[0] + step * (lam * spread + 2.0 * shear * g_x0)
    new_yy = stress0[1] + step * (lam * spread + 2.0 * shear * g_y1)
    new_zz = stress0[2] + step * (lam * spread + 2.0 * shear * g_z2)
    new_xy = stress0[3] + step * shear * (gy(0) + gx(1))
    new_xz = stress0[4] + step * shear * (gz(0) + gx(2))
    new_yz = stress0[5] + step * shear * (gz(1) + gy(2))
    return jnp.concatenate(
        [inner, jnp.stack([new_xx, new_yy, new_zz, new_xy, new_xz, new_yz])], 0
    )


def interp_matrix(n_fine, n_coarse):
    fine_pos = jnp.arange(n_fine, dtype=jnp.int32)
    whole = fine_pos // 3
    rest = fine_pos - 3 * whole
    lower = jnp.where(rest == 0, whole - 1, whole)
    frac = jnp.where(rest == 0, 2.0 / 3.0, jnp.where(rest == 1, 0.0, 1.0 / 3.0)).astype(jnp.float32)
    below = lower < 0
    lower = jnp.where(below, 0, lower)
    frac = jnp.where(below, 0.0, frac)
    above = lower >= n_coarse - 1
    lower = jnp.where(above, n_coarse - 2, lower)
    frac = jnp.where(above, 1.0, frac)
    cols = jnp.arange(n_coarse, dtype=jnp.int32)
    low_hit = (cols[None, :] == lower[:, None]).astype(jnp.float32)
    high_hit = (cols[None, :] == lower[:, None] + 1).astype(jnp.float32)
    return (1.0 - frac)[:, None] * low_hit + frac[:, None] * high_hit


def interp_np(n_fine, n_coarse):
    fine_pos = np.arange(n_fine)
    whole = fine_pos // 3
    rest = fine_pos - 3 * whole
    lower = np.where(rest == 0, whole - 1, whole)
    frac = np.where(rest == 0, 2.0 / 3.0, np.where(rest == 1, 0.0, 1.0 / 3.0))
    frac = np.where(lower < 0, 0.0, frac)
    lower = np.where(lower < 0, 0, lower)
    above = lower >= n_coarse - 1
    lower = np.where(above, n_coarse - 2, lower)
    frac = np.where(above, 1.0, frac)
    out = np.zeros((n_fine, n_coarse))
    out[fine_pos, lower] += 1.0 - frac
    out[fine_pos, lower + 1] += frac
    return out


def ramp(first, count, total, tile):
    place = first + jnp.arange(count, dtype=jnp.int32)
    margin = jnp.minimum(place, total - 1 - place).astype(jnp.float32) + 0.5
    part = jnp.maximum(1.0 - margin / tile, 0.0)
    return part * part


def local(region_state, region_material, fine_state, fine_material, material_table):
    count_x = lax.axis_size("gx")
    count_y = lax.axis_size("gy")
    flat = ("gx", "gy")
    n_flat = count_x * count_y
    me_y = lax.axis_index("gy")
    fine_x = fine_state.shape[1]
    fine_y = fine_state.shape[2]
    fine_z = fine_state.shape[3]
    own = region_state.shape[1]
    reg_y = region_state.shape[2]
    rows_each = reg_y // count_y
    reach_y = 6

    region_pay, lam_r, mu_r = lookup(region_material, material_table, region_state, 0.6, False)
    (fine_pay,) = lookup(
        jnp.transpose(fine_material, (1, 0, 2)),
        material_table,
        jnp.transpose(fine_state, (0, 2, 1, 3)),
        0.2,
        True,
    )

    fine_lo = lax.ppermute(fine_pay[:, -reach_y:], "gy", shifted(count_y, 1))
    fine_hi = lax.ppermute(fine_pay[:, :reach_y], "gy", shifted(count_y, -1))
    reg_lo = lax.ppermute(region_pay, flat, shifted(n_flat, 1))
    reg_hi = lax.ppermute(region_pay, flat, shifted(n_flat, -1))
    lows, highs = [reg_lo], [reg_hi]
    for d in range(2, -(-2 // own) + 1):
        lows.insert(0, lax.ppermute(region_pay, flat, shifted(n_flat, d)))
        highs.append(lax.ppermute(region_pay, flat, shifted(n_flat, -d)))
    reg_ext = jnp.concatenate(
        [jnp.concatenate(lows, 1)[:, -2:], region_pay, jnp.concatenate(highs, 1)[:, :2]], 1
    )
    region_next = step_wide(
        reg_ext, reg_ext[9, 1:-1], region_state[3:], lam_r, mu_r, 0.6, 3.0, True
    )

    both = jnp.concatenate([region_state, region_next], 0).astype(jnp.bfloat16)
    tile_np = interp_np(fine_y, rows_each)
    blocks_np = np.kron(np.eye(3), tile_np)[fine_y - 4: 2 * fine_y + 4]
    used = np.nonzero(np.any(blocks_np != 0.0, axis=0))[0]
    lo, hi = int(used[0]), int(used[-1]) + 1
    both = jnp.pad(both, ((0, 0), (0, 0), (rows_each, rows_each), (0, 0)))
    send = jnp.concatenate(
        [both[:, :, rows_each * d + lo: rows_each * d + hi] for d in range(count_y)], 2
    )
    band = lax.all_to_all(send, "gy", 2, 1, tiled=True).astype(jnp.float32)
    columns = band.shape[1]
    high = lax.Precision.HIGH
    along_y_w = interp_matrix(fine_y, rows_each)
    zeros_w = jnp.zeros_like(along_y_w)
    tiles_w = jnp.concatenate(
        [
            jnp.concatenate([along_y_w, zeros_w, zeros_w], 1),
            jnp.concatenate([zeros_w, along_y_w, zeros_w], 1),
            jnp.concatenate([zeros_w, zeros_w, along_y_w], 1),
        ],
        0,
    )[fine_y - 4: 2 * fine_y + 4, lo:hi]
    first = jnp.einsum("fa,cabz->cfbz", interp_matrix(fine_x, columns), band, precision=high)
    second = jnp.einsum("gb,cfbz->cgfz", tiles_w, first, precision=high)
    background = jnp.einsum(
        "kz,cgfz->cgfk", interp_matrix(fine_z, band.shape[3]), second, precision=high
    )
    along_x = ramp(lax.axis_index("gx") * fine_x, fine_x, count_x * fine_x, fine_x)
    along_y = ramp(me_y * fine_y - 4, fine_y + 8, count_y * fine_y, fine_y)
    relax = (0.1 + 0.4 * jnp.maximum(along_y[:, None], along_x[None, :]))[:, :, None]

    wide = jnp.concatenate([fine_lo, fine_pay, fine_hi], axis=1)
    lam_w, mu_w = wide[10], wide[11]
    state = wide[:9]
    coef_w = None
    for sub in range(1, 4):
        if sub == 1:
            ext = x_halo(wide[:10], 2)
            coef_w = ext[9, :, 1:-1]
            ext = ext[:9]
        else:
            ext = x_halo(state, 2)
        off = 2 * (sub - 1)
        rows = state.shape[1]
        state = step_wide(
            ext,
            coef_w[off + 1: off + rows - 1],
            state[3:, 2:-2],
            lam_w[off + 2: off + rows - 2],
            mu_w[off + 2: off + rows - 2],
            0.2,
            1.0,
            False,
            swap=True,
        )
        share = sub / 3.0
        target = background[:9, off: off + rows - 4] + share * (
            background[9:, off: off + rows - 4] - background[:9, off: off + rows - 4]
        )
        state = state + relax[None, off: off + rows - 4] * (target - state)
    return (region_next, jnp.transpose(state, (0, 2, 1, 3)))


def solution(mesh):
    return jax.shard_map(
        local,
        mesh=mesh,
        in_specs=(
            P(None, ("gx", "gy"), None, None),
            P(("gx", "gy"), None, None),
            P(None, "gx", "gy", None),
            P("gx", "gy", None),
            P(),
        ),
        out_specs=(P(None, ("gx", "gy"), None, None), P(None, "gx", "gy", None)),
        check_vma=False,
    )
```

```python
import numpy as np
import jax
import jax.numpy as jnp
from jax import lax
from jax.sharding import PartitionSpec as P
from jax.experimental import pallas as pl
from jax.experimental.pallas import tpu as pltpu


def shifted(n, s):
    return [(i, i + s) for i in range(n) if 0 <= i + s < n]


def x_halo(field, width):
    nx = lax.axis_size("gx")
    from_left = lax.ppermute(field[:, :, -width:], "gx", shifted(nx, 1))
    from_right = lax.ppermute(field[:, :, :width], "gx", shifted(nx, -1))
    return jnp.concatenate([from_left, field, from_right], axis=2)


def lookup_kernel(step, extra, idx_ref, tab_ref, state_ref, pay_ref, *rest):
    idx = idx_ref[...]
    rho = jnp.zeros(idx.shape, jnp.float32)
    lam = jnp.zeros(idx.shape, jnp.float32)
    shear = jnp.zeros(idx.shape, jnp.float32)
    for material in range(tab_ref.shape[1]):
        match = idx == material
        rho = jnp.where(match, tab_ref[0, material], rho)
        lam = jnp.where(match, tab_ref[1, material], lam)
        shear = jnp.where(match, tab_ref[2, material], shear)
    comps = state_ref.shape[0]
    pay_ref[:comps] = state_ref[...]
    pay_ref[comps] = step / rho
    if extra:
        pay_ref[comps + 1] = lam
        pay_ref[comps + 2] = shear
    else:
        rest[0][...] = lam
        rest[1][...] = shear


def lookup(index, table, state, step, extra):
    comps = state.shape[0]
    vmem = pl.BlockSpec(memory_space=pltpu.VMEM)
    cell = jax.ShapeDtypeStruct(index.shape, jnp.float32)
    pay = jax.ShapeDtypeStruct((comps + (3 if extra else 1),) + index.shape, jnp.float32)
    outs = (pay,) if extra else (pay, cell, cell)
    return pl.pallas_call(
        lambda *refs: lookup_kernel(step, extra, *refs),
        out_shape=outs,
        in_specs=[vmem, pl.BlockSpec(memory_space=pltpu.SMEM), vmem],
        out_specs=tuple(vmem for _ in outs),
    )(index, table, state)


def along(f, axis):
    n = f.shape[axis]
    zero = jnp.zeros_like(lax.slice_in_dim(f, 0, 1, axis=axis))
    up = jnp.concatenate([lax.slice_in_dim(f, 1, n, axis=axis), zero], axis=axis)
    down = jnp.concatenate([zero, lax.slice_in_dim(f, 0, n - 1, axis=axis)], axis=axis)
    return up - down


def step_wide(ext, coef, stress0, lam, shear, step, spacing, y_local, swap=False):
    scale = 0.5 / spacing
    s = ext[3:9]
    if y_local:
        mid_s = s[:, 1:-1]
        dx = lambda c: (s[c, 2:] - s[c, :-2]) * scale
        dy = lambda c: along(mid_s[c], 1) * scale
        dz = lambda c: along(mid_s[c], 2) * scale
        vel_old = ext[0:3, 1:-1]
    else:
        mid_s = s[:, 1:-1, 1:-1]
        dx = lambda c: (s[c, 2:, 1:-1] - s[c, :-2, 1:-1]) * scale
        dy = lambda c: (s[c, 1:-1, 2:] - s[c, 1:-1, :-2]) * scale
        if swap:
            dx, dy = dy, dx
        dz = lambda c: along(mid_s[c], 2) * scale
        vel_old = ext[0:3, 1:-1, 1:-1]
    acc_x = dx(0) + dy(3) + dz(4)
    acc_y = dx(3) + dy(1) + dz(5)
    acc_z = dx(4) + dy(5) + dz(2)
    vel = vel_old + coef[None] * jnp.stack([acc_x, acc_y, acc_z])
    if y_local:
        inner = vel[:, 1:-1]
        gx = lambda c: (vel[c, 2:] - vel[c, :-2]) * scale
        gy = lambda c: along(inner[c], 1) * scale
        gz = lambda c: along(inner[c], 2) * scale
    else:
        inner = vel[:, 1:-1, 1:-1]
        gx = lambda c: (vel[c, 2:, 1:-1] - vel[c, :-2, 1:-1]) * scale
        gy = lambda c: (vel[c, 1:-1, 2:] - vel[c, 1:-1, :-2]) * scale
        if swap:
            gx, gy = gy, gx
        gz = lambda c: along(inner[c], 2) * scale
    g_x0, g_y1, g_z2 = gx(0), gy(1), gz(2)
    spread = g_x0 + g_y1 + g_z2
    new_xx = stress0[0] + step * (lam * spread + 2.0 * shear * g_x0)
    new_yy = stress0[1] + step * (lam * spread + 2.0 * shear * g_y1)
    new_zz = stress0[2] + step * (lam * spread + 2.0 * shear * g_z2)
    new_xy = stress0[3] + step * shear * (gy(0) + gx(1))
    new_xz = stress0[4] + step * shear * (gz(0) + gx(2))
    new_yz = stress0[5] + step * shear * (gz(1) + gy(2))
    return jnp.concatenate(
        [inner, jnp.stack([new_xx, new_yy, new_zz, new_xy, new_xz, new_yz])], 0
    )


def interp_matrix(n_fine, n_coarse):
    fine_pos = jnp.arange(n_fine, dtype=jnp.int32)
    whole = fine_pos // 3
    rest = fine_pos - 3 * whole
    lower = jnp.where(rest == 0, whole - 1, whole)
    frac = jnp.where(rest == 0, 2.0 / 3.0, jnp.where(rest == 1, 0.0, 1.0 / 3.0)).astype(jnp.float32)
    below = lower < 0
    lower = jnp.where(below, 0, lower)
    frac = jnp.where(below, 0.0, frac)
    above = lower >= n_coarse - 1
    lower = jnp.where(above, n_coarse - 2, lower)
    frac = jnp.where(above, 1.0, frac)
    cols = jnp.arange(n_coarse, dtype=jnp.int32)
    low_hit = (cols[None, :] == lower[:, None]).astype(jnp.float32)
    high_hit = (cols[None, :] == lower[:, None] + 1).astype(jnp.float32)
    return (1.0 - frac)[:, None] * low_hit + frac[:, None] * high_hit


def interp_np(n_fine, n_coarse):
    fine_pos = np.arange(n_fine)
    whole = fine_pos // 3
    rest = fine_pos - 3 * whole
    lower = np.where(rest == 0, whole - 1, whole)
    frac = np.where(rest == 0, 2.0 / 3.0, np.where(rest == 1, 0.0, 1.0 / 3.0))
    frac = np.where(lower < 0, 0.0, frac)
    lower = np.where(lower < 0, 0, lower)
    above = lower >= n_coarse - 1
    lower = np.where(above, n_coarse - 2, lower)
    frac = np.where(above, 1.0, frac)
    out = np.zeros((n_fine, n_coarse))
    out[fine_pos, lower] += 1.0 - frac
    out[fine_pos, lower + 1] += frac
    return out


def ramp(first, count, total, tile):
    place = first + jnp.arange(count, dtype=jnp.int32)
    margin = jnp.minimum(place, total - 1 - place).astype(jnp.float32) + 0.5
    part = jnp.maximum(1.0 - margin / tile, 0.0)
    return part * part


def local(region_state, region_material, fine_state, fine_material, material_table):
    count_x = lax.axis_size("gx")
    count_y = lax.axis_size("gy")
    flat = ("gx", "gy")
    n_flat = count_x * count_y
    me_y = lax.axis_index("gy")
    fine_x = fine_state.shape[1]
    fine_y = fine_state.shape[2]
    fine_z = fine_state.shape[3]
    own = region_state.shape[1]
    reg_y = region_state.shape[2]
    rows_each = reg_y // count_y
    reach_y = 6

    region_pay, lam_r, mu_r = lookup(region_material, material_table, region_state, 0.6, False)
    (fine_pay,) = lookup(
        jnp.transpose(fine_material, (1, 0, 2)),
        material_table,
        jnp.transpose(fine_state, (0, 2, 1, 3)),
        0.2,
        True,
    )

    fine_lo = lax.ppermute(fine_pay[:, -reach_y:], "gy", shifted(count_y, 1))
    fine_hi = lax.ppermute(fine_pay[:, :reach_y], "gy", shifted(count_y, -1))
    reg_lo = lax.ppermute(region_pay, flat, shifted(n_flat, 1))
    reg_hi = lax.ppermute(region_pay, flat, shifted(n_flat, -1))
    lows, highs = [reg_lo], [reg_hi]
    for d in range(2, -(-2 // own) + 1):
        lows.insert(0, lax.ppermute(region_pay, flat, shifted(n_flat, d)))
        highs.append(lax.ppermute(region_pay, flat, shifted(n_flat, -d)))
    reg_ext = jnp.concatenate(
        [jnp.concatenate(lows, 1)[:, -2:], region_pay, jnp.concatenate(highs, 1)[:, :2]], 1
    )
    region_next = step_wide(
        reg_ext, reg_ext[9, 1:-1], region_state[3:], lam_r, mu_r, 0.6, 3.0, True
    )

    tile_np = interp_np(fine_y, rows_each)
    blocks_np = np.kron(np.eye(3), tile_np)[fine_y - 4: 2 * fine_y + 4]
    used = np.nonzero(np.any(blocks_np != 0.0, axis=0))[0]
    lo, hi = int(used[0]), int(used[-1]) + 1
    high = lax.Precision.HIGH
    along_y_w = interp_matrix(fine_y, rows_each)
    zeros_w = jnp.zeros_like(along_y_w)
    tiles_w = jnp.concatenate(
        [
            jnp.concatenate([along_y_w, zeros_w, zeros_w], 1),
            jnp.concatenate([zeros_w, along_y_w, zeros_w], 1),
            jnp.concatenate([zeros_w, zeros_w, along_y_w], 1),
        ],
        0,
    )[fine_y - 4: 2 * fine_y + 4, lo:hi]

    def background_of(part):
        part = jnp.pad(
            part.astype(jnp.bfloat16), ((0, 0), (0, 0), (rows_each, rows_each), (0, 0))
        )
        send = jnp.concatenate(
            [part[:, :, rows_each * d + lo: rows_each * d + hi] for d in range(count_y)], 2
        )
        band = lax.all_to_all(send, "gy", 2, 1, tiled=True).astype(jnp.float32)
        first = jnp.einsum(
            "fa,cabz->cfbz", interp_matrix(fine_x, band.shape[1]), band, precision=high
        )
        second = jnp.einsum("gb,cfbz->cgfz", tiles_w, first, precision=high)
        return jnp.einsum(
            "kz,cgfz->cgfk", interp_matrix(fine_z, band.shape[3]), second, precision=high
        )

    background = jnp.concatenate(
        [background_of(region_state), background_of(region_next)], 0
    )
    along_x = ramp(lax.axis_index("gx") * fine_x, fine_x, count_x * fine_x, fine_x)
    along_y = ramp(me_y * fine_y - 4, fine_y + 8, count_y * fine_y, fine_y)
    relax = (0.1 + 0.4 * jnp.maximum(along_y[:, None], along_x[None, :]))[:, :, None]

    wide = jnp.concatenate([fine_lo, fine_pay, fine_hi], axis=1)
    lam_w, mu_w = wide[10], wide[11]
    state = wide[:9]
    coef_w = None
    for sub in range(1, 4):
        if sub == 1:
            ext = x_halo(wide[:10], 2)
            coef_w = ext[9, :, 1:-1]
            ext = ext[:9]
        else:
            ext = x_halo(state, 2)
        off = 2 * (sub - 1)
        rows = state.shape[1]
        state = step_wide(
            ext,
            coef_w[off + 1: off + rows - 1],
            state[3:, 2:-2],
            lam_w[off + 2: off + rows - 2],
            mu_w[off + 2: off + rows - 2],
            0.2,
            1.0,
            False,
            swap=True,
        )
        share = sub / 3.0
        target = background[:9, off: off + rows - 4] + share * (
            background[9:, off: off + rows - 4] - background[:9, off: off + rows - 4]
        )
        state = state + relax[None, off: off + rows - 4] * (target - state)
    return (region_next, jnp.transpose(state, (0, 2, 1, 3)))


def solution(mesh):
    return jax.shard_map(
        local,
        mesh=mesh,
        in_specs=(
            P(None, ("gx", "gy"), None, None),
            P(("gx", "gy"), None, None),
            P(None, "gx", "gy", None),
            P("gx", "gy", None),
            P(),
        ),
        out_specs=(P(None, ("gx", "gy"), None, None), P(None, "gx", "gy", None)),
        check_vma=False,
    )
```

```python
import numpy as np
import jax
import jax.numpy as jnp
from jax import lax
from jax.sharding import PartitionSpec as P
from jax.experimental import pallas as pl
from jax.experimental.pallas import tpu as pltpu


def shifted(n, s):
    return [(i, i + s) for i in range(n) if 0 <= i + s < n]


def x_halo(field, width):
    nx = lax.axis_size("gx")
    me = lax.axis_index("gx")
    cycle = [(i, (i + 1) % nx) for i in range(nx)]
    back = [(j, i) for i, j in cycle]
    from_left = lax.ppermute(field[:, :, -width:], "gx", cycle)
    from_right = lax.ppermute(field[:, :, :width], "gx", back)
    from_left = jnp.where(me > 0, from_left, 0.0)
    from_right = jnp.where(me < nx - 1, from_right, 0.0)
    return jnp.concatenate([from_left, field, from_right], axis=2)


def lookup_kernel(step, extra, idx_ref, tab_ref, state_ref, pay_ref, *rest):
    idx = idx_ref[...]
    rho = jnp.zeros(idx.shape, jnp.float32)
    lam = jnp.zeros(idx.shape, jnp.float32)
    shear = jnp.zeros(idx.shape, jnp.float32)
    for material in range(tab_ref.shape[1]):
        match = idx == material
        rho = jnp.where(match, tab_ref[0, material], rho)
        lam = jnp.where(match, tab_ref[1, material], lam)
        shear = jnp.where(match, tab_ref[2, material], shear)
    comps = state_ref.shape[0]
    pay_ref[:comps] = state_ref[...]
    pay_ref[comps] = step / rho
    if extra:
        pay_ref[comps + 1] = lam
        pay_ref[comps + 2] = shear
    else:
        rest[0][...] = lam
        rest[1][...] = shear


def lookup(index, table, state, step, extra):
    comps = state.shape[0]
    vmem = pl.BlockSpec(memory_space=pltpu.VMEM)
    cell = jax.ShapeDtypeStruct(index.shape, jnp.float32)
    pay = jax.ShapeDtypeStruct((comps + (3 if extra else 1),) + index.shape, jnp.float32)
    outs = (pay,) if extra else (pay, cell, cell)
    return pl.pallas_call(
        lambda *refs: lookup_kernel(step, extra, *refs),
        out_shape=outs,
        in_specs=[vmem, pl.BlockSpec(memory_space=pltpu.SMEM), vmem],
        out_specs=tuple(vmem for _ in outs),
    )(index, table, state)


def along(f, axis):
    n = f.shape[axis]
    zero = jnp.zeros_like(lax.slice_in_dim(f, 0, 1, axis=axis))
    up = jnp.concatenate([lax.slice_in_dim(f, 1, n, axis=axis), zero], axis=axis)
    down = jnp.concatenate([zero, lax.slice_in_dim(f, 0, n - 1, axis=axis)], axis=axis)
    return up - down


def step_wide(ext, coef, stress0, lam, shear, step, spacing, y_local, swap=False):
    scale = 0.5 / spacing
    s = ext[3:9]
    if y_local:
        mid_s = s[:, 1:-1]
        dx = lambda c: (s[c, 2:] - s[c, :-2]) * scale
        dy = lambda c: along(mid_s[c], 1) * scale
        dz = lambda c: along(mid_s[c], 2) * scale
        vel_old = ext[0:3, 1:-1]
    else:
        mid_s = s[:, 1:-1, 1:-1]
        dx = lambda c: (s[c, 2:, 1:-1] - s[c, :-2, 1:-1]) * scale
        dy = lambda c: (s[c, 1:-1, 2:] - s[c, 1:-1, :-2]) * scale
        if swap:
            dx, dy = dy, dx
        dz = lambda c: along(mid_s[c], 2) * scale
        vel_old = ext[0:3, 1:-1, 1:-1]
    acc_x = dx(0) + dy(3) + dz(4)
    acc_y = dx(3) + dy(1) + dz(5)
    acc_z = dx(4) + dy(5) + dz(2)
    vel = vel_old + coef[None] * jnp.stack([acc_x, acc_y, acc_z])
    if y_local:
        inner = vel[:, 1:-1]
        gx = lambda c: (vel[c, 2:] - vel[c, :-2]) * scale
        gy = lambda c: along(inner[c], 1) * scale
        gz = lambda c: along(inner[c], 2) * scale
    else:
        inner = vel[:, 1:-1, 1:-1]
        gx = lambda c: (vel[c, 2:, 1:-1] - vel[c, :-2, 1:-1]) * scale
        gy = lambda c: (vel[c, 1:-1, 2:] - vel[c, 1:-1, :-2]) * scale
        if swap:
            gx, gy = gy, gx
        gz = lambda c: along(inner[c], 2) * scale
    g_x0, g_y1, g_z2 = gx(0), gy(1), gz(2)
    spread = g_x0 + g_y1 + g_z2
    new_xx = stress0[0] + step * (lam * spread + 2.0 * shear * g_x0)
    new_yy = stress0[1] + step * (lam * spread + 2.0 * shear * g_y1)
    new_zz = stress0[2] + step * (lam * spread + 2.0 * shear * g_z2)
    new_xy = stress0[3] + step * shear * (gy(0) + gx(1))
    new_xz = stress0[4] + step * shear * (gz(0) + gx(2))
    new_yz = stress0[5] + step * shear * (gz(1) + gy(2))
    return jnp.concatenate(
        [inner, jnp.stack([new_xx, new_yy, new_zz, new_xy, new_xz, new_yz])], 0
    )


def interp_matrix(n_fine, n_coarse):
    fine_pos = jnp.arange(n_fine, dtype=jnp.int32)
    whole = fine_pos // 3
    rest = fine_pos - 3 * whole
    lower = jnp.where(rest == 0, whole - 1, whole)
    frac = jnp.where(rest == 0, 2.0 / 3.0, jnp.where(rest == 1, 0.0, 1.0 / 3.0)).astype(jnp.float32)
    below = lower < 0
    lower = jnp.where(below, 0, lower)
    frac = jnp.where(below, 0.0, frac)
    above = lower >= n_coarse - 1
    lower = jnp.where(above, n_coarse - 2, lower)
    frac = jnp.where(above, 1.0, frac)
    cols = jnp.arange(n_coarse, dtype=jnp.int32)
    low_hit = (cols[None, :] == lower[:, None]).astype(jnp.float32)
    high_hit = (cols[None, :] == lower[:, None] + 1).astype(jnp.float32)
    return (1.0 - frac)[:, None] * low_hit + frac[:, None] * high_hit


def interp_np(n_fine, n_coarse):
    fine_pos = np.arange(n_fine)
    whole = fine_pos // 3
    rest = fine_pos - 3 * whole
    lower = np.where(rest == 0, whole - 1, whole)
    frac = np.where(rest == 0, 2.0 / 3.0, np.where(rest == 1, 0.0, 1.0 / 3.0))
    frac = np.where(lower < 0, 0.0, frac)
    lower = np.where(lower < 0, 0, lower)
    above = lower >= n_coarse - 1
    lower = np.where(above, n_coarse - 2, lower)
    frac = np.where(above, 1.0, frac)
    out = np.zeros((n_fine, n_coarse))
    out[fine_pos, lower] += 1.0 - frac
    out[fine_pos, lower + 1] += frac
    return out


def ramp(first, count, total, tile):
    place = first + jnp.arange(count, dtype=jnp.int32)
    margin = jnp.minimum(place, total - 1 - place).astype(jnp.float32) + 0.5
    part = jnp.maximum(1.0 - margin / tile, 0.0)
    return part * part


def local(region_state, region_material, fine_state, fine_material, material_table):
    count_x = lax.axis_size("gx")
    count_y = lax.axis_size("gy")
    flat = ("gx", "gy")
    n_flat = count_x * count_y
    me_y = lax.axis_index("gy")
    fine_x = fine_state.shape[1]
    fine_y = fine_state.shape[2]
    fine_z = fine_state.shape[3]
    own = region_state.shape[1]
    reg_y = region_state.shape[2]
    rows_each = reg_y // count_y
    reach_y = 6

    region_pay, lam_r, mu_r = lookup(region_material, material_table, region_state, 0.6, False)
    (fine_pay,) = lookup(
        jnp.transpose(fine_material, (1, 0, 2)),
        material_table,
        jnp.transpose(fine_state, (0, 2, 1, 3)),
        0.2,
        True,
    )

    fine_lo = lax.ppermute(fine_pay[:, -reach_y:], "gy", shifted(count_y, 1))
    fine_hi = lax.ppermute(fine_pay[:, :reach_y], "gy", shifted(count_y, -1))
    reg_lo = lax.ppermute(region_pay, flat, shifted(n_flat, 1))
    reg_hi = lax.ppermute(region_pay, flat, shifted(n_flat, -1))
    lows, highs = [reg_lo], [reg_hi]
    for d in range(2, -(-2 // own) + 1):
        lows.insert(0, lax.ppermute(region_pay, flat, shifted(n_flat, d)))
        highs.append(lax.ppermute(region_pay, flat, shifted(n_flat, -d)))
    reg_ext = jnp.concatenate(
        [jnp.concatenate(lows, 1)[:, -2:], region_pay, jnp.concatenate(highs, 1)[:, :2]], 1
    )
    region_next = step_wide(
        reg_ext, reg_ext[9, 1:-1], region_state[3:], lam_r, mu_r, 0.6, 3.0, True
    )

    both = jnp.concatenate([region_state, region_next], 0).astype(jnp.bfloat16)
    tile_np = interp_np(fine_y, rows_each)
    blocks_np = np.kron(np.eye(3), tile_np)[fine_y - 4: 2 * fine_y + 4]
    used = np.nonzero(np.any(blocks_np != 0.0, axis=0))[0]
    lo, hi = int(used[0]), int(used[-1]) + 1
    both = jnp.pad(both, ((0, 0), (0, 0), (rows_each, rows_each), (0, 0)))
    send = jnp.concatenate(
        [both[:, :, rows_each * d + lo: rows_each * d + hi] for d in range(count_y)], 2
    )
    band = lax.all_to_all(send, "gy", 2, 1, tiled=True).astype(jnp.float32)
    columns = band.shape[1]
    high = lax.Precision.HIGH
    along_y_w = interp_matrix(fine_y, rows_each)
    zeros_w = jnp.zeros_like(along_y_w)
    tiles_w = jnp.concatenate(
        [
            jnp.concatenate([along_y_w, zeros_w, zeros_w], 1),
            jnp.concatenate([zeros_w, along_y_w, zeros_w], 1),
            jnp.concatenate([zeros_w, zeros_w, along_y_w], 1),
        ],
        0,
    )[fine_y - 4: 2 * fine_y + 4, lo:hi]
    first = jnp.einsum("fa,cabz->cfbz", interp_matrix(fine_x, columns), band, precision=high)
    second = jnp.einsum("gb,cfbz->cgfz", tiles_w, first, precision=high)
    background = jnp.einsum(
        "kz,cgfz->cgfk", interp_matrix(fine_z, band.shape[3]), second, precision=high
    )
    along_x = ramp(lax.axis_index("gx") * fine_x, fine_x, count_x * fine_x, fine_x)
    along_y = ramp(me_y * fine_y - 4, fine_y + 8, count_y * fine_y, fine_y)
    relax = (0.1 + 0.4 * jnp.maximum(along_y[:, None], along_x[None, :]))[:, :, None]

    wide = jnp.concatenate([fine_lo, fine_pay, fine_hi], axis=1)
    lam_w, mu_w = wide[10], wide[11]
    state = wide[:9]
    coef_w = None
    for sub in range(1, 4):
        if sub == 1:
            ext = x_halo(wide[:10], 2)
            coef_w = ext[9, :, 1:-1]
            ext = ext[:9]
        else:
            ext = x_halo(state, 2)
        off = 2 * (sub - 1)
        rows = state.shape[1]
        state = step_wide(
            ext,
            coef_w[off + 1: off + rows - 1],
            state[3:, 2:-2],
            lam_w[off + 2: off + rows - 2],
            mu_w[off + 2: off + rows - 2],
            0.2,
            1.0,
            False,
            swap=True,
        )
        share = sub / 3.0
        target = background[:9, off: off + rows - 4] + share * (
            background[9:, off: off + rows - 4] - background[:9, off: off + rows - 4]
        )
        state = state + relax[None, off: off + rows - 4] * (target - state)
    return (region_next, jnp.transpose(state, (0, 2, 1, 3)))


def solution(mesh):
    return jax.shard_map(
        local,
        mesh=mesh,
        in_specs=(
            P(None, ("gx", "gy"), None, None),
            P(("gx", "gy"), None, None),
            P(None, "gx", "gy", None),
            P("gx", "gy", None),
            P(),
        ),
        out_specs=(P(None, ("gx", "gy"), None, None), P(None, "gx", "gy", None)),
        check_vma=False,
    )
```

```python
import numpy as np
import jax
import jax.numpy as jnp
from jax import lax
from jax.sharding import PartitionSpec as P
from jax.experimental import pallas as pl
from jax.experimental.pallas import tpu as pltpu


def shifted(n, s):
    return [(i, i + s) for i in range(n) if 0 <= i + s < n]


def from_cycle(field, axis, n, d, me):
    got = lax.ppermute(field, axis, [(i, (i + d) % n) for i in range(n)])
    return jnp.where((me - d >= 0) & (me - d < n), got, 0.0)


def x_halo(field, width):
    nx = lax.axis_size("gx")
    me = lax.axis_index("gx")
    cycle = [(i, (i + 1) % nx) for i in range(nx)]
    back = [(j, i) for i, j in cycle]
    from_left = lax.ppermute(field[:, :, -width:], "gx", cycle)
    from_right = lax.ppermute(field[:, :, :width], "gx", back)
    from_left = jnp.where(me > 0, from_left, 0.0)
    from_right = jnp.where(me < nx - 1, from_right, 0.0)
    return jnp.concatenate([from_left, field, from_right], axis=2)


def lookup_kernel(step, extra, idx_ref, tab_ref, state_ref, pay_ref, *rest):
    idx = idx_ref[...]
    rho = jnp.zeros(idx.shape, jnp.float32)
    lam = jnp.zeros(idx.shape, jnp.float32)
    shear = jnp.zeros(idx.shape, jnp.float32)
    for material in range(tab_ref.shape[1]):
        match = idx == material
        rho = jnp.where(match, tab_ref[0, material], rho)
        lam = jnp.where(match, tab_ref[1, material], lam)
        shear = jnp.where(match, tab_ref[2, material], shear)
    comps = state_ref.shape[0]
    pay_ref[:comps] = state_ref[...]
    pay_ref[comps] = step / rho
    if extra:
        pay_ref[comps + 1] = lam
        pay_ref[comps + 2] = shear
    else:
        rest[0][...] = lam
        rest[1][...] = shear


def lookup(index, table, state, step, extra):
    comps = state.shape[0]
    vmem = pl.BlockSpec(memory_space=pltpu.VMEM)
    cell = jax.ShapeDtypeStruct(index.shape, jnp.float32)
    pay = jax.ShapeDtypeStruct((comps + (3 if extra else 1),) + index.shape, jnp.float32)
    outs = (pay,) if extra else (pay, cell, cell)
    return pl.pallas_call(
        lambda *refs: lookup_kernel(step, extra, *refs),
        out_shape=outs,
        in_specs=[vmem, pl.BlockSpec(memory_space=pltpu.SMEM), vmem],
        out_specs=tuple(vmem for _ in outs),
    )(index, table, state)


def along(f, axis):
    n = f.shape[axis]
    zero = jnp.zeros_like(lax.slice_in_dim(f, 0, 1, axis=axis))
    up = jnp.concatenate([lax.slice_in_dim(f, 1, n, axis=axis), zero], axis=axis)
    down = jnp.concatenate([zero, lax.slice_in_dim(f, 0, n - 1, axis=axis)], axis=axis)
    return up - down


def step_wide(ext, coef, stress0, lam, shear, step, spacing, y_local, swap=False):
    scale = 0.5 / spacing
    s = ext[3:9]
    if y_local:
        mid_s = s[:, 1:-1]
        dx = lambda c: (s[c, 2:] - s[c, :-2]) * scale
        dy = lambda c: along(mid_s[c], 1) * scale
        dz = lambda c: along(mid_s[c], 2) * scale
        vel_old = ext[0:3, 1:-1]
    else:
        mid_s = s[:, 1:-1, 1:-1]
        dx = lambda c: (s[c, 2:, 1:-1] - s[c, :-2, 1:-1]) * scale
        dy = lambda c: (s[c, 1:-1, 2:] - s[c, 1:-1, :-2]) * scale
        if swap:
            dx, dy = dy, dx
        dz = lambda c: along(mid_s[c], 2) * scale
        vel_old = ext[0:3, 1:-1, 1:-1]
    acc_x = dx(0) + dy(3) + dz(4)
    acc_y = dx(3) + dy(1) + dz(5)
    acc_z = dx(4) + dy(5) + dz(2)
    vel = vel_old + coef[None] * jnp.stack([acc_x, acc_y, acc_z])
    if y_local:
        inner = vel[:, 1:-1]
        gx = lambda c: (vel[c, 2:] - vel[c, :-2]) * scale
        gy = lambda c: along(inner[c], 1) * scale
        gz = lambda c: along(inner[c], 2) * scale
    else:
        inner = vel[:, 1:-1, 1:-1]
        gx = lambda c: (vel[c, 2:, 1:-1] - vel[c, :-2, 1:-1]) * scale
        gy = lambda c: (vel[c, 1:-1, 2:] - vel[c, 1:-1, :-2]) * scale
        if swap:
            gx, gy = gy, gx
        gz = lambda c: along(inner[c], 2) * scale
    g_x0, g_y1, g_z2 = gx(0), gy(1), gz(2)
    spread = g_x0 + g_y1 + g_z2
    new_xx = stress0[0] + step * (lam * spread + 2.0 * shear * g_x0)
    new_yy = stress0[1] + step * (lam * spread + 2.0 * shear * g_y1)
    new_zz = stress0[2] + step * (lam * spread + 2.0 * shear * g_z2)
    new_xy = stress0[3] + step * shear * (gy(0) + gx(1))
    new_xz = stress0[4] + step * shear * (gz(0) + gx(2))
    new_yz = stress0[5] + step * shear * (gz(1) + gy(2))
    return jnp.concatenate(
        [inner, jnp.stack([new_xx, new_yy, new_zz, new_xy, new_xz, new_yz])], 0
    )


def interp_matrix(n_fine, n_coarse):
    fine_pos = jnp.arange(n_fine, dtype=jnp.int32)
    whole = fine_pos // 3
    rest = fine_pos - 3 * whole
    lower = jnp.where(rest == 0, whole - 1, whole)
    frac = jnp.where(rest == 0, 2.0 / 3.0, jnp.where(rest == 1, 0.0, 1.0 / 3.0)).astype(jnp.float32)
    below = lower < 0
    lower = jnp.where(below, 0, lower)
    frac = jnp.where(below, 0.0, frac)
    above = lower >= n_coarse - 1
    lower = jnp.where(above, n_coarse - 2, lower)
    frac = jnp.where(above, 1.0, frac)
    cols = jnp.arange(n_coarse, dtype=jnp.int32)
    low_hit = (cols[None, :] == lower[:, None]).astype(jnp.float32)
    high_hit = (cols[None, :] == lower[:, None] + 1).astype(jnp.float32)
    return (1.0 - frac)[:, None] * low_hit + frac[:, None] * high_hit


def interp_np(n_fine, n_coarse):
    fine_pos = np.arange(n_fine)
    whole = fine_pos // 3
    rest = fine_pos - 3 * whole
    lower = np.where(rest == 0, whole - 1, whole)
    frac = np.where(rest == 0, 2.0 / 3.0, np.where(rest == 1, 0.0, 1.0 / 3.0))
    frac = np.where(lower < 0, 0.0, frac)
    lower = np.where(lower < 0, 0, lower)
    above = lower >= n_coarse - 1
    lower = np.where(above, n_coarse - 2, lower)
    frac = np.where(above, 1.0, frac)
    out = np.zeros((n_fine, n_coarse))
    out[fine_pos, lower] += 1.0 - frac
    out[fine_pos, lower + 1] += frac
    return out


def ramp(first, count, total, tile):
    place = first + jnp.arange(count, dtype=jnp.int32)
    margin = jnp.minimum(place, total - 1 - place).astype(jnp.float32) + 0.5
    part = jnp.maximum(1.0 - margin / tile, 0.0)
    return part * part


def local(region_state, region_material, fine_state, fine_material, material_table):
    count_x = lax.axis_size("gx")
    count_y = lax.axis_size("gy")
    flat = ("gx", "gy")
    n_flat = count_x * count_y
    me_y = lax.axis_index("gy")
    fine_x = fine_state.shape[1]
    fine_y = fine_state.shape[2]
    fine_z = fine_state.shape[3]
    own = region_state.shape[1]
    reg_y = region_state.shape[2]
    rows_each = reg_y // count_y
    reach_y = 6

    region_pay, lam_r, mu_r = lookup(region_material, material_table, region_state, 0.6, False)
    (fine_pay,) = lookup(
        jnp.transpose(fine_material, (1, 0, 2)),
        material_table,
        jnp.transpose(fine_state, (0, 2, 1, 3)),
        0.2,
        True,
    )

    me_flat = lax.axis_index("gx") * count_y + me_y
    fine_lo = from_cycle(fine_pay[:, -reach_y:], "gy", count_y, 1, me_y)
    fine_hi = from_cycle(fine_pay[:, :reach_y], "gy", count_y, -1, me_y)
    reg_lo = from_cycle(region_pay, flat, n_flat, 1, me_flat)
    reg_hi = from_cycle(region_pay, flat, n_flat, -1, me_flat)
    lows, highs = [reg_lo], [reg_hi]
    for d in range(2, -(-2 // own) + 1):
        lows.insert(0, from_cycle(region_pay, flat, n_flat, d, me_flat))
        highs.append(from_cycle(region_pay, flat, n_flat, -d, me_flat))
    reg_ext = jnp.concatenate(
        [jnp.concatenate(lows, 1)[:, -2:], region_pay, jnp.concatenate(highs, 1)[:, :2]], 1
    )
    region_next = step_wide(
        reg_ext, reg_ext[9, 1:-1], region_state[3:], lam_r, mu_r, 0.6, 3.0, True
    )

    both = jnp.concatenate([region_state, region_next], 0).astype(jnp.bfloat16)
    tile_np = interp_np(fine_y, rows_each)
    blocks_np = np.kron(np.eye(3), tile_np)[fine_y - 4: 2 * fine_y + 4]
    used = np.nonzero(np.any(blocks_np != 0.0, axis=0))[0]
    lo, hi = int(used[0]), int(used[-1]) + 1
    both = jnp.pad(both, ((0, 0), (0, 0), (rows_each, rows_each), (0, 0)))
    send = jnp.concatenate(
        [both[:, :, rows_each * d + lo: rows_each * d + hi] for d in range(count_y)], 2
    )
    band = lax.all_to_all(send, "gy", 2, 1, tiled=True).astype(jnp.float32)
    columns = band.shape[1]
    high = lax.Precision.HIGH
    along_y_w = interp_matrix(fine_y, rows_each)
    zeros_w = jnp.zeros_like(along_y_w)
    tiles_w = jnp.concatenate(
        [
            jnp.concatenate([along_y_w, zeros_w, zeros_w], 1),
            jnp.concatenate([zeros_w, along_y_w, zeros_w], 1),
            jnp.concatenate([zeros_w, zeros_w, along_y_w], 1),
        ],
        0,
    )[fine_y - 4: 2 * fine_y + 4, lo:hi]
    first = jnp.einsum("fa,cabz->cfbz", interp_matrix(fine_x, columns), band, precision=high)
    second = jnp.einsum("gb,cfbz->cgfz", tiles_w, first, precision=high)
    background = jnp.einsum(
        "kz,cgfz->cgfk", interp_matrix(fine_z, band.shape[3]), second, precision=high
    )
    along_x = ramp(lax.axis_index("gx") * fine_x, fine_x, count_x * fine_x, fine_x)
    along_y = ramp(me_y * fine_y - 4, fine_y + 8, count_y * fine_y, fine_y)
    relax = (0.1 + 0.4 * jnp.maximum(along_y[:, None], along_x[None, :]))[:, :, None]

    wide = jnp.concatenate([fine_lo, fine_pay, fine_hi], axis=1)
    lam_w, mu_w = wide[10], wide[11]
    state = wide[:9]
    coef_w = None
    for sub in range(1, 4):
        if sub == 1:
            ext = x_halo(wide[:10], 2)
            coef_w = ext[9, :, 1:-1]
            ext = ext[:9]
        else:
            ext = x_halo(state, 2)
        off = 2 * (sub - 1)
        rows = state.shape[1]
        state = step_wide(
            ext,
            coef_w[off + 1: off + rows - 1],
            state[3:, 2:-2],
            lam_w[off + 2: off + rows - 2],
            mu_w[off + 2: off + rows - 2],
            0.2,
            1.0,
            False,
            swap=True,
        )
        share = sub / 3.0
        target = background[:9, off: off + rows - 4] + share * (
            background[9:, off: off + rows - 4] - background[:9, off: off + rows - 4]
        )
        state = state + relax[None, off: off + rows - 4] * (target - state)
    return (region_next, jnp.transpose(state, (0, 2, 1, 3)))


def solution(mesh):
    return jax.shard_map(
        local,
        mesh=mesh,
        in_specs=(
            P(None, ("gx", "gy"), None, None),
            P(("gx", "gy"), None, None),
            P(None, "gx", "gy", None),
            P("gx", "gy", None),
            P(),
        ),
        out_specs=(P(None, ("gx", "gy"), None, None), P(None, "gx", "gy", None)),
        check_vma=False,
    )
```

```python
import numpy as np
import jax
import jax.numpy as jnp
from jax import lax
from jax.sharding import PartitionSpec as P
from jax.experimental import pallas as pl
from jax.experimental.pallas import tpu as pltpu


def shifted(n, s):
    return [(i, i + s) for i in range(n) if 0 <= i + s < n]


def from_cycle(field, axis, n, d, me):
    got = lax.ppermute(field, axis, [(i, (i + d) % n) for i in range(n)])
    return jnp.where((me - d >= 0) & (me - d < n), got, 0.0)


def x_halo(field, width):
    nx = lax.axis_size("gx")
    me = lax.axis_index("gx")
    cycle = [(i, (i + 1) % nx) for i in range(nx)]
    back = [(j, i) for i, j in cycle]
    from_left = lax.ppermute(field[:, :, -width:], "gx", cycle)
    from_right = lax.ppermute(field[:, :, :width], "gx", back)
    from_left = jnp.where(me > 0, from_left, 0.0)
    from_right = jnp.where(me < nx - 1, from_right, 0.0)
    return jnp.concatenate([from_left, field, from_right], axis=2)


def lookup_kernel(step, extra, idx_ref, tab_ref, state_ref, pay_ref, *rest):
    idx = idx_ref[...]
    rho = jnp.zeros(idx.shape, jnp.float32)
    lam = jnp.zeros(idx.shape, jnp.float32)
    shear = jnp.zeros(idx.shape, jnp.float32)
    for material in range(tab_ref.shape[1]):
        match = idx == material
        rho = jnp.where(match, tab_ref[0, material], rho)
        lam = jnp.where(match, tab_ref[1, material], lam)
        shear = jnp.where(match, tab_ref[2, material], shear)
    comps = state_ref.shape[0]
    pay_ref[:comps] = state_ref[...]
    pay_ref[comps] = step / rho
    if extra:
        pay_ref[comps + 1] = lam
        pay_ref[comps + 2] = shear
    else:
        rest[0][...] = lam
        rest[1][...] = shear


def lookup(index, table, state, step, extra):
    comps = state.shape[0]
    vmem = pl.BlockSpec(memory_space=pltpu.VMEM)
    cell = jax.ShapeDtypeStruct(index.shape, jnp.float32)
    pay = jax.ShapeDtypeStruct((comps + (3 if extra else 1),) + index.shape, jnp.float32)
    outs = (pay,) if extra else (pay, cell, cell)
    return pl.pallas_call(
        lambda *refs: lookup_kernel(step, extra, *refs),
        out_shape=outs,
        in_specs=[vmem, pl.BlockSpec(memory_space=pltpu.SMEM), vmem],
        out_specs=tuple(vmem for _ in outs),
    )(index, table, state)


def along(f, axis):
    n = f.shape[axis]
    zero = jnp.zeros_like(lax.slice_in_dim(f, 0, 1, axis=axis))
    up = jnp.concatenate([lax.slice_in_dim(f, 1, n, axis=axis), zero], axis=axis)
    down = jnp.concatenate([zero, lax.slice_in_dim(f, 0, n - 1, axis=axis)], axis=axis)
    return up - down


def step_wide(ext, coef, stress0, lam, shear, step, spacing, y_local, swap=False):
    scale = 0.5 / spacing
    s = ext[3:9]
    if y_local:
        mid_s = s[:, 1:-1]
        dx = lambda c: (s[c, 2:] - s[c, :-2]) * scale
        dy = lambda c: along(mid_s[c], 1) * scale
        dz = lambda c: along(mid_s[c], 2) * scale
        vel_old = ext[0:3, 1:-1]
    else:
        mid_s = s[:, 1:-1, 1:-1]
        dx = lambda c: (s[c, 2:, 1:-1] - s[c, :-2, 1:-1]) * scale
        dy = lambda c: (s[c, 1:-1, 2:] - s[c, 1:-1, :-2]) * scale
        if swap:
            dx, dy = dy, dx
        dz = lambda c: along(mid_s[c], 2) * scale
        vel_old = ext[0:3, 1:-1, 1:-1]
    acc_x = dx(0) + dy(3) + dz(4)
    acc_y = dx(3) + dy(1) + dz(5)
    acc_z = dx(4) + dy(5) + dz(2)
    vel = vel_old + coef[None] * jnp.stack([acc_x, acc_y, acc_z])
    if y_local:
        inner = vel[:, 1:-1]
        gx = lambda c: (vel[c, 2:] - vel[c, :-2]) * scale
        gy = lambda c: along(inner[c], 1) * scale
        gz = lambda c: along(inner[c], 2) * scale
    else:
        inner = vel[:, 1:-1, 1:-1]
        gx = lambda c: (vel[c, 2:, 1:-1] - vel[c, :-2, 1:-1]) * scale
        gy = lambda c: (vel[c, 1:-1, 2:] - vel[c, 1:-1, :-2]) * scale
        if swap:
            gx, gy = gy, gx
        gz = lambda c: along(inner[c], 2) * scale
    g_x0, g_y1, g_z2 = gx(0), gy(1), gz(2)
    spread = g_x0 + g_y1 + g_z2
    new_xx = stress0[0] + step * (lam * spread + 2.0 * shear * g_x0)
    new_yy = stress0[1] + step * (lam * spread + 2.0 * shear * g_y1)
    new_zz = stress0[2] + step * (lam * spread + 2.0 * shear * g_z2)
    new_xy = stress0[3] + step * shear * (gy(0) + gx(1))
    new_xz = stress0[4] + step * shear * (gz(0) + gx(2))
    new_yz = stress0[5] + step * shear * (gz(1) + gy(2))
    return jnp.concatenate(
        [inner, jnp.stack([new_xx, new_yy, new_zz, new_xy, new_xz, new_yz])], 0
    )


def interp_matrix(n_fine, n_coarse):
    fine_pos = jnp.arange(n_fine, dtype=jnp.int32)
    whole = fine_pos // 3
    rest = fine_pos - 3 * whole
    lower = jnp.where(rest == 0, whole - 1, whole)
    frac = jnp.where(rest == 0, 2.0 / 3.0, jnp.where(rest == 1, 0.0, 1.0 / 3.0)).astype(jnp.float32)
    below = lower < 0
    lower = jnp.where(below, 0, lower)
    frac = jnp.where(below, 0.0, frac)
    above = lower >= n_coarse - 1
    lower = jnp.where(above, n_coarse - 2, lower)
    frac = jnp.where(above, 1.0, frac)
    cols = jnp.arange(n_coarse, dtype=jnp.int32)
    low_hit = (cols[None, :] == lower[:, None]).astype(jnp.float32)
    high_hit = (cols[None, :] == lower[:, None] + 1).astype(jnp.float32)
    return (1.0 - frac)[:, None] * low_hit + frac[:, None] * high_hit


def interp_np(n_fine, n_coarse):
    fine_pos = np.arange(n_fine)
    whole = fine_pos // 3
    rest = fine_pos - 3 * whole
    lower = np.where(rest == 0, whole - 1, whole)
    frac = np.where(rest == 0, 2.0 / 3.0, np.where(rest == 1, 0.0, 1.0 / 3.0))
    frac = np.where(lower < 0, 0.0, frac)
    lower = np.where(lower < 0, 0, lower)
    above = lower >= n_coarse - 1
    lower = np.where(above, n_coarse - 2, lower)
    frac = np.where(above, 1.0, frac)
    out = np.zeros((n_fine, n_coarse))
    out[fine_pos, lower] += 1.0 - frac
    out[fine_pos, lower + 1] += frac
    return out


def ramp(first, count, total, tile):
    place = first + jnp.arange(count, dtype=jnp.int32)
    margin = jnp.minimum(place, total - 1 - place).astype(jnp.float32) + 0.5
    part = jnp.maximum(1.0 - margin / tile, 0.0)
    return part * part


def local(region_state, region_material, fine_state, fine_material, material_table):
    count_x = lax.axis_size("gx")
    count_y = lax.axis_size("gy")
    flat = ("gx", "gy")
    n_flat = count_x * count_y
    me_y = lax.axis_index("gy")
    fine_x = fine_state.shape[1]
    fine_y = fine_state.shape[2]
    fine_z = fine_state.shape[3]
    own = region_state.shape[1]
    reg_y = region_state.shape[2]
    rows_each = reg_y // count_y
    reach_y = 6

    region_pay, lam_r, mu_r = lookup(region_material, material_table, region_state, 0.6, False)
    (fine_pay,) = lookup(
        jnp.transpose(fine_material, (1, 0, 2)),
        material_table,
        jnp.transpose(fine_state, (0, 2, 1, 3)),
        0.2,
        True,
    )

    me_flat = lax.axis_index("gx") * count_y + me_y
    fine_xw = x_halo(fine_pay, 2)
    fine_lo = from_cycle(fine_xw[:, -reach_y:], "gy", count_y, 1, me_y)
    fine_hi = from_cycle(fine_xw[:, :reach_y], "gy", count_y, -1, me_y)
    reg_lo = from_cycle(region_pay, flat, n_flat, 1, me_flat)
    reg_hi = from_cycle(region_pay, flat, n_flat, -1, me_flat)
    lows, highs = [reg_lo], [reg_hi]
    for d in range(2, -(-2 // own) + 1):
        lows.insert(0, from_cycle(region_pay, flat, n_flat, d, me_flat))
        highs.append(from_cycle(region_pay, flat, n_flat, -d, me_flat))
    reg_ext = jnp.concatenate(
        [jnp.concatenate(lows, 1)[:, -2:], region_pay, jnp.concatenate(highs, 1)[:, :2]], 1
    )
    region_next = step_wide(
        reg_ext, reg_ext[9, 1:-1], region_state[3:], lam_r, mu_r, 0.6, 3.0, True
    )

    both = jnp.concatenate([region_state, region_next], 0).astype(jnp.bfloat16)
    tile_np = interp_np(fine_y, rows_each)
    blocks_np = np.kron(np.eye(3), tile_np)[fine_y - 4: 2 * fine_y + 4]
    used = np.nonzero(np.any(blocks_np != 0.0, axis=0))[0]
    lo, hi = int(used[0]), int(used[-1]) + 1
    both = jnp.pad(both, ((0, 0), (0, 0), (rows_each, rows_each), (0, 0)))
    send = jnp.concatenate(
        [both[:, :, rows_each * d + lo: rows_each * d + hi] for d in range(count_y)], 2
    )
    band = lax.all_to_all(send, "gy", 2, 1, tiled=True).astype(jnp.float32)
    columns = band.shape[1]
    high = lax.Precision.HIGH
    along_y_w = interp_matrix(fine_y, rows_each)
    zeros_w = jnp.zeros_like(along_y_w)
    tiles_w = jnp.concatenate(
        [
            jnp.concatenate([along_y_w, zeros_w, zeros_w], 1),
            jnp.concatenate([zeros_w, along_y_w, zeros_w], 1),
            jnp.concatenate([zeros_w, zeros_w, along_y_w], 1),
        ],
        0,
    )[fine_y - 4: 2 * fine_y + 4, lo:hi]
    first = jnp.einsum("fa,cabz->cfbz", interp_matrix(fine_x, columns), band, precision=high)
    second = jnp.einsum("gb,cfbz->cgfz", tiles_w, first, precision=high)
    background = jnp.einsum(
        "kz,cgfz->cgfk", interp_matrix(fine_z, band.shape[3]), second, precision=high
    )
    along_x = ramp(lax.axis_index("gx") * fine_x, fine_x, count_x * fine_x, fine_x)
    along_y = ramp(me_y * fine_y - 4, fine_y + 8, count_y * fine_y, fine_y)
    relax = (0.1 + 0.4 * jnp.maximum(along_y[:, None], along_x[None, :]))[:, :, None]

    wide = jnp.concatenate([fine_lo, fine_xw, fine_hi], axis=1)
    coef_w, lam_w, mu_w = wide[9, :, 1:-1], wide[10, :, 2:-2], wide[11, :, 2:-2]
    state = wide[:9, :, 2:-2]
    for sub in range(1, 4):
        if sub == 1:
            ext = wide[:9]
        else:
            ext = x_halo(state, 2)
        off = 2 * (sub - 1)
        rows = state.shape[1]
        state = step_wide(
            ext,
            coef_w[off + 1: off + rows - 1],
            state[3:, 2:-2],
            lam_w[off + 2: off + rows - 2],
            mu_w[off + 2: off + rows - 2],
            0.2,
            1.0,
            False,
            swap=True,
        )
        share = sub / 3.0
        target = background[:9, off: off + rows - 4] + share * (
            background[9:, off: off + rows - 4] - background[:9, off: off + rows - 4]
        )
        state = state + relax[None, off: off + rows - 4] * (target - state)
    return (region_next, jnp.transpose(state, (0, 2, 1, 3)))


def solution(mesh):
    return jax.shard_map(
        local,
        mesh=mesh,
        in_specs=(
            P(None, ("gx", "gy"), None, None),
            P(("gx", "gy"), None, None),
            P(None, "gx", "gy", None),
            P("gx", "gy", None),
            P(),
        ),
        out_specs=(P(None, ("gx", "gy"), None, None), P(None, "gx", "gy", None)),
        check_vma=False,
    )
```

```python
import numpy as np
import jax
import jax.numpy as jnp
from jax import lax
from jax.sharding import PartitionSpec as P
from jax.experimental import pallas as pl
from jax.experimental.pallas import tpu as pltpu


def shifted(n, s):
    return [(i, i + s) for i in range(n) if 0 <= i + s < n]


def from_cycle(field, axis, n, d, me):
    got = lax.ppermute(field, axis, [(i, (i + d) % n) for i in range(n)])
    return jnp.where((me - d >= 0) & (me - d < n), got, 0.0)


def x_halo(field, width):
    nx = lax.axis_size("gx")
    me = lax.axis_index("gx")
    cycle = [(i, (i + 1) % nx) for i in range(nx)]
    back = [(j, i) for i, j in cycle]
    from_left = lax.ppermute(field[:, :, -width:], "gx", cycle)
    from_right = lax.ppermute(field[:, :, :width], "gx", back)
    from_left = jnp.where(me > 0, from_left, 0.0)
    from_right = jnp.where(me < nx - 1, from_right, 0.0)
    return jnp.concatenate([from_left, field, from_right], axis=2)


def lookup_kernel(step, extra, idx_ref, tab_ref, state_ref, pay_ref, *rest):
    idx = idx_ref[...]
    rho = jnp.zeros(idx.shape, jnp.float32)
    lam = jnp.zeros(idx.shape, jnp.float32)
    shear = jnp.zeros(idx.shape, jnp.float32)
    for material in range(tab_ref.shape[1]):
        match = idx == material
        rho = jnp.where(match, tab_ref[0, material], rho)
        lam = jnp.where(match, tab_ref[1, material], lam)
        shear = jnp.where(match, tab_ref[2, material], shear)
    comps = state_ref.shape[0]
    pay_ref[:comps] = state_ref[...]
    pay_ref[comps] = step / rho
    if extra:
        pay_ref[comps + 1] = lam
        pay_ref[comps + 2] = shear
    else:
        rest[0][...] = lam
        rest[1][...] = shear


def lookup(index, table, state, step, extra):
    comps = state.shape[0]
    vmem = pl.BlockSpec(memory_space=pltpu.VMEM)
    cell = jax.ShapeDtypeStruct(index.shape, jnp.float32)
    pay = jax.ShapeDtypeStruct((comps + (3 if extra else 1),) + index.shape, jnp.float32)
    outs = (pay,) if extra else (pay, cell, cell)
    return pl.pallas_call(
        lambda *refs: lookup_kernel(step, extra, *refs),
        out_shape=outs,
        in_specs=[vmem, pl.BlockSpec(memory_space=pltpu.SMEM), vmem],
        out_specs=tuple(vmem for _ in outs),
    )(index, table, state)


def along(f, axis):
    n = f.shape[axis]
    zero = jnp.zeros_like(lax.slice_in_dim(f, 0, 1, axis=axis))
    up = jnp.concatenate([lax.slice_in_dim(f, 1, n, axis=axis), zero], axis=axis)
    down = jnp.concatenate([zero, lax.slice_in_dim(f, 0, n - 1, axis=axis)], axis=axis)
    return up - down


def step_wide(ext, coef, stress0, lam, shear, step, spacing, y_local, swap=False):
    scale = 0.5 / spacing
    s = ext[3:9]
    if y_local:
        mid_s = s[:, 1:-1]
        dx = lambda c: (s[c, 2:] - s[c, :-2]) * scale
        dy = lambda c: along(mid_s[c], 1) * scale
        dz = lambda c: along(mid_s[c], 2) * scale
        vel_old = ext[0:3, 1:-1]
    else:
        mid_s = s[:, 1:-1, 1:-1]
        dx = lambda c: (s[c, 2:, 1:-1] - s[c, :-2, 1:-1]) * scale
        dy = lambda c: (s[c, 1:-1, 2:] - s[c, 1:-1, :-2]) * scale
        if swap:
            dx, dy = dy, dx
        dz = lambda c: along(mid_s[c], 2) * scale
        vel_old = ext[0:3, 1:-1, 1:-1]
    acc_x = dx(0) + dy(3) + dz(4)
    acc_y = dx(3) + dy(1) + dz(5)
    acc_z = dx(4) + dy(5) + dz(2)
    vel = vel_old + coef[None] * jnp.stack([acc_x, acc_y, acc_z])
    if y_local:
        inner = vel[:, 1:-1]
        gx = lambda c: (vel[c, 2:] - vel[c, :-2]) * scale
        gy = lambda c: along(inner[c], 1) * scale
        gz = lambda c: along(inner[c], 2) * scale
    else:
        inner = vel[:, 1:-1, 1:-1]
        gx = lambda c: (vel[c, 2:, 1:-1] - vel[c, :-2, 1:-1]) * scale
        gy = lambda c: (vel[c, 1:-1, 2:] - vel[c, 1:-1, :-2]) * scale
        if swap:
            gx, gy = gy, gx
        gz = lambda c: along(inner[c], 2) * scale
    g_x0, g_y1, g_z2 = gx(0), gy(1), gz(2)
    spread = g_x0 + g_y1 + g_z2
    new_xx = stress0[0] + step * (lam * spread + 2.0 * shear * g_x0)
    new_yy = stress0[1] + step * (lam * spread + 2.0 * shear * g_y1)
    new_zz = stress0[2] + step * (lam * spread + 2.0 * shear * g_z2)
    new_xy = stress0[3] + step * shear * (gy(0) + gx(1))
    new_xz = stress0[4] + step * shear * (gz(0) + gx(2))
    new_yz = stress0[5] + step * shear * (gz(1) + gy(2))
    return jnp.concatenate(
        [inner, jnp.stack([new_xx, new_yy, new_zz, new_xy, new_xz, new_yz])], 0
    )


def interp_matrix(n_fine, n_coarse):
    fine_pos = jnp.arange(n_fine, dtype=jnp.int32)
    whole = fine_pos // 3
    rest = fine_pos - 3 * whole
    lower = jnp.where(rest == 0, whole - 1, whole)
    frac = jnp.where(rest == 0, 2.0 / 3.0, jnp.where(rest == 1, 0.0, 1.0 / 3.0)).astype(jnp.float32)
    below = lower < 0
    lower = jnp.where(below, 0, lower)
    frac = jnp.where(below, 0.0, frac)
    above = lower >= n_coarse - 1
    lower = jnp.where(above, n_coarse - 2, lower)
    frac = jnp.where(above, 1.0, frac)
    cols = jnp.arange(n_coarse, dtype=jnp.int32)
    low_hit = (cols[None, :] == lower[:, None]).astype(jnp.float32)
    high_hit = (cols[None, :] == lower[:, None] + 1).astype(jnp.float32)
    return (1.0 - frac)[:, None] * low_hit + frac[:, None] * high_hit


def interp_np(n_fine, n_coarse):
    fine_pos = np.arange(n_fine)
    whole = fine_pos // 3
    rest = fine_pos - 3 * whole
    lower = np.where(rest == 0, whole - 1, whole)
    frac = np.where(rest == 0, 2.0 / 3.0, np.where(rest == 1, 0.0, 1.0 / 3.0))
    frac = np.where(lower < 0, 0.0, frac)
    lower = np.where(lower < 0, 0, lower)
    above = lower >= n_coarse - 1
    lower = np.where(above, n_coarse - 2, lower)
    frac = np.where(above, 1.0, frac)
    out = np.zeros((n_fine, n_coarse))
    out[fine_pos, lower] += 1.0 - frac
    out[fine_pos, lower + 1] += frac
    return out


def ramp(first, count, total, tile):
    place = first + jnp.arange(count, dtype=jnp.int32)
    margin = jnp.minimum(place, total - 1 - place).astype(jnp.float32) + 0.5
    part = jnp.maximum(1.0 - margin / tile, 0.0)
    return part * part


def local(region_state, region_material, fine_state, fine_material, material_table):
    count_x = lax.axis_size("gx")
    count_y = lax.axis_size("gy")
    flat = ("gx", "gy")
    n_flat = count_x * count_y
    me_y = lax.axis_index("gy")
    fine_x = fine_state.shape[1]
    fine_y = fine_state.shape[2]
    fine_z = fine_state.shape[3]
    own = region_state.shape[1]
    reg_y = region_state.shape[2]
    rows_each = reg_y // count_y
    reach_y = 6

    region_pay, lam_r, mu_r = lookup(region_material, material_table, region_state, 0.6, False)
    (fine_pay,) = lookup(
        jnp.transpose(fine_material, (1, 0, 2)),
        material_table,
        jnp.transpose(fine_state, (0, 2, 1, 3)),
        0.2,
        True,
    )

    me_flat = lax.axis_index("gx") * count_y + me_y
    fine_lo = from_cycle(fine_pay[:, -reach_y:], "gy", count_y, 1, me_y)
    fine_hi = from_cycle(fine_pay[:, :reach_y], "gy", count_y, -1, me_y)
    reg_lo = from_cycle(region_pay, flat, n_flat, 1, me_flat)
    reg_hi = from_cycle(region_pay, flat, n_flat, -1, me_flat)
    lows, highs = [reg_lo], [reg_hi]
    for d in range(2, -(-2 // own) + 1):
        outer = jnp.concatenate([region_pay[3:4], region_pay[6:8]], 0)
        lo_far = from_cycle(outer, flat, n_flat, d, me_flat)
        hi_far = from_cycle(outer, flat, n_flat, -d, me_flat)
        lows.insert(0, jnp.zeros_like(region_pay).at[jnp.array([3, 6, 7])].set(lo_far))
        highs.append(jnp.zeros_like(region_pay).at[jnp.array([3, 6, 7])].set(hi_far))
    reg_ext = jnp.concatenate(
        [jnp.concatenate(lows, 1)[:, -2:], region_pay, jnp.concatenate(highs, 1)[:, :2]], 1
    )
    region_next = step_wide(
        reg_ext, reg_ext[9, 1:-1], region_state[3:], lam_r, mu_r, 0.6, 3.0, True
    )

    both = jnp.concatenate([region_state, region_next], 0).astype(jnp.bfloat16)
    tile_np = interp_np(fine_y, rows_each)
    blocks_np = np.kron(np.eye(3), tile_np)[fine_y - 4: 2 * fine_y + 4]
    used = np.nonzero(np.any(blocks_np != 0.0, axis=0))[0]
    lo, hi = int(used[0]), int(used[-1]) + 1
    both = jnp.pad(both, ((0, 0), (0, 0), (rows_each, rows_each), (0, 0)))
    send = jnp.concatenate(
        [both[:, :, rows_each * d + lo: rows_each * d + hi] for d in range(count_y)], 2
    )
    band = lax.all_to_all(send, "gy", 2, 1, tiled=True).astype(jnp.float32)
    columns = band.shape[1]
    high = lax.Precision.HIGH
    along_y_w = interp_matrix(fine_y, rows_each)
    zeros_w = jnp.zeros_like(along_y_w)
    tiles_w = jnp.concatenate(
        [
            jnp.concatenate([along_y_w, zeros_w, zeros_w], 1),
            jnp.concatenate([zeros_w, along_y_w, zeros_w], 1),
            jnp.concatenate([zeros_w, zeros_w, along_y_w], 1),
        ],
        0,
    )[fine_y - 4: 2 * fine_y + 4, lo:hi]
    first = jnp.einsum("fa,cabz->cfbz", interp_matrix(fine_x, columns), band, precision=high)
    second = jnp.einsum("gb,cfbz->cgfz", tiles_w, first, precision=high)
    background = jnp.einsum(
        "kz,cgfz->cgfk", interp_matrix(fine_z, band.shape[3]), second, precision=high
    )
    along_x = ramp(lax.axis_index("gx") * fine_x, fine_x, count_x * fine_x, fine_x)
    along_y = ramp(me_y * fine_y - 4, fine_y + 8, count_y * fine_y, fine_y)
    relax = (0.1 + 0.4 * jnp.maximum(along_y[:, None], along_x[None, :]))[:, :, None]

    wide = jnp.concatenate([fine_lo, fine_pay, fine_hi], axis=1)
    lam_w, mu_w = wide[10], wide[11]
    state = wide[:9]
    coef_w = None
    for sub in range(1, 4):
        if sub == 1:
            ext = x_halo(wide[:10], 2)
            coef_w = ext[9, :, 1:-1]
            ext = ext[:9]
        else:
            ext = x_halo(state, 2)
        off = 2 * (sub - 1)
        rows = state.shape[1]
        state = step_wide(
            ext,
            coef_w[off + 1: off + rows - 1],
            state[3:, 2:-2],
            lam_w[off + 2: off + rows - 2],
            mu_w[off + 2: off + rows - 2],
            0.2,
            1.0,
            False,
            swap=True,
        )
        share = sub / 3.0
        target = background[:9, off: off + rows - 4] + share * (
            background[9:, off: off + rows - 4] - background[:9, off: off + rows - 4]
        )
        state = state + relax[None, off: off + rows - 4] * (target - state)
    return (region_next, jnp.transpose(state, (0, 2, 1, 3)))


def solution(mesh):
    return jax.shard_map(
        local,
        mesh=mesh,
        in_specs=(
            P(None, ("gx", "gy"), None, None),
            P(("gx", "gy"), None, None),
            P(None, "gx", "gy", None),
            P("gx", "gy", None),
            P(),
        ),
        out_specs=(P(None, ("gx", "gy"), None, None), P(None, "gx", "gy", None)),
        check_vma=False,
    )
```

```python
import numpy as np
import jax
import jax.numpy as jnp
from jax import lax
from jax.sharding import PartitionSpec as P
from jax.experimental import pallas as pl
from jax.experimental.pallas import tpu as pltpu


def shifted(n, s):
    return [(i, i + s) for i in range(n) if 0 <= i + s < n]


def from_cycle(field, axis, n, d, me):
    got = lax.ppermute(field, axis, [(i, (i + d) % n) for i in range(n)])
    return jnp.where((me - d >= 0) & (me - d < n), got, 0.0)


def x_halo(field, width):
    nx = lax.axis_size("gx")
    me = lax.axis_index("gx")
    cycle = [(i, (i + 1) % nx) for i in range(nx)]
    back = [(j, i) for i, j in cycle]
    from_left = lax.ppermute(field[:, :, -width:], "gx", cycle)
    from_right = lax.ppermute(field[:, :, :width], "gx", back)
    from_left = jnp.where(me > 0, from_left, 0.0)
    from_right = jnp.where(me < nx - 1, from_right, 0.0)
    return jnp.concatenate([from_left, field, from_right], axis=2)


def lookup_kernel(step, extra, idx_ref, tab_ref, state_ref, pay_ref, *rest):
    idx = idx_ref[...]
    rho = jnp.zeros(idx.shape, jnp.float32)
    lam = jnp.zeros(idx.shape, jnp.float32)
    shear = jnp.zeros(idx.shape, jnp.float32)
    for material in range(tab_ref.shape[1]):
        match = idx == material
        rho = jnp.where(match, tab_ref[0, material], rho)
        lam = jnp.where(match, tab_ref[1, material], lam)
        shear = jnp.where(match, tab_ref[2, material], shear)
    comps = state_ref.shape[0]
    pay_ref[:comps] = state_ref[...]
    pay_ref[comps] = step / rho
    if extra:
        pay_ref[comps + 1] = lam
        pay_ref[comps + 2] = shear
    else:
        rest[0][...] = lam
        rest[1][...] = shear


def lookup(index, table, state, step, extra):
    comps = state.shape[0]
    vmem = pl.BlockSpec(memory_space=pltpu.VMEM)
    cell = jax.ShapeDtypeStruct(index.shape, jnp.float32)
    pay = jax.ShapeDtypeStruct((comps + (3 if extra else 1),) + index.shape, jnp.float32)
    outs = (pay,) if extra else (pay, cell, cell)
    return pl.pallas_call(
        lambda *refs: lookup_kernel(step, extra, *refs),
        out_shape=outs,
        in_specs=[vmem, pl.BlockSpec(memory_space=pltpu.SMEM), vmem],
        out_specs=tuple(vmem for _ in outs),
    )(index, table, state)


def along(f, axis):
    n = f.shape[axis]
    zero = jnp.zeros_like(lax.slice_in_dim(f, 0, 1, axis=axis))
    up = jnp.concatenate([lax.slice_in_dim(f, 1, n, axis=axis), zero], axis=axis)
    down = jnp.concatenate([zero, lax.slice_in_dim(f, 0, n - 1, axis=axis)], axis=axis)
    return up - down


def step_wide(ext, coef, stress0, lam, shear, step, spacing, y_local, swap=False):
    scale = 0.5 / spacing
    s = ext[3:9]
    if y_local:
        mid_s = s[:, 1:-1]
        dx = lambda c: (s[c, 2:] - s[c, :-2]) * scale
        dy = lambda c: along(mid_s[c], 1) * scale
        dz = lambda c: along(mid_s[c], 2) * scale
        vel_old = ext[0:3, 1:-1]
    else:
        mid_s = s[:, 1:-1, 1:-1]
        dx = lambda c: (s[c, 2:, 1:-1] - s[c, :-2, 1:-1]) * scale
        dy = lambda c: (s[c, 1:-1, 2:] - s[c, 1:-1, :-2]) * scale
        if swap:
            dx, dy = dy, dx
        dz = lambda c: along(mid_s[c], 2) * scale
        vel_old = ext[0:3, 1:-1, 1:-1]
    acc_x = dx(0) + dy(3) + dz(4)
    acc_y = dx(3) + dy(1) + dz(5)
    acc_z = dx(4) + dy(5) + dz(2)
    vel = vel_old + coef[None] * jnp.stack([acc_x, acc_y, acc_z])
    if y_local:
        inner = vel[:, 1:-1]
        gx = lambda c: (vel[c, 2:] - vel[c, :-2]) * scale
        gy = lambda c: along(inner[c], 1) * scale
        gz = lambda c: along(inner[c], 2) * scale
    else:
        inner = vel[:, 1:-1, 1:-1]
        gx = lambda c: (vel[c, 2:, 1:-1] - vel[c, :-2, 1:-1]) * scale
        gy = lambda c: (vel[c, 1:-1, 2:] - vel[c, 1:-1, :-2]) * scale
        if swap:
            gx, gy = gy, gx
        gz = lambda c: along(inner[c], 2) * scale
    g_x0, g_y1, g_z2 = gx(0), gy(1), gz(2)
    spread = g_x0 + g_y1 + g_z2
    new_xx = stress0[0] + step * (lam * spread + 2.0 * shear * g_x0)
    new_yy = stress0[1] + step * (lam * spread + 2.0 * shear * g_y1)
    new_zz = stress0[2] + step * (lam * spread + 2.0 * shear * g_z2)
    new_xy = stress0[3] + step * shear * (gy(0) + gx(1))
    new_xz = stress0[4] + step * shear * (gz(0) + gx(2))
    new_yz = stress0[5] + step * shear * (gz(1) + gy(2))
    return jnp.concatenate(
        [inner, jnp.stack([new_xx, new_yy, new_zz, new_xy, new_xz, new_yz])], 0
    )


def interp_matrix(n_fine, n_coarse):
    fine_pos = jnp.arange(n_fine, dtype=jnp.int32)
    whole = fine_pos // 3
    rest = fine_pos - 3 * whole
    lower = jnp.where(rest == 0, whole - 1, whole)
    frac = jnp.where(rest == 0, 2.0 / 3.0, jnp.where(rest == 1, 0.0, 1.0 / 3.0)).astype(jnp.float32)
    below = lower < 0
    lower = jnp.where(below, 0, lower)
    frac = jnp.where(below, 0.0, frac)
    above = lower >= n_coarse - 1
    lower = jnp.where(above, n_coarse - 2, lower)
    frac = jnp.where(above, 1.0, frac)
    cols = jnp.arange(n_coarse, dtype=jnp.int32)
    low_hit = (cols[None, :] == lower[:, None]).astype(jnp.float32)
    high_hit = (cols[None, :] == lower[:, None] + 1).astype(jnp.float32)
    return (1.0 - frac)[:, None] * low_hit + frac[:, None] * high_hit


def interp_np(n_fine, n_coarse):
    fine_pos = np.arange(n_fine)
    whole = fine_pos // 3
    rest = fine_pos - 3 * whole
    lower = np.where(rest == 0, whole - 1, whole)
    frac = np.where(rest == 0, 2.0 / 3.0, np.where(rest == 1, 0.0, 1.0 / 3.0))
    frac = np.where(lower < 0, 0.0, frac)
    lower = np.where(lower < 0, 0, lower)
    above = lower >= n_coarse - 1
    lower = np.where(above, n_coarse - 2, lower)
    frac = np.where(above, 1.0, frac)
    out = np.zeros((n_fine, n_coarse))
    out[fine_pos, lower] += 1.0 - frac
    out[fine_pos, lower + 1] += frac
    return out


def ramp(first, count, total, tile):
    place = first + jnp.arange(count, dtype=jnp.int32)
    margin = jnp.minimum(place, total - 1 - place).astype(jnp.float32) + 0.5
    part = jnp.maximum(1.0 - margin / tile, 0.0)
    return part * part


def local(region_state, region_material, fine_state, fine_material, material_table):
    count_x = lax.axis_size("gx")
    count_y = lax.axis_size("gy")
    flat = ("gx", "gy")
    n_flat = count_x * count_y
    me_y = lax.axis_index("gy")
    fine_x = fine_state.shape[1]
    fine_y = fine_state.shape[2]
    fine_z = fine_state.shape[3]
    own = region_state.shape[1]
    reg_y = region_state.shape[2]
    rows_each = reg_y // count_y
    reach_y = 6

    region_pay, lam_r, mu_r = lookup(region_material, material_table, region_state, 0.6, False)
    (fine_pay,) = lookup(
        jnp.transpose(fine_material, (1, 0, 2)),
        material_table,
        jnp.transpose(fine_state, (0, 2, 1, 3)),
        0.2,
        True,
    )

    me_flat = lax.axis_index("gx") * count_y + me_y
    fine_lo = from_cycle(fine_pay[:, -reach_y:], "gy", count_y, 1, me_y)
    fine_hi = from_cycle(fine_pay[:, :reach_y], "gy", count_y, -1, me_y)
    reg_lo = from_cycle(region_pay, flat, n_flat, 1, me_flat)
    reg_hi = from_cycle(region_pay, flat, n_flat, -1, me_flat)
    lows, highs = [reg_lo], [reg_hi]
    for d in range(2, -(-2 // own) + 1):
        lows.insert(0, from_cycle(region_pay, flat, n_flat, d, me_flat))
        highs.append(from_cycle(region_pay, flat, n_flat, -d, me_flat))
    reg_ext = jnp.concatenate(
        [jnp.concatenate(lows, 1)[:, -2:], region_pay, jnp.concatenate(highs, 1)[:, :2]], 1
    )
    region_next = step_wide(
        reg_ext, reg_ext[9, 1:-1], region_state[3:], lam_r, mu_r, 0.6, 3.0, True
    )

    both = jnp.concatenate([region_state, region_next], 0).astype(jnp.bfloat16)
    tile_np = interp_np(fine_y, rows_each)
    blocks_np = np.kron(np.eye(3), tile_np)[fine_y - 4: 2 * fine_y + 4]
    used = np.nonzero(np.any(blocks_np != 0.0, axis=0))[0]
    lo, hi = int(used[0]), int(used[-1]) + 1
    both = jnp.pad(both, ((0, 0), (0, 0), (rows_each, rows_each), (0, 0)))
    depth_np = interp_np(fine_z, both.shape[3])
    deep = int(np.nonzero(np.any(depth_np != 0.0, axis=0))[0][-1]) + 1
    send = jnp.concatenate(
        [both[:, :, rows_each * d + lo: rows_each * d + hi, :deep] for d in range(count_y)], 2
    )
    band = lax.all_to_all(send, "gy", 2, 1, tiled=True).astype(jnp.float32)
    columns = band.shape[1]
    high = lax.Precision.HIGH
    along_y_w = interp_matrix(fine_y, rows_each)
    zeros_w = jnp.zeros_like(along_y_w)
    tiles_w = jnp.concatenate(
        [
            jnp.concatenate([along_y_w, zeros_w, zeros_w], 1),
            jnp.concatenate([zeros_w, along_y_w, zeros_w], 1),
            jnp.concatenate([zeros_w, zeros_w, along_y_w], 1),
        ],
        0,
    )[fine_y - 4: 2 * fine_y + 4, lo:hi]
    first = jnp.einsum("fa,cabz->cfbz", interp_matrix(fine_x, columns), band, precision=high)
    second = jnp.einsum("gb,cfbz->cgfz", tiles_w, first, precision=high)
    background = jnp.einsum(
        "kz,cgfz->cgfk", interp_matrix(fine_z, both.shape[3])[:, :deep], second, precision=high
    )
    along_x = ramp(lax.axis_index("gx") * fine_x, fine_x, count_x * fine_x, fine_x)
    along_y = ramp(me_y * fine_y - 4, fine_y + 8, count_y * fine_y, fine_y)
    relax = (0.1 + 0.4 * jnp.maximum(along_y[:, None], along_x[None, :]))[:, :, None]

    wide = jnp.concatenate([fine_lo, fine_pay, fine_hi], axis=1)
    lam_w, mu_w = wide[10], wide[11]
    state = wide[:9]
    coef_w = None
    for sub in range(1, 4):
        if sub == 1:
            ext = x_halo(wide[:10], 2)
            coef_w = ext[9, :, 1:-1]
            ext = ext[:9]
        else:
            ext = x_halo(state, 2)
        off = 2 * (sub - 1)
        rows = state.shape[1]
        state = step_wide(
            ext,
            coef_w[off + 1: off + rows - 1],
            state[3:, 2:-2],
            lam_w[off + 2: off + rows - 2],
            mu_w[off + 2: off + rows - 2],
            0.2,
            1.0,
            False,
            swap=True,
        )
        share = sub / 3.0
        target = background[:9, off: off + rows - 4] + share * (
            background[9:, off: off + rows - 4] - background[:9, off: off + rows - 4]
        )
        state = state + relax[None, off: off + rows - 4] * (target - state)
    return (region_next, jnp.transpose(state, (0, 2, 1, 3)))


def solution(mesh):
    return jax.shard_map(
        local,
        mesh=mesh,
        in_specs=(
            P(None, ("gx", "gy"), None, None),
            P(("gx", "gy"), None, None),
            P(None, "gx", "gy", None),
            P("gx", "gy", None),
            P(),
        ),
        out_specs=(P(None, ("gx", "gy"), None, None), P(None, "gx", "gy", None)),
        check_vma=False,
    )
```

```python
import numpy as np
import jax
import jax.numpy as jnp
from jax import lax
from jax.sharding import PartitionSpec as P
from jax.experimental import pallas as pl
from jax.experimental.pallas import tpu as pltpu


def shifted(n, s):
    return [(i, i + s) for i in range(n) if 0 <= i + s < n]


def from_cycle(field, axis, n, d, me):
    got = lax.ppermute(field, axis, [(i, (i + d) % n) for i in range(n)])
    return jnp.where((me - d >= 0) & (me - d < n), got, 0.0)


def x_halo(field, width):
    nx = lax.axis_size("gx")
    me = lax.axis_index("gx")
    cycle = [(i, (i + 1) % nx) for i in range(nx)]
    back = [(j, i) for i, j in cycle]
    from_left = lax.ppermute(field[:, :, -width:], "gx", cycle)
    from_right = lax.ppermute(field[:, :, :width], "gx", back)
    from_left = jnp.where(me > 0, from_left, 0.0)
    from_right = jnp.where(me < nx - 1, from_right, 0.0)
    return jnp.concatenate([from_left, field, from_right], axis=2)


def lookup_kernel(step, extra, idx_ref, tab_ref, state_ref, pay_ref, *rest):
    idx = idx_ref[...]
    rho = jnp.zeros(idx.shape, jnp.float32)
    lam = jnp.zeros(idx.shape, jnp.float32)
    shear = jnp.zeros(idx.shape, jnp.float32)
    for material in range(tab_ref.shape[1]):
        match = idx == material
        rho = jnp.where(match, tab_ref[0, material], rho)
        lam = jnp.where(match, tab_ref[1, material], lam)
        shear = jnp.where(match, tab_ref[2, material], shear)
    comps = state_ref.shape[0]
    pay_ref[:comps] = state_ref[...]
    pay_ref[comps] = step / rho
    if extra:
        pay_ref[comps + 1] = lam
        pay_ref[comps + 2] = shear
    else:
        rest[0][...] = lam
        rest[1][...] = shear


def lookup(index, table, state, step, extra):
    comps = state.shape[0]
    vmem = pl.BlockSpec(memory_space=pltpu.VMEM)
    cell = jax.ShapeDtypeStruct(index.shape, jnp.float32)
    pay = jax.ShapeDtypeStruct((comps + (3 if extra else 1),) + index.shape, jnp.float32)
    outs = (pay,) if extra else (pay, cell, cell)
    return pl.pallas_call(
        lambda *refs: lookup_kernel(step, extra, *refs),
        out_shape=outs,
        in_specs=[vmem, pl.BlockSpec(memory_space=pltpu.SMEM), vmem],
        out_specs=tuple(vmem for _ in outs),
    )(index, table, state)


def along(f, axis):
    n = f.shape[axis]
    zero = jnp.zeros_like(lax.slice_in_dim(f, 0, 1, axis=axis))
    up = jnp.concatenate([lax.slice_in_dim(f, 1, n, axis=axis), zero], axis=axis)
    down = jnp.concatenate([zero, lax.slice_in_dim(f, 0, n - 1, axis=axis)], axis=axis)
    return up - down


def step_wide(ext, coef, stress0, lam, shear, step, spacing, y_local, swap=False):
    scale = 0.5 / spacing
    s = ext[3:9]
    if y_local:
        mid_s = s[:, 1:-1]
        dx = lambda c: (s[c, 2:] - s[c, :-2]) * scale
        dy = lambda c: along(mid_s[c], 1) * scale
        dz = lambda c: along(mid_s[c], 2) * scale
        vel_old = ext[0:3, 1:-1]
    else:
        mid_s = s[:, 1:-1, 1:-1]
        dx = lambda c: (s[c, 2:, 1:-1] - s[c, :-2, 1:-1]) * scale
        dy = lambda c: (s[c, 1:-1, 2:] - s[c, 1:-1, :-2]) * scale
        if swap:
            dx, dy = dy, dx
        dz = lambda c: along(mid_s[c], 2) * scale
        vel_old = ext[0:3, 1:-1, 1:-1]
    acc_x = dx(0) + dy(3) + dz(4)
    acc_y = dx(3) + dy(1) + dz(5)
    acc_z = dx(4) + dy(5) + dz(2)
    vel = vel_old + coef[None] * jnp.stack([acc_x, acc_y, acc_z])
    if y_local:
        inner = vel[:, 1:-1]
        gx = lambda c: (vel[c, 2:] - vel[c, :-2]) * scale
        gy = lambda c: along(inner[c], 1) * scale
        gz = lambda c: along(inner[c], 2) * scale
    else:
        inner = vel[:, 1:-1, 1:-1]
        gx = lambda c: (vel[c, 2:, 1:-1] - vel[c, :-2, 1:-1]) * scale
        gy = lambda c: (vel[c, 1:-1, 2:] - vel[c, 1:-1, :-2]) * scale
        if swap:
            gx, gy = gy, gx
        gz = lambda c: along(inner[c], 2) * scale
    g_x0, g_y1, g_z2 = gx(0), gy(1), gz(2)
    spread = g_x0 + g_y1 + g_z2
    new_xx = stress0[0] + step * (lam * spread + 2.0 * shear * g_x0)
    new_yy = stress0[1] + step * (lam * spread + 2.0 * shear * g_y1)
    new_zz = stress0[2] + step * (lam * spread + 2.0 * shear * g_z2)
    new_xy = stress0[3] + step * shear * (gy(0) + gx(1))
    new_xz = stress0[4] + step * shear * (gz(0) + gx(2))
    new_yz = stress0[5] + step * shear * (gz(1) + gy(2))
    return jnp.concatenate(
        [inner, jnp.stack([new_xx, new_yy, new_zz, new_xy, new_xz, new_yz])], 0
    )


def interp_matrix(n_fine, n_coarse):
    fine_pos = jnp.arange(n_fine, dtype=jnp.int32)
    whole = fine_pos // 3
    rest = fine_pos - 3 * whole
    lower = jnp.where(rest == 0, whole - 1, whole)
    frac = jnp.where(rest == 0, 2.0 / 3.0, jnp.where(rest == 1, 0.0, 1.0 / 3.0)).astype(jnp.float32)
    below = lower < 0
    lower = jnp.where(below, 0, lower)
    frac = jnp.where(below, 0.0, frac)
    above = lower >= n_coarse - 1
    lower = jnp.where(above, n_coarse - 2, lower)
    frac = jnp.where(above, 1.0, frac)
    cols = jnp.arange(n_coarse, dtype=jnp.int32)
    low_hit = (cols[None, :] == lower[:, None]).astype(jnp.float32)
    high_hit = (cols[None, :] == lower[:, None] + 1).astype(jnp.float32)
    return (1.0 - frac)[:, None] * low_hit + frac[:, None] * high_hit


def interp_np(n_fine, n_coarse):
    fine_pos = np.arange(n_fine)
    whole = fine_pos // 3
    rest = fine_pos - 3 * whole
    lower = np.where(rest == 0, whole - 1, whole)
    frac = np.where(rest == 0, 2.0 / 3.0, np.where(rest == 1, 0.0, 1.0 / 3.0))
    frac = np.where(lower < 0, 0.0, frac)
    lower = np.where(lower < 0, 0, lower)
    above = lower >= n_coarse - 1
    lower = np.where(above, n_coarse - 2, lower)
    frac = np.where(above, 1.0, frac)
    out = np.zeros((n_fine, n_coarse))
    out[fine_pos, lower] += 1.0 - frac
    out[fine_pos, lower + 1] += frac
    return out


def ramp(first, count, total, tile):
    place = first + jnp.arange(count, dtype=jnp.int32)
    margin = jnp.minimum(place, total - 1 - place).astype(jnp.float32) + 0.5
    part = jnp.maximum(1.0 - margin / tile, 0.0)
    return part * part


def local(region_state, region_material, fine_state, fine_material, material_table):
    count_x = lax.axis_size("gx")
    count_y = lax.axis_size("gy")
    flat = ("gx", "gy")
    n_flat = count_x * count_y
    me_y = lax.axis_index("gy")
    fine_x = fine_state.shape[1]
    fine_y = fine_state.shape[2]
    fine_z = fine_state.shape[3]
    own = region_state.shape[1]
    reg_y = region_state.shape[2]
    rows_each = reg_y // count_y
    reach_y = 6

    region_pay, lam_r, mu_r = lookup(region_material, material_table, region_state, 0.6, False)

    me_flat = lax.axis_index("gx") * count_y + me_y
    reg_lo = from_cycle(region_pay, flat, n_flat, 1, me_flat)
    reg_hi = from_cycle(region_pay, flat, n_flat, -1, me_flat)
    lows, highs = [reg_lo], [reg_hi]
    for d in range(2, -(-2 // own) + 1):
        lows.insert(0, from_cycle(region_pay, flat, n_flat, d, me_flat))
        highs.append(from_cycle(region_pay, flat, n_flat, -d, me_flat))
    reg_ext = jnp.concatenate(
        [jnp.concatenate(lows, 1)[:, -2:], region_pay, jnp.concatenate(highs, 1)[:, :2]], 1
    )
    region_next = step_wide(
        reg_ext, reg_ext[9, 1:-1], region_state[3:], lam_r, mu_r, 0.6, 3.0, True
    )

    both = jnp.concatenate([region_state, region_next], 0).astype(jnp.bfloat16)
    tile_np = interp_np(fine_y, rows_each)
    blocks_np = np.kron(np.eye(3), tile_np)[fine_y - 4: 2 * fine_y + 4]
    used = np.nonzero(np.any(blocks_np != 0.0, axis=0))[0]
    lo, hi = int(used[0]), int(used[-1]) + 1
    both = jnp.pad(both, ((0, 0), (0, 0), (rows_each, rows_each), (0, 0)))
    depth_np = interp_np(fine_z, both.shape[3])
    deep = int(np.nonzero(np.any(depth_np != 0.0, axis=0))[0][-1]) + 1
    send = jnp.concatenate(
        [both[:, :, rows_each * d + lo: rows_each * d + hi, :deep] for d in range(count_y)], 2
    )
    send, fine_mat, fine_in = lax.optimization_barrier((send, fine_material, fine_state))
    band = lax.all_to_all(send, "gy", 2, 1, tiled=True).astype(jnp.float32)
    (fine_pay,) = lookup(
        jnp.transpose(fine_mat, (1, 0, 2)),
        material_table,
        jnp.transpose(fine_in, (0, 2, 1, 3)),
        0.2,
        True,
    )
    fine_lo = from_cycle(fine_pay[:, -reach_y:], "gy", count_y, 1, me_y)
    fine_hi = from_cycle(fine_pay[:, :reach_y], "gy", count_y, -1, me_y)
    columns = band.shape[1]
    high = lax.Precision.HIGH
    along_y_w = interp_matrix(fine_y, rows_each)
    zeros_w = jnp.zeros_like(along_y_w)
    tiles_w = jnp.concatenate(
        [
            jnp.concatenate([along_y_w, zeros_w, zeros_w], 1),
            jnp.concatenate([zeros_w, along_y_w, zeros_w], 1),
            jnp.concatenate([zeros_w, zeros_w, along_y_w], 1),
        ],
        0,
    )[fine_y - 4: 2 * fine_y + 4, lo:hi]
    first = jnp.einsum("fa,cabz->cfbz", interp_matrix(fine_x, columns), band, precision=high)
    second = jnp.einsum("gb,cfbz->cgfz", tiles_w, first, precision=high)
    background = jnp.einsum(
        "kz,cgfz->cgfk", interp_matrix(fine_z, both.shape[3])[:, :deep], second, precision=high
    )
    along_x = ramp(lax.axis_index("gx") * fine_x, fine_x, count_x * fine_x, fine_x)
    along_y = ramp(me_y * fine_y - 4, fine_y + 8, count_y * fine_y, fine_y)
    relax = (0.1 + 0.4 * jnp.maximum(along_y[:, None], along_x[None, :]))[:, :, None]

    wide = jnp.concatenate([fine_lo, fine_pay, fine_hi], axis=1)
    lam_w, mu_w = wide[10], wide[11]
    state = wide[:9]
    coef_w = None
    for sub in range(1, 4):
        if sub == 1:
            ext = x_halo(wide[:10], 2)
            coef_w = ext[9, :, 1:-1]
            ext = ext[:9]
        else:
            ext = x_halo(state, 2)
        off = 2 * (sub - 1)
        rows = state.shape[1]
        state = step_wide(
            ext,
            coef_w[off + 1: off + rows - 1],
            state[3:, 2:-2],
            lam_w[off + 2: off + rows - 2],
            mu_w[off + 2: off + rows - 2],
            0.2,
            1.0,
            False,
            swap=True,
        )
        share = sub / 3.0
        target = background[:9, off: off + rows - 4] + share * (
            background[9:, off: off + rows - 4] - background[:9, off: off + rows - 4]
        )
        state = state + relax[None, off: off + rows - 4] * (target - state)
    return (region_next, jnp.transpose(state, (0, 2, 1, 3)))


def solution(mesh):
    return jax.shard_map(
        local,
        mesh=mesh,
        in_specs=(
            P(None, ("gx", "gy"), None, None),
            P(("gx", "gy"), None, None),
            P(None, "gx", "gy", None),
            P("gx", "gy", None),
            P(),
        ),
        out_specs=(P(None, ("gx", "gy"), None, None), P(None, "gx", "gy", None)),
        check_vma=False,
    )
```
